512 devices in a mesh: tgt: 32 (over z_hi, x, core), src: 16 (over z_lo, y).
Axes of the slice: x: 4, y: 8, z: 8 (z_hi: 4, z_lo: 2; z = z_hi * 2 + z_lo), core: 2. Of those that a mesh axis runs over, the one named last changes fastest.
Arguments:
- states_late: bfloat16 [32768, 128], P('src'), may hold values from -12 to 12
- offset_late: bfloat16 [32768], P('src'), may hold values from 0 to 2
- values_late: bfloat16 [32768, 64], P('src'), may hold values from -6 to 6
- states_mid: bfloat16 [32768, 128], P('tgt'), may hold values from -12 to 12
- offset_mid: bfloat16 [32768], P('src'), may hold values from 0 to 2
- exercise_mid: bfloat16 [32768, 64], P('tgt'), may hold values from -6 to 6
- mask_mid: int32 [64, 64], replicated, may hold values from 0 to 1, as said below
- states_early: bfloat16 [32768, 128], P('tgt'), may hold values from -12 to 12
- exercise_early: bfloat16 [32768, 64], P('tgt'), may hold values from -6 to 6
- mask_early: int32 [64, 64], replicated, may hold values from 0 to 1, as said below
Outputs:
- value_mid: bfloat16 [32768, 64], P('tgt')
- value_early: bfloat16 [32768, 64], P('tgt')
The draws below stay inside these ranges and needn't reach their ends.
Inputs may be any that keep to these rules, and one draw needn't show every extreme that they name: `mask_mid`: 1 marks a live tile of 512 x 512 paths; every diagonal tile is live. `mask_early`: 1 marks a live tile of 512 x 512 paths; every diagonal tile is live.
All inputs are finite; a program needn't handle non-finite values.
Results may differ from the reference program's by a relative error of at most 0.0055.
Values may be sent and summed in bfloat16 or wider, within the bound.
No kernel may reach another device: no remote copies, remote signals or barrier semaphores. Data moves between devices by JAX's collectives and lax.ppermute only.
A program may use at most 64 MiB of HBM per device.

```python
import math
import jax
import jax.numpy as jnp
from jax import lax

K = 128
V = 64
BLOCK = 512
PATHS = 32768
NB = 64


def hot_signs(key):
    flips = jax.random.bernoulli(jax.random.fold_in(key, 99), 0.5, (K,))
    amplitude = math.sqrt(60.0) * K ** (-0.25)
    return jnp.where(flips, amplitude, -amplitude).astype(jnp.float32)


def state_draw(key, role):
    noise = jnp.clip(jax.random.normal(jax.random.fold_in(key, 11 + role), (PATHS, K), jnp.float32), -6.0, 6.0)
    signs = hot_signs(key)
    path_ids = jnp.arange(PATHS)
    block_ids = path_ids // BLOCK
    within = path_ids % BLOCK
    levels = jnp.array([0.8, 1.1, 1.4], jnp.float32)
    strength = levels[block_ids // 4 % 3]
    hot_block = block_ids % 4 == 0
    first = hot_block & (within == 1)
    second = hot_block & (within == 3) & (role > 0)
    gain = jnp.where(first, strength, jnp.where(second, strength - 0.01, 0.0))
    chosen = first | second
    noise = jnp.where(chosen[:, None], gain[:, None] * signs[None, :], noise)
    return noise.astype(jnp.bfloat16)


def tile_mask_draw(key, salt):
    rates = jax.random.randint(jax.random.fold_in(key, salt), (NB, 1), 2, 9)
    rolls = jax.random.randint(jax.random.fold_in(key, salt + 1), (NB, NB), 0, 8)
    diagonal = jnp.arange(NB)[:, None] == jnp.arange(NB)[None, :]
    return ((rolls < rates) | diagonal).astype(jnp.int32)


def draw_states_late(key, part):
    return state_draw(key, 2)


def draw_states_mid(key, part):
    return state_draw(key, 1)


def draw_states_early(key, part):
    return state_draw(key, 0)


def draw_mask_mid(key, part):
    return tile_mask_draw(key, 41)


def draw_mask_early(key, part):
    return tile_mask_draw(key, 51)


def block_levels(own_key, extent, split, least, high):
    level, own = 1.0, jax.random.fold_in(own_key, 6)
    for dim, shards_of in split:
        heights = jnp.exp(jax.random.uniform(jax.random.fold_in(own, dim), (shards_of,), jnp.float32, least / len(split), high / len(split)))
        level = level * jnp.repeat(heights, extent[dim] // shards_of).reshape([-1 if axis == dim else 1 for axis in range(len(extent))])
    return level


def bell_draw(rng, extent, width, most, cuts=(), dtype=jnp.bfloat16):
    drawn = width * jax.random.normal(rng, extent, jnp.float32)
    if cuts:
        drawn = drawn * block_levels(rng, extent, cuts, -0.22, 0.18)
    return jnp.clip(drawn, -most, most).astype(dtype)


def setup_inputs(seed: int = 0) -> dict:
    keys = jax.random.split(jax.random.key(seed), 11)
    return {
        "states_late": draw_states_late(jax.random.fold_in(keys[10], 71), 0),
        "offset_late": jnp.clip(2.0 * jax.random.uniform(keys[1], (PATHS,), jnp.float32) ** block_levels(keys[1], (PATHS,), ((0, 16),), -0.2, 0.2), 0.0, 2.0).astype(jnp.bfloat16),
        "values_late": bell_draw(keys[2], (PATHS, V), 1.0, 6.0, ((0, 16),)),
        "states_mid": draw_states_mid(jax.random.fold_in(keys[10], 71), 0),
        "offset_mid": jnp.clip(2.0 * jax.random.uniform(keys[4], (PATHS,), jnp.float32) ** block_levels(keys[4], (PATHS,), ((0, 16),), -0.2, 0.2), 0.0, 2.0).astype(jnp.bfloat16),
        "exercise_mid": bell_draw(keys[5], (PATHS, V), 0.4, 6.0, ((0, 32),)),
        "mask_mid": draw_mask_mid(jax.random.fold_in(keys[10], 71), 0),
        "states_early": draw_states_early(jax.random.fold_in(keys[10], 71), 0),
        "exercise_early": bell_draw(keys[8], (PATHS, V), 0.4, 6.0, ((0, 32),)),
        "mask_early": draw_mask_early(jax.random.fold_in(keys[10], 71), 0),
    }


sharpness = 3.5
very_low = -1.0e30


def date_values(targets, sources, offsets, values, tile_mask, exercise):
    score_scale = sharpness / (K ** 0.5)
    source_f = sources.astype(jnp.float32)
    offset_f = offsets.astype(jnp.float32)
    value_f = values.astype(jnp.float32)
    live_table = jnp.repeat(tile_mask, BLOCK, axis=1)
    target_blocks = targets.reshape(NB, BLOCK, K)
    exercise_blocks = exercise.reshape(NB, BLOCK, V)

    def block_values(inputs):
        target_rows, exercise_rows, live_row = inputs
        scores = jnp.dot(target_rows.astype(jnp.float32), source_f.T, precision=lax.Precision.HIGHEST)
        scores = scores * score_scale - offset_f[None, :]
        live_cols = (live_row > 0)[None, :]
        scores = jnp.where(live_cols, scores, very_low)
        row_peak = jnp.max(scores, axis=1)
        weights = jnp.where(live_cols, jnp.exp(scores - row_peak[:, None]), 0.0)
        weight_sum = jnp.sum(weights, axis=1)
        rounded = lax.optimization_barrier(weights.astype(jnp.bfloat16)).astype(jnp.float32)
        weighted = jnp.dot(rounded, value_f, precision=lax.Precision.HIGHEST)
        continuation = weighted / weight_sum[:, None]
        return jnp.maximum(continuation, exercise_rows.astype(jnp.float32)).astype(jnp.bfloat16)

    result = lax.map(block_values, (target_blocks, exercise_blocks, live_table))
    return result.reshape(PATHS, V)


def reference(states_late, offset_late, values_late, states_mid, offset_mid, exercise_mid, mask_mid, states_early, exercise_early, mask_early):
    value_mid = date_values(states_mid, states_late, offset_late, values_late, mask_mid, exercise_mid)
    value_early = date_values(states_early, states_mid, offset_mid, value_mid, mask_early, exercise_early)
    return (value_mid, value_early)
```

```python
import jax
import jax.numpy as jnp
from jax import lax
from jax.sharding import PartitionSpec as P

BLOCK = 512


sharpness = 3.5
very_low = -1e30

HALVING_BITS = (3, 0, 1, 2)


def date_partials(targets, sources, offsets, values, tile_mask, col_tile_ids):
    row_count = targets.shape[0]
    factors = targets.shape[1]
    value_width = values.shape[1]
    row_tiles = row_count // BLOCK
    col_tiles = sources.shape[0] // BLOCK
    score_scale = sharpness / factors**0.5
    row_ids = lax.axis_index("tgt") * row_tiles + jnp.arange(row_tiles)
    local_mask = tile_mask[row_ids][:, col_tile_ids]
    source_tiles = sources.reshape(col_tiles, BLOCK, factors)
    offset_tiles = offsets.astype(jnp.float32).reshape(col_tiles, BLOCK)
    value_tiles = values.reshape(col_tiles, BLOCK, value_width)
    peaks, sums, weighted_all = ([], [], [])
    for row_block in range(row_tiles):
        target_rows = targets[row_block * BLOCK : (row_block + 1) * BLOCK]

        def step(carry, inputs):
            source_tile, offset_tile, value_tile, tile_live = inputs

            def active(carry_in):
                row_peak, weight_sum, weighted = carry_in
                scores = lax.dot_general(
                    target_rows,
                    source_tile,
                    (((1,), (1,)), ((), ())),
                    preferred_element_type=jnp.float32,
                )
                scores = scores * score_scale - offset_tile[None, :]
                new_peak = jnp.maximum(row_peak, jnp.max(scores, axis=1))
                shrink = jnp.exp(row_peak - new_peak)
                weights = jnp.exp(scores - new_peak[:, None])
                new_sum = weight_sum * shrink + jnp.sum(weights, axis=1)
                new_weighted = weighted * shrink[:, None] + jnp.dot(
                    weights.astype(jnp.bfloat16), value_tile, preferred_element_type=jnp.float32
                )
                return (new_peak, new_sum, new_weighted)

            def skipped(carry_in):
                return carry_in

            return (lax.cond(tile_live > 0, active, skipped, carry), None)

        start = (
            jnp.full((BLOCK,), very_low, jnp.float32),
            jnp.zeros((BLOCK,), jnp.float32),
            jnp.zeros((BLOCK, value_width), jnp.float32),
        )
        result, _ = lax.scan(
            step, start, (source_tiles, offset_tiles, value_tiles, local_mask[row_block])
        )
        peaks.append(result[0])
        sums.append(result[1])
        weighted_all.append(result[2])
    return (jnp.concatenate(peaks, 0), jnp.concatenate(sums, 0), jnp.concatenate(weighted_all, 0))


def xor_perm(size, bit):
    return [(i, i ^ (1 << bit)) for i in range(size)]


def merge(mine, theirs):
    width = mine.shape[1] - 2
    peak_a, peak_b = mine[:, width + 1], theirs[:, width + 1]
    peak = jnp.maximum(peak_a, peak_b)
    scale_a = jnp.exp(peak_a - peak)
    scale_b = jnp.exp(peak_b - peak)
    body = mine[:, : width + 1] * scale_a[:, None] + theirs[:, : width + 1] * scale_b[:, None]
    return jnp.concatenate([body, peak[:, None]], axis=1)


def finish(partials, exercise):
    row_peak, weight_sum, weighted = partials
    src_size = lax.axis_size("src")
    me = lax.axis_index("src")
    packed = jnp.concatenate([weighted, weight_sum[:, None], row_peak[:, None]], axis=1)
    exercise = exercise.astype(jnp.float32)
    for bit in HALVING_BITS:
        half = packed.shape[0] // 2
        mine_hi = (me >> bit) & 1
        low, high = packed[:half], packed[half:]
        keep = jnp.where(mine_hi == 1, high, low)
        send = jnp.where(mine_hi == 1, low, high)
        got = lax.ppermute(send, "src", xor_perm(src_size, bit))
        packed = merge(keep, got)
        exercise = jnp.where(mine_hi == 1, exercise[half:], exercise[:half])
    width = packed.shape[1] - 2
    continuation = packed[:, :width] / packed[:, width : width + 1]
    value = jnp.maximum(continuation, exercise).astype(jnp.bfloat16)
    for bit in reversed(HALVING_BITS):
        mine_hi = (me >> bit) & 1
        got = lax.ppermute(value, "src", xor_perm(src_size, bit))
        value = jnp.where(
            mine_hi == 1,
            jnp.concatenate([got, value], 0),
            jnp.concatenate([value, got], 0),
        )
    return value


def regroup(block_rows):
    tgt_size = lax.axis_size("tgt")
    src_size = lax.axis_size("src")
    per_owner = tgt_size // src_size

    def lin(t, s):
        return t * src_size + s

    perms = []
    for flip in range(per_owner):
        pairs = []
        for u in range(tgt_size):
            for v in range(src_size):
                part = u % per_owner
                t = per_owner * v + ((part + flip) % per_owner)
                pairs.append((lin(u, v), lin(t, u // per_owner)))
        perms.append(pairs)
    got = [lax.ppermute(block_rows, ("tgt", "src"), p) for p in perms]
    return got


def regroup_order(got):
    per_owner = len(got)
    t = lax.axis_index("tgt")
    ordered = []
    for part in range(per_owner):
        flip = (t - part) % per_owner
        pick = got[0]
        for f in range(1, per_owner):
            pick = jnp.where(flip == f, got[f], pick)
        ordered.append(pick)
    return jnp.concatenate(ordered, 0)


def per_device(
    states_late,
    offset_late,
    values_late,
    states_mid,
    offset_mid,
    exercise_mid,
    mask_mid,
    states_early,
    exercise_early,
    mask_early,
):
    src_tiles = states_late.shape[0] // BLOCK
    col_ids = lax.axis_index("src") * src_tiles + jnp.arange(src_tiles)
    mid_sources = regroup_order(regroup(states_mid))
    value_mid = finish(
        date_partials(states_mid, states_late, offset_late, values_late, mask_mid, col_ids),
        exercise_mid,
    )
    mid_values = regroup_order(regroup(value_mid))
    value_early = finish(
        date_partials(states_early, mid_sources, offset_mid, mid_values, mask_early, col_ids),
        exercise_early,
    )
    return (value_mid, value_early)


def solution(mesh):
    in_specs = (
        P("src", None),
        P("src"),
        P("src", None),
        P("tgt", None),
        P("src"),
        P("tgt", None),
        P(),
        P("tgt", None),
        P("tgt", None),
        P(),
    )
    out_specs = (P("tgt", None), P("tgt", None))
    return jax.shard_map(
        per_device, mesh=mesh, in_specs=in_specs, out_specs=out_specs, check_vma=False
    )
```

```python
import jax
import jax.numpy as jnp
from jax import lax
from jax.sharding import PartitionSpec as P

BLOCK = 512


sharpness = 3.5
very_low = -1e30

HALVING_BITS = (3, 0, 1, 2)


def date_partials(targets, sources, offsets, values, tile_mask, col_tile_ids):
    row_count = targets.shape[0]
    factors = targets.shape[1]
    value_width = values.shape[1]
    row_tiles = row_count // BLOCK
    col_tiles = sources.shape[0] // BLOCK
    score_scale = sharpness / factors**0.5
    row_ids = lax.axis_index("tgt") * row_tiles + jnp.arange(row_tiles)
    local_mask = tile_mask[row_ids][:, col_tile_ids]
    source_tiles = sources.reshape(col_tiles, BLOCK, factors)
    offset_tiles = offsets.astype(jnp.float32).reshape(col_tiles, BLOCK)
    value_tiles = values.reshape(col_tiles, BLOCK, value_width)
    peaks, sums, weighted_all = ([], [], [])
    for row_block in range(row_tiles):
        target_rows = targets[row_block * BLOCK : (row_block + 1) * BLOCK]

        def step(carry, inputs):
            source_tile, offset_tile, value_tile, tile_live = inputs

            def active(carry_in):
                row_peak, weight_sum, weighted = carry_in
                scores = lax.dot_general(
                    target_rows,
                    source_tile,
                    (((1,), (1,)), ((), ())),
                    preferred_element_type=jnp.float32,
                )
                scores = scores * score_scale - offset_tile[None, :]
                new_peak = jnp.maximum(row_peak, jnp.max(scores, axis=1))
                shrink = jnp.exp(row_peak - new_peak)
                weights = jnp.exp(scores - new_peak[:, None])
                new_sum = weight_sum * shrink + jnp.sum(weights, axis=1)
                new_weighted = weighted * shrink[:, None] + jnp.dot(
                    weights.astype(jnp.bfloat16), value_tile, preferred_element_type=jnp.float32
                )
                return (new_peak, new_sum, new_weighted)

            def skipped(carry_in):
                return carry_in

            return (lax.cond(tile_live > 0, active, skipped, carry), None)

        start = (
            jnp.full((BLOCK,), very_low, jnp.float32),
            jnp.zeros((BLOCK,), jnp.float32),
            jnp.zeros((BLOCK, value_width), jnp.float32),
        )
        result, _ = lax.scan(
            step, start, (source_tiles, offset_tiles, value_tiles, local_mask[row_block])
        )
        peaks.append(result[0])
        sums.append(result[1])
        weighted_all.append(result[2])
    return (jnp.concatenate(peaks, 0), jnp.concatenate(sums, 0), jnp.concatenate(weighted_all, 0))


def xor_perm(size, bit):
    return [(i, i ^ (1 << bit)) for i in range(size)]


def merge(mine, theirs):
    width = mine.shape[1] - 2
    peak_a, peak_b = mine[:, width + 1], theirs[:, width + 1]
    peak = jnp.maximum(peak_a, peak_b)
    scale_a = jnp.exp(peak_a - peak)
    scale_b = jnp.exp(peak_b - peak)
    body = mine[:, : width + 1] * scale_a[:, None] + theirs[:, : width + 1] * scale_b[:, None]
    return jnp.concatenate([body, peak[:, None]], axis=1)


def finish(partials, exercise):
    row_peak, weight_sum, weighted = partials
    src_size = lax.axis_size("src")
    me = lax.axis_index("src")
    packed = jnp.concatenate([weighted, weight_sum[:, None], row_peak[:, None]], axis=1)
    exercise = exercise.astype(jnp.float32)
    for bit in HALVING_BITS:
        half = packed.shape[0] // 2
        mine_hi = (me >> bit) & 1
        low, high = packed[:half], packed[half:]
        keep = jnp.where(mine_hi == 1, high, low)
        send = jnp.where(mine_hi == 1, low, high)
        got = lax.ppermute(send, "src", xor_perm(src_size, bit))
        packed = merge(keep, got)
        exercise = jnp.where(mine_hi == 1, exercise[half:], exercise[:half])
    width = packed.shape[1] - 2
    continuation = packed[:, :width] / packed[:, width : width + 1]
    value = jnp.maximum(continuation, exercise).astype(jnp.bfloat16)
    for bit in reversed(HALVING_BITS):
        mine_hi = (me >> bit) & 1
        got = lax.ppermute(value, "src", xor_perm(src_size, bit))
        value = jnp.where(
            mine_hi == 1,
            jnp.concatenate([got, value], 0),
            jnp.concatenate([value, got], 0),
        )
    return value


def lin(t, s):
    return t * lax.axis_size("src") + s


def source_pair(t, s):
    x_count = lax.axis_size("tgt") // 8
    z_hi, x = t // (2 * x_count), (t // 2) % x_count
    return ((z_hi + s // 4) % 4) * x_count + (x + s % 4) % x_count


def regroup(block_rows):
    tgt_size = lax.axis_size("tgt")
    src_size = lax.axis_size("src")
    perms = ([], [])
    for t in range(tgt_size):
        for s in range(src_size):
            pair = source_pair(t, s)
            for flip in range(2):
                u = 2 * pair + ((t % 2) ^ flip)
                perms[flip].append((lin(u, s), lin(t, s)))
    return [lax.ppermute(block_rows, ("tgt", "src"), p) for p in perms]


def regroup_order(got):
    odd = lax.axis_index("tgt") % 2 == 1
    return jnp.concatenate(
        [jnp.where(odd, got[1], got[0]), jnp.where(odd, got[0], got[1])], 0
    )


def regroup_offsets(offsets):
    tgt_size = lax.axis_size("tgt")
    src_size = lax.axis_size("src")
    pairs = [
        (lin(t, source_pair(t, s)), lin(t, s)) for t in range(tgt_size) for s in range(src_size)
    ]
    return lax.ppermute(offsets, ("tgt", "src"), pairs)


def per_device(
    states_late,
    offset_late,
    values_late,
    states_mid,
    offset_mid,
    exercise_mid,
    mask_mid,
    states_early,
    exercise_early,
    mask_early,
):
    src_tiles = states_late.shape[0] // BLOCK
    col_ids = lax.axis_index("src") * src_tiles + jnp.arange(src_tiles)
    pair = source_pair(lax.axis_index("tgt"), lax.axis_index("src"))
    early_col_ids = pair * src_tiles + jnp.arange(src_tiles)
    mid_sources = regroup_order(regroup(states_mid))
    mid_offsets = regroup_offsets(offset_mid)
    partials = date_partials(states_mid, states_late, offset_late, values_late, mask_mid, col_ids)
    partials, mid_sources, mid_offsets = lax.optimization_barrier(
        (partials, mid_sources, mid_offsets)
    )
    value_mid = finish(partials, exercise_mid)
    mid_values = regroup_order(regroup(value_mid))
    value_early = finish(
        date_partials(
            states_early, mid_sources, mid_offsets, mid_values, mask_early, early_col_ids
        ),
        exercise_early,
    )
    return (value_mid, value_early)


def solution(mesh):
    in_specs = (
        P("src", None),
        P("src"),
        P("src", None),
        P("tgt", None),
        P("src"),
        P("tgt", None),
        P(),
        P("tgt", None),
        P("tgt", None),
        P(),
    )
    out_specs = (P("tgt", None), P("tgt", None))
    return jax.shard_map(
        per_device, mesh=mesh, in_specs=in_specs, out_specs=out_specs, check_vma=False
    )
```

```python
import jax
import jax.numpy as jnp
from jax import lax
from jax.sharding import PartitionSpec as P

BLOCK = 512


sharpness = 3.5
very_low = -1e30

def date_partials(targets, sources, offsets, values, tile_mask, col_tile_ids):
    row_count = targets.shape[0]
    factors = targets.shape[1]
    value_width = values.shape[1]
    row_tiles = row_count // BLOCK
    col_tiles = sources.shape[0] // BLOCK
    score_scale = sharpness / factors**0.5
    row_ids = lax.axis_index("tgt") * row_tiles + jnp.arange(row_tiles)
    local_mask = tile_mask[row_ids][:, col_tile_ids]
    source_tiles = sources.reshape(col_tiles, BLOCK, factors)
    offset_tiles = offsets.astype(jnp.float32).reshape(col_tiles, BLOCK)
    value_tiles = values.reshape(col_tiles, BLOCK, value_width)
    peaks, sums, weighted_all = ([], [], [])
    for row_block in range(row_tiles):
        target_rows = targets[row_block * BLOCK : (row_block + 1) * BLOCK]

        def step(carry, inputs):
            source_tile, offset_tile, value_tile, tile_live = inputs

            def active(carry_in):
                row_peak, weight_sum, weighted = carry_in
                scores = lax.dot_general(
                    target_rows,
                    source_tile,
                    (((1,), (1,)), ((), ())),
                    preferred_element_type=jnp.float32,
                )
                scores = scores * score_scale - offset_tile[None, :]
                new_peak = jnp.maximum(row_peak, jnp.max(scores, axis=1))
                shrink = jnp.exp(row_peak - new_peak)
                weights = jnp.exp(scores - new_peak[:, None])
                new_sum = weight_sum * shrink + jnp.sum(weights, axis=1)
                new_weighted = weighted * shrink[:, None] + jnp.dot(
                    weights.astype(jnp.bfloat16), value_tile, preferred_element_type=jnp.float32
                )
                return (new_peak, new_sum, new_weighted)

            def skipped(carry_in):
                return carry_in

            return (lax.cond(tile_live > 0, active, skipped, carry), None)

        start = (
            jnp.full((BLOCK,), very_low, jnp.float32),
            jnp.zeros((BLOCK,), jnp.float32),
            jnp.zeros((BLOCK, value_width), jnp.float32),
        )
        result, _ = lax.scan(
            step, start, (source_tiles, offset_tiles, value_tiles, local_mask[row_block])
        )
        peaks.append(result[0])
        sums.append(result[1])
        weighted_all.append(result[2])
    return (jnp.concatenate(peaks, 0), jnp.concatenate(sums, 0), jnp.concatenate(weighted_all, 0))


DIGIT_GROUPS = ((3, 0), (1, 2))


def digit_of(me, bits):
    return sum(((me >> b) & 1) << i for i, b in enumerate(bits))


def partner_perm(size, bits, k):
    pairs = []
    for i in range(size):
        j = i
        for n, b in enumerate(bits):
            if (k >> n) & 1:
                j ^= 1 << b
        pairs.append((i, j))
    return pairs


def merge_all(parts):
    width = parts[0].shape[1] - 2
    peaks = [p[:, width + 1] for p in parts]
    peak = peaks[0]
    for other in peaks[1:]:
        peak = jnp.maximum(peak, other)
    body = parts[0][:, : width + 1] * jnp.exp(peaks[0] - peak)[:, None]
    for p, pk in zip(parts[1:], peaks[1:]):
        body = body + p[:, : width + 1] * jnp.exp(pk - peak)[:, None]
    return jnp.concatenate([body, peak[:, None]], axis=1)


def finish(partials, exercise):
    row_peak, weight_sum, weighted = partials
    src_size = lax.axis_size("src")
    me = lax.axis_index("src")
    packed = jnp.concatenate([weighted, weight_sum[:, None], row_peak[:, None]], axis=1)
    exercise = exercise.astype(jnp.float32)
    for bits in DIGIT_GROUPS:
        radix = 1 << len(bits)
        rows = packed.shape[0] // radix
        d = digit_of(me, bits)
        parts = [lax.dynamic_slice_in_dim(packed, d * rows, rows, 0)]
        for k in range(1, radix):
            send = lax.dynamic_slice_in_dim(packed, (d ^ k) * rows, rows, 0)
            parts.append(lax.ppermute(send, "src", partner_perm(src_size, bits, k)))
        packed = merge_all(parts)
        exercise = lax.dynamic_slice_in_dim(exercise, d * rows, rows, 0)
    width = packed.shape[1] - 2
    continuation = packed[:, :width] / packed[:, width : width + 1]
    value = jnp.maximum(continuation, exercise).astype(jnp.bfloat16)
    for bits in reversed(DIGIT_GROUPS):
        radix = 1 << len(bits)
        rows = value.shape[0]
        d = digit_of(me, bits)
        whole = jnp.zeros((rows * radix, value.shape[1]), value.dtype)
        whole = lax.dynamic_update_slice_in_dim(whole, value, d * rows, 0)
        for k in range(1, radix):
            got = lax.ppermute(value, "src", partner_perm(src_size, bits, k))
            whole = lax.dynamic_update_slice_in_dim(whole, got, (d ^ k) * rows, 0)
        value = whole
    return value


def lin(t, s):
    return t * lax.axis_size("src") + s


def source_pair(t, s):
    x_count = lax.axis_size("tgt") // 8
    z_hi, x = t // (2 * x_count), (t // 2) % x_count
    return ((z_hi + s // 4) % 4) * x_count + (x + s % 4) % x_count


def regroup(block_rows):
    tgt_size = lax.axis_size("tgt")
    src_size = lax.axis_size("src")
    perms = ([], [])
    for t in range(tgt_size):
        for s in range(src_size):
            pair = source_pair(t, s)
            for flip in range(2):
                u = 2 * pair + ((t % 2) ^ flip)
                perms[flip].append((lin(u, s), lin(t, s)))
    return [lax.ppermute(block_rows, ("tgt", "src"), p) for p in perms]


def regroup_order(got):
    odd = lax.axis_index("tgt") % 2 == 1
    return jnp.concatenate(
        [jnp.where(odd, got[1], got[0]), jnp.where(odd, got[0], got[1])], 0
    )


def regroup_offsets(offsets):
    tgt_size = lax.axis_size("tgt")
    src_size = lax.axis_size("src")
    pairs = [
        (lin(t, source_pair(t, s)), lin(t, s)) for t in range(tgt_size) for s in range(src_size)
    ]
    return lax.ppermute(offsets, ("tgt", "src"), pairs)


def per_device(
    states_late,
    offset_late,
    values_late,
    states_mid,
    offset_mid,
    exercise_mid,
    mask_mid,
    states_early,
    exercise_early,
    mask_early,
):
    src_tiles = states_late.shape[0] // BLOCK
    col_ids = lax.axis_index("src") * src_tiles + jnp.arange(src_tiles)
    pair = source_pair(lax.axis_index("tgt"), lax.axis_index("src"))
    early_col_ids = pair * src_tiles + jnp.arange(src_tiles)
    mid_sources = regroup_order(regroup(states_mid))
    mid_offsets = regroup_offsets(offset_mid)
    partials = date_partials(states_mid, states_late, offset_late, values_late, mask_mid, col_ids)
    partials, mid_sources, mid_offsets = lax.optimization_barrier(
        (partials, mid_sources, mid_offsets)
    )
    value_mid = finish(partials, exercise_mid)
    mid_values = regroup_order(regroup(value_mid))
    value_early = finish(
        date_partials(
            states_early, mid_sources, mid_offsets, mid_values, mask_early, early_col_ids
        ),
        exercise_early,
    )
    return (value_mid, value_early)


def solution(mesh):
    in_specs = (
        P("src", None),
        P("src"),
        P("src", None),
        P("tgt", None),
        P("src"),
        P("tgt", None),
        P(),
        P("tgt", None),
        P("tgt", None),
        P(),
    )
    out_specs = (P("tgt", None), P("tgt", None))
    return jax.shard_map(
        per_device, mesh=mesh, in_specs=in_specs, out_specs=out_specs, check_vma=False
    )
```

```python
import jax
import jax.numpy as jnp
from jax import lax
from jax.sharding import PartitionSpec as P

BLOCK = 512


sharpness = 3.5
very_low = -1e30

def date_partials(targets, sources, offsets, values, tile_mask, col_tile_ids):
    row_count = targets.shape[0]
    factors = targets.shape[1]
    value_width = values.shape[1]
    row_tiles = row_count // BLOCK
    col_tiles = sources.shape[0] // BLOCK
    score_scale = sharpness / factors**0.5
    row_ids = lax.axis_index("tgt") * row_tiles + jnp.arange(row_tiles)
    local_mask = tile_mask[row_ids][:, col_tile_ids]
    source_tiles = sources.reshape(col_tiles, BLOCK, factors)
    offset_tiles = offsets.astype(jnp.float32).reshape(col_tiles, BLOCK)
    value_tiles = values.reshape(col_tiles, BLOCK, value_width)
    peaks, sums, weighted_all = ([], [], [])
    for row_block in range(row_tiles):
        target_rows = targets[row_block * BLOCK : (row_block + 1) * BLOCK]

        def step(carry, inputs):
            source_tile, offset_tile, value_tile, tile_live = inputs

            def active(carry_in):
                row_peak, weight_sum, weighted = carry_in
                scores = lax.dot_general(
                    target_rows,
                    source_tile,
                    (((1,), (1,)), ((), ())),
                    preferred_element_type=jnp.float32,
                )
                scores = scores * score_scale - offset_tile[None, :]
                new_peak = jnp.maximum(row_peak, jnp.max(scores, axis=1))
                shrink = jnp.exp(row_peak - new_peak)
                weights = jnp.exp(scores - new_peak[:, None])
                new_sum = weight_sum * shrink + jnp.sum(weights, axis=1)
                new_weighted = weighted * shrink[:, None] + jnp.dot(
                    weights.astype(jnp.bfloat16), value_tile, preferred_element_type=jnp.float32
                )
                return (new_peak, new_sum, new_weighted)

            def skipped(carry_in):
                return carry_in

            return (lax.cond(tile_live > 0, active, skipped, carry), None)

        start = (
            jnp.full((BLOCK,), very_low, jnp.float32),
            jnp.zeros((BLOCK,), jnp.float32),
            jnp.zeros((BLOCK, value_width), jnp.float32),
        )
        result, _ = lax.scan(
            step, start, (source_tiles, offset_tiles, value_tiles, local_mask[row_block])
        )
        peaks.append(result[0])
        sums.append(result[1])
        weighted_all.append(result[2])
    return (jnp.concatenate(peaks, 0), jnp.concatenate(sums, 0), jnp.concatenate(weighted_all, 0))


HALVING_BITS = (3,)
EXCHANGE_BITS = (0, 1, 2)


def xor_perm(size, bit):
    return [(i, i ^ (1 << bit)) for i in range(size)]


def merge(mine, theirs):
    width = mine.shape[1] - 2
    peak_a, peak_b = mine[:, width + 1], theirs[:, width + 1]
    peak = jnp.maximum(peak_a, peak_b)
    scale_a = jnp.exp(peak_a - peak)
    scale_b = jnp.exp(peak_b - peak)
    body = mine[:, : width + 1] * scale_a[:, None] + theirs[:, : width + 1] * scale_b[:, None]
    return jnp.concatenate([body, peak[:, None]], axis=1)


def finish(partials, exercise):
    row_peak, weight_sum, weighted = partials
    src_size = lax.axis_size("src")
    me = lax.axis_index("src")
    packed = jnp.concatenate([weighted, weight_sum[:, None], row_peak[:, None]], axis=1)
    exercise = exercise.astype(jnp.float32)
    for bit in HALVING_BITS:
        half = packed.shape[0] // 2
        mine_hi = (me >> bit) & 1
        keep = lax.dynamic_slice_in_dim(packed, mine_hi * half, half, 0)
        send = lax.dynamic_slice_in_dim(packed, (1 - mine_hi) * half, half, 0)
        packed = merge(keep, lax.ppermute(send, "src", xor_perm(src_size, bit)))
        exercise = lax.dynamic_slice_in_dim(exercise, mine_hi * half, half, 0)
    for bit in EXCHANGE_BITS:
        packed = merge(packed, lax.ppermute(packed, "src", xor_perm(src_size, bit)))
    width = packed.shape[1] - 2
    continuation = packed[:, :width] / packed[:, width : width + 1]
    value = jnp.maximum(continuation, exercise).astype(jnp.bfloat16)
    for bit in reversed(HALVING_BITS):
        mine_hi = (me >> bit) & 1
        got = lax.ppermute(value, "src", xor_perm(src_size, bit))
        value = jnp.where(
            mine_hi == 1,
            jnp.concatenate([got, value], 0),
            jnp.concatenate([value, got], 0),
        )
    return value


def lin(t, s):
    return t * lax.axis_size("src") + s


def source_pair(t, s):
    x_count = lax.axis_size("tgt") // 8
    z_hi, x = t // (2 * x_count), (t // 2) % x_count
    return ((z_hi + s // 4) % 4) * x_count + (x + s % 4) % x_count


def regroup(block_rows):
    tgt_size = lax.axis_size("tgt")
    src_size = lax.axis_size("src")
    perms = ([], [])
    for t in range(tgt_size):
        for s in range(src_size):
            pair = source_pair(t, s)
            for flip in range(2):
                u = 2 * pair + ((t % 2) ^ flip)
                perms[flip].append((lin(u, s), lin(t, s)))
    return [lax.ppermute(block_rows, ("tgt", "src"), p) for p in perms]


def regroup_order(got):
    odd = lax.axis_index("tgt") % 2 == 1
    return jnp.concatenate(
        [jnp.where(odd, got[1], got[0]), jnp.where(odd, got[0], got[1])], 0
    )


def regroup_offsets(offsets):
    tgt_size = lax.axis_size("tgt")
    src_size = lax.axis_size("src")
    pairs = [
        (lin(t, source_pair(t, s)), lin(t, s)) for t in range(tgt_size) for s in range(src_size)
    ]
    return lax.ppermute(offsets, ("tgt", "src"), pairs)


def per_device(
    states_late,
    offset_late,
    values_late,
    states_mid,
    offset_mid,
    exercise_mid,
    mask_mid,
    states_early,
    exercise_early,
    mask_early,
):
    src_tiles = states_late.shape[0] // BLOCK
    col_ids = lax.axis_index("src") * src_tiles + jnp.arange(src_tiles)
    pair = source_pair(lax.axis_index("tgt"), lax.axis_index("src"))
    early_col_ids = pair * src_tiles + jnp.arange(src_tiles)
    mid_sources = regroup_order(regroup(states_mid))
    mid_offsets = regroup_offsets(offset_mid)
    partials = date_partials(states_mid, states_late, offset_late, values_late, mask_mid, col_ids)
    partials, mid_sources, mid_offsets = lax.optimization_barrier(
        (partials, mid_sources, mid_offsets)
    )
    value_mid = finish(partials, exercise_mid)
    mid_values = regroup_order(regroup(value_mid))
    value_early = finish(
        date_partials(
            states_early, mid_sources, mid_offsets, mid_values, mask_early, early_col_ids
        ),
        exercise_early,
    )
    return (value_mid, value_early)


def solution(mesh):
    in_specs = (
        P("src", None),
        P("src"),
        P("src", None),
        P("tgt", None),
        P("src"),
        P("tgt", None),
        P(),
        P("tgt", None),
        P("tgt", None),
        P(),
    )
    out_specs = (P("tgt", None), P("tgt", None))
    return jax.shard_map(
        per_device, mesh=mesh, in_specs=in_specs, out_specs=out_specs, check_vma=False
    )
```

```python
import jax
import jax.numpy as jnp
from jax import lax
from jax.experimental import pallas as pl
from jax.experimental.pallas import tpu as pltpu
from jax.sharding import PartitionSpec as P

BLOCK = 512


sharpness = 3.5
very_low = -1e30

def partials_kernel(mask_ref, x_ref, y_ref, off_ref, v_ref, out_ref, m_ref, l_ref, acc_ref, *, scale, col_tiles):
    i = pl.program_id(0)
    j = pl.program_id(1)

    @pl.when(j == 0)
    def _():
        m_ref[...] = jnp.full(m_ref.shape, very_low, jnp.float32)
        l_ref[...] = jnp.zeros(l_ref.shape, jnp.float32)
        acc_ref[...] = jnp.zeros(acc_ref.shape, jnp.float32)

    @pl.when(mask_ref[i * col_tiles + j] > 0)
    def _():
        s = lax.dot_general(x_ref[...], y_ref[...], (((1,), (1,)), ((), ())), preferred_element_type=jnp.float32)
        s = s * scale - off_ref[...]
        m_old = m_ref[...]
        m_new = jnp.maximum(m_old, jnp.max(s, axis=1, keepdims=True))
        shrink = jnp.exp(m_old - m_new)
        p = jnp.exp(s - m_new)
        l_ref[...] = l_ref[...] * shrink + jnp.sum(p, axis=1, keepdims=True)
        acc_ref[...] = acc_ref[...] * shrink + jnp.dot(p.astype(jnp.bfloat16), v_ref[...], preferred_element_type=jnp.float32)
        m_ref[...] = m_new

    @pl.when(j == col_tiles - 1)
    def _():
        w = acc_ref.shape[1]
        out_ref[:, 0:w] = acc_ref[...]
        out_ref[:, w:w + 1] = l_ref[...]
        out_ref[:, w + 1:w + 2] = m_ref[...]


def date_partials_kernel(targets, sources, offsets, values, live):
    rows, factors = targets.shape
    cols = sources.shape[0]
    width = values.shape[1]
    row_tiles, col_tiles = rows // BLOCK, cols // BLOCK
    kernel = lambda *refs: partials_kernel(*refs, scale=sharpness / factors**0.5, col_tiles=col_tiles)
    return pl.pallas_call(
        kernel,
        out_shape=jax.ShapeDtypeStruct((rows, width + 2), jnp.float32),
        grid_spec=pltpu.PrefetchScalarGridSpec(
            num_scalar_prefetch=1,
            grid=(row_tiles, col_tiles),
            in_specs=[
                pl.BlockSpec((BLOCK, factors), lambda i, j, m: (i, 0)),
                pl.BlockSpec((BLOCK, factors), lambda i, j, m: (j, 0)),
                pl.BlockSpec((1, BLOCK), lambda i, j, m: (0, j)),
                pl.BlockSpec((BLOCK, width), lambda i, j, m: (j, 0)),
            ],
            out_specs=pl.BlockSpec((BLOCK, width + 2), lambda i, j, m: (i, 0)),
            scratch_shapes=[
                pltpu.VMEM((BLOCK, 1), jnp.float32),
                pltpu.VMEM((BLOCK, 1), jnp.float32),
                pltpu.VMEM((BLOCK, width), jnp.float32),
            ],
        ),
        compiler_params=pltpu.CompilerParams(dimension_semantics=("arbitrary", "arbitrary")),
    )(live.reshape(-1).astype(jnp.int32), targets, sources, offsets.astype(jnp.float32).reshape(1, cols), values)


def date_partials(targets, sources, offsets, values, tile_mask, col_tile_ids):
    row_tiles = targets.shape[0] // BLOCK
    row_ids = lax.axis_index("tgt") * row_tiles + jnp.arange(row_tiles)
    live = tile_mask[row_ids][:, col_tile_ids]
    return date_partials_kernel(targets, sources, offsets, values, live)


HALVING_BITS = (3,)
EXCHANGE_BITS = (0, 1, 2)


def xor_perm(size, bit):
    return [(i, i ^ (1 << bit)) for i in range(size)]


def merge(mine, theirs):
    width = mine.shape[1] - 2
    peak_a, peak_b = mine[:, width + 1], theirs[:, width + 1]
    peak = jnp.maximum(peak_a, peak_b)
    scale_a = jnp.exp(peak_a - peak)
    scale_b = jnp.exp(peak_b - peak)
    body = mine[:, : width + 1] * scale_a[:, None] + theirs[:, : width + 1] * scale_b[:, None]
    return jnp.concatenate([body, peak[:, None]], axis=1)


def finish(partials, exercise):
    src_size = lax.axis_size("src")
    me = lax.axis_index("src")
    packed = partials
    exercise = exercise.astype(jnp.float32)
    for bit in HALVING_BITS:
        half = packed.shape[0] // 2
        mine_hi = (me >> bit) & 1
        keep = lax.dynamic_slice_in_dim(packed, mine_hi * half, half, 0)
        send = lax.dynamic_slice_in_dim(packed, (1 - mine_hi) * half, half, 0)
        packed = merge(keep, lax.ppermute(send, "src", xor_perm(src_size, bit)))
        exercise = lax.dynamic_slice_in_dim(exercise, mine_hi * half, half, 0)
    for bit in EXCHANGE_BITS:
        packed = merge(packed, lax.ppermute(packed, "src", xor_perm(src_size, bit)))
    width = packed.shape[1] - 2
    continuation = packed[:, :width] / packed[:, width : width + 1]
    value = jnp.maximum(continuation, exercise).astype(jnp.bfloat16)
    for bit in reversed(HALVING_BITS):
        mine_hi = (me >> bit) & 1
        got = lax.ppermute(value, "src", xor_perm(src_size, bit))
        value = jnp.where(
            mine_hi == 1,
            jnp.concatenate([got, value], 0),
            jnp.concatenate([value, got], 0),
        )
    return value


def lin(t, s):
    return t * lax.axis_size("src") + s


def source_pair(t, s):
    x_count = lax.axis_size("tgt") // 8
    z_hi, x = t // (2 * x_count), (t // 2) % x_count
    return ((z_hi + s // 4) % 4) * x_count + (x + s % 4) % x_count


def regroup(block_rows):
    tgt_size = lax.axis_size("tgt")
    src_size = lax.axis_size("src")
    perms = ([], [])
    for t in range(tgt_size):
        for s in range(src_size):
            pair = source_pair(t, s)
            for flip in range(2):
                u = 2 * pair + ((t % 2) ^ flip)
                perms[flip].append((lin(u, s), lin(t, s)))
    return [lax.ppermute(block_rows, ("tgt", "src"), p) for p in perms]


def regroup_order(got):
    odd = lax.axis_index("tgt") % 2 == 1
    return jnp.concatenate(
        [jnp.where(odd, got[1], got[0]), jnp.where(odd, got[0], got[1])], 0
    )


def regroup_offsets(offsets):
    tgt_size = lax.axis_size("tgt")
    src_size = lax.axis_size("src")
    pairs = [
        (lin(t, source_pair(t, s)), lin(t, s)) for t in range(tgt_size) for s in range(src_size)
    ]
    return lax.ppermute(offsets, ("tgt", "src"), pairs)


def per_device(
    states_late,
    offset_late,
    values_late,
    states_mid,
    offset_mid,
    exercise_mid,
    mask_mid,
    states_early,
    exercise_early,
    mask_early,
):
    src_tiles = states_late.shape[0] // BLOCK
    col_ids = lax.axis_index("src") * src_tiles + jnp.arange(src_tiles)
    pair = source_pair(lax.axis_index("tgt"), lax.axis_index("src"))
    early_col_ids = pair * src_tiles + jnp.arange(src_tiles)
    mid_sources = regroup_order(regroup(states_mid))
    mid_offsets = regroup_offsets(offset_mid)
    partials = date_partials(states_mid, states_late, offset_late, values_late, mask_mid, col_ids)
    partials, mid_sources, mid_offsets = lax.optimization_barrier(
        (partials, mid_sources, mid_offsets)
    )
    value_mid = finish(partials, exercise_mid)
    mid_values = regroup_order(regroup(value_mid))
    value_early = finish(
        date_partials(
            states_early, mid_sources, mid_offsets, mid_values, mask_early, early_col_ids
        ),
        exercise_early,
    )
    return (value_mid, value_early)


def solution(mesh):
    in_specs = (
        P("src", None),
        P("src"),
        P("src", None),
        P("tgt", None),
        P("src"),
        P("tgt", None),
        P(),
        P("tgt", None),
        P("tgt", None),
        P(),
    )
    out_specs = (P("tgt", None), P("tgt", None))
    return jax.shard_map(
        per_device, mesh=mesh, in_specs=in_specs, out_specs=out_specs, check_vma=False
    )
```

```python
import jax
import jax.numpy as jnp
from jax import lax
from jax.experimental import pallas as pl
from jax.experimental.pallas import tpu as pltpu
from jax.sharding import PartitionSpec as P

BLOCK = 512


sharpness = 3.5
very_low = -1e30

def partials_kernel(mask_ref, x_ref, y_ref, off_ref, v_ref, out_ref, m_ref, l_ref, acc_ref, *, scale, col_tiles):
    i = pl.program_id(0)
    j = pl.program_id(1)

    @pl.when(j == 0)
    def _():
        m_ref[...] = jnp.full(m_ref.shape, very_low, jnp.float32)
        l_ref[...] = jnp.zeros(l_ref.shape, jnp.float32)
        acc_ref[...] = jnp.zeros(acc_ref.shape, jnp.float32)

    @pl.when(mask_ref[i * col_tiles + j] > 0)
    def _():
        s = lax.dot_general(y_ref[...], x_ref[...], (((1,), (1,)), ((), ())), preferred_element_type=jnp.float32)
        s = s * scale - off_ref[...]
        m_old = m_ref[...]
        m_new = jnp.maximum(m_old, jnp.max(s, axis=0, keepdims=True))
        shrink = jnp.exp(m_old - m_new)
        p = jnp.exp(s - m_new)
        l_ref[...] = l_ref[...] * shrink + jnp.sum(p, axis=0, keepdims=True)
        acc_ref[...] = acc_ref[...] * shrink + jnp.dot(v_ref[...], p.astype(jnp.bfloat16), preferred_element_type=jnp.float32)
        m_ref[...] = m_new

    @pl.when(j == col_tiles - 1)
    def _():
        w = acc_ref.shape[0]
        out_ref[0:w, :] = acc_ref[...]
        out_ref[w:w + 1, :] = l_ref[...]
        out_ref[w + 1:w + 2, :] = m_ref[...]


def date_partials_kernel(targets, sources, offsets, values_t, live):
    rows, factors = targets.shape
    cols = sources.shape[0]
    width = values_t.shape[0]
    row_tiles, col_tiles = rows // BLOCK, cols // BLOCK
    kernel = lambda *refs: partials_kernel(*refs, scale=sharpness / factors**0.5, col_tiles=col_tiles)
    return pl.pallas_call(
        kernel,
        out_shape=jax.ShapeDtypeStruct((width + 2, rows), jnp.float32),
        grid_spec=pltpu.PrefetchScalarGridSpec(
            num_scalar_prefetch=1,
            grid=(row_tiles, col_tiles),
            in_specs=[
                pl.BlockSpec((BLOCK, factors), lambda i, j, m: (i, 0)),
                pl.BlockSpec((BLOCK, factors), lambda i, j, m: (j, 0)),
                pl.BlockSpec((BLOCK, 1), lambda i, j, m: (j, 0)),
                pl.BlockSpec((width, BLOCK), lambda i, j, m: (0, j)),
            ],
            out_specs=pl.BlockSpec((width + 2, BLOCK), lambda i, j, m: (0, i)),
            scratch_shapes=[
                pltpu.VMEM((1, BLOCK), jnp.float32),
                pltpu.VMEM((1, BLOCK), jnp.float32),
                pltpu.VMEM((width, BLOCK), jnp.float32),
            ],
        ),
        compiler_params=pltpu.CompilerParams(dimension_semantics=("arbitrary", "arbitrary")),
    )(live.reshape(-1).astype(jnp.int32), targets, sources, offsets.astype(jnp.float32).reshape(cols, 1), values_t)


def date_partials(targets, sources, offsets, values_t, tile_mask, col_tile_ids):
    row_tiles = targets.shape[0] // BLOCK
    row_ids = lax.axis_index("tgt") * row_tiles + jnp.arange(row_tiles)
    live = tile_mask[row_ids][:, col_tile_ids]
    return date_partials_kernel(targets, sources, offsets, values_t, live)


HALVING_BITS = (3,)
EXCHANGE_BITS = (0, 1, 2)


def xor_perm(size, bit):
    return [(i, i ^ (1 << bit)) for i in range(size)]


def merge(mine, theirs):
    width = mine.shape[0] - 2
    peak_a, peak_b = mine[width + 1 :], theirs[width + 1 :]
    peak = jnp.maximum(peak_a, peak_b)
    scale_a = jnp.exp(peak_a - peak)
    scale_b = jnp.exp(peak_b - peak)
    body = mine[: width + 1] * scale_a + theirs[: width + 1] * scale_b
    return jnp.concatenate([body, peak], axis=0)


def finish(packed, exercise):
    src_size = lax.axis_size("src")
    me = lax.axis_index("src")
    exercise = exercise.astype(jnp.float32)
    for bit in HALVING_BITS:
        half = packed.shape[1] // 2
        mine_hi = (me >> bit) & 1
        keep = lax.dynamic_slice_in_dim(packed, mine_hi * half, half, 1)
        send = lax.dynamic_slice_in_dim(packed, (1 - mine_hi) * half, half, 1)
        packed = merge(keep, lax.ppermute(send, "src", xor_perm(src_size, bit)))
        exercise = lax.dynamic_slice_in_dim(exercise, mine_hi * half, half, 0)
    for bit in EXCHANGE_BITS:
        packed = merge(packed, lax.ppermute(packed, "src", xor_perm(src_size, bit)))
    width = packed.shape[0] - 2
    continuation = packed[:width] / packed[width : width + 1]
    value = jnp.maximum(continuation, exercise.T).astype(jnp.bfloat16)
    for bit in reversed(HALVING_BITS):
        mine_hi = (me >> bit) & 1
        got = lax.ppermute(value, "src", xor_perm(src_size, bit))
        value = jnp.where(
            mine_hi == 1,
            jnp.concatenate([got, value], 1),
            jnp.concatenate([value, got], 1),
        )
    return value


def lin(t, s):
    return t * lax.axis_size("src") + s


def source_pair(t, s):
    x_count = lax.axis_size("tgt") // 8
    z_hi, x = t // (2 * x_count), (t // 2) % x_count
    return ((z_hi + s // 4) % 4) * x_count + (x + s % 4) % x_count


def regroup(block_rows):
    tgt_size = lax.axis_size("tgt")
    src_size = lax.axis_size("src")
    perms = ([], [])
    for t in range(tgt_size):
        for s in range(src_size):
            pair = source_pair(t, s)
            for flip in range(2):
                u = 2 * pair + ((t % 2) ^ flip)
                perms[flip].append((lin(u, s), lin(t, s)))
    return [lax.ppermute(block_rows, ("tgt", "src"), p) for p in perms]


def regroup_order(got, axis=0):
    odd = lax.axis_index("tgt") % 2 == 1
    return jnp.concatenate(
        [jnp.where(odd, got[1], got[0]), jnp.where(odd, got[0], got[1])], axis
    )


def regroup_offsets(offsets):
    tgt_size = lax.axis_size("tgt")
    src_size = lax.axis_size("src")
    pairs = [
        (lin(t, source_pair(t, s)), lin(t, s)) for t in range(tgt_size) for s in range(src_size)
    ]
    return lax.ppermute(offsets, ("tgt", "src"), pairs)


def per_device(
    states_late,
    offset_late,
    values_late,
    states_mid,
    offset_mid,
    exercise_mid,
    mask_mid,
    states_early,
    exercise_early,
    mask_early,
):
    src_tiles = states_late.shape[0] // BLOCK
    col_ids = lax.axis_index("src") * src_tiles + jnp.arange(src_tiles)
    pair = source_pair(lax.axis_index("tgt"), lax.axis_index("src"))
    early_col_ids = pair * src_tiles + jnp.arange(src_tiles)
    mid_sources = regroup_order(regroup(states_mid))
    mid_offsets = regroup_offsets(offset_mid)
    partials = date_partials(states_mid, states_late, offset_late, values_late.T, mask_mid, col_ids)
    partials, mid_sources, mid_offsets = lax.optimization_barrier(
        (partials, mid_sources, mid_offsets)
    )
    value_mid_t = finish(partials, exercise_mid)
    mid_values_t = regroup_order(regroup(value_mid_t), axis=1)
    value_early_t = finish(
        date_partials(
            states_early, mid_sources, mid_offsets, mid_values_t, mask_early, early_col_ids
        ),
        exercise_early,
    )
    value_mid, value_early = value_mid_t.T, value_early_t.T
    return (value_mid, value_early)


def solution(mesh):
    in_specs = (
        P("src", None),
        P("src"),
        P("src", None),
        P("tgt", None),
        P("src"),
        P("tgt", None),
        P(),
        P("tgt", None),
        P("tgt", None),
        P(),
    )
    out_specs = (P("tgt", None), P("tgt", None))
    return jax.shard_map(
        per_device, mesh=mesh, in_specs=in_specs, out_specs=out_specs, check_vma=False
    )
```

```python
import jax
import jax.numpy as jnp
from jax import lax
from jax.experimental import pallas as pl
from jax.experimental.pallas import tpu as pltpu
from jax.sharding import PartitionSpec as P

BLOCK = 512


sharpness = 3.5
very_low = -1e30

def partials_kernel(mask_ref, x_ref, y_ref, off_ref, v_ref, out_ref, m_ref, l_ref, acc_ref, *, scale, col_tiles):
    i = pl.program_id(0)
    j = pl.program_id(1)

    @pl.when(j == 0)
    def _():
        m_ref[...] = jnp.full(m_ref.shape, very_low, jnp.float32)
        l_ref[...] = jnp.zeros(l_ref.shape, jnp.float32)
        acc_ref[...] = jnp.zeros(acc_ref.shape, jnp.float32)

    @pl.when(mask_ref[i * col_tiles + j] > 0)
    def _():
        s = lax.dot_general(y_ref[...], x_ref[...], (((1,), (1,)), ((), ())), preferred_element_type=jnp.float32)
        s = s * scale - off_ref[...]
        m_old = m_ref[...]
        m_new = jnp.maximum(m_old, jnp.max(s, axis=0, keepdims=True))
        shrink = jnp.exp(m_old - m_new)
        p = jnp.exp(s - m_new)
        l_ref[...] = l_ref[...] * shrink + jnp.sum(p, axis=0, keepdims=True)
        acc_ref[...] = acc_ref[...] * shrink + jnp.dot(v_ref[...], p.astype(jnp.bfloat16), preferred_element_type=jnp.float32)
        m_ref[...] = m_new

    @pl.when(j == col_tiles - 1)
    def _():
        w = acc_ref.shape[0]
        out_ref[0:w, :] = acc_ref[...]
        out_ref[w:w + 1, :] = l_ref[...]
        out_ref[w + 1:w + 2, :] = m_ref[...]


def date_partials_kernel(targets, sources, offsets, values_t, live):
    rows, factors = targets.shape
    cols = sources.shape[0]
    width = values_t.shape[0]
    row_tiles, col_tiles = rows // BLOCK, cols // BLOCK
    kernel = lambda *refs: partials_kernel(*refs, scale=sharpness / factors**0.5, col_tiles=col_tiles)
    return pl.pallas_call(
        kernel,
        out_shape=jax.ShapeDtypeStruct((width + 2, rows), jnp.float32),
        grid_spec=pltpu.PrefetchScalarGridSpec(
            num_scalar_prefetch=1,
            grid=(row_tiles, col_tiles),
            in_specs=[
                pl.BlockSpec((BLOCK, factors), lambda i, j, m: (i, 0)),
                pl.BlockSpec((BLOCK, factors), lambda i, j, m: (j, 0)),
                pl.BlockSpec((BLOCK, 1), lambda i, j, m: (j, 0)),
                pl.BlockSpec((width, BLOCK), lambda i, j, m: (0, j)),
            ],
            out_specs=pl.BlockSpec((width + 2, BLOCK), lambda i, j, m: (0, i)),
            scratch_shapes=[
                pltpu.VMEM((1, BLOCK), jnp.float32),
                pltpu.VMEM((1, BLOCK), jnp.float32),
                pltpu.VMEM((width, BLOCK), jnp.float32),
            ],
        ),
        compiler_params=pltpu.CompilerParams(dimension_semantics=("arbitrary", "arbitrary")),
    )(live.reshape(-1).astype(jnp.int32), targets, sources, offsets.astype(jnp.float32).reshape(cols, 1), values_t)


def weights_kernel(mask_ref, x_ref, y_ref, off_ref, p_ref, stats_ref, *, scale, col_tiles):
    i = pl.program_id(0)

    def scores(j):
        y = y_ref[j * BLOCK : (j + 1) * BLOCK, :]
        s = lax.dot_general(y, x_ref[...], (((1,), (1,)), ((), ())), preferred_element_type=jnp.float32)
        return s * scale - off_ref[j * BLOCK : (j + 1) * BLOCK, :]

    stats_ref[...] = jnp.concatenate(
        [jnp.zeros((1, BLOCK), jnp.float32), jnp.full((1, BLOCK), very_low, jnp.float32)], 0
    )
    for j in range(col_tiles):

        @pl.when(mask_ref[i * col_tiles + j] > 0)
        def _():
            tile_peak = jnp.max(scores(j), axis=0, keepdims=True)
            stats_ref[1:2, :] = jnp.maximum(stats_ref[1:2, :], tile_peak)

    for j in range(col_tiles):
        live = mask_ref[i * col_tiles + j] > 0

        @pl.when(live)
        def _():
            p = jnp.exp(scores(j) - stats_ref[1:2, :])
            p_ref[j * BLOCK : (j + 1) * BLOCK, :] = p.astype(jnp.bfloat16)
            stats_ref[0:1, :] = stats_ref[0:1, :] + jnp.sum(p, axis=0, keepdims=True)

        @pl.when(jnp.logical_not(live))
        def _():
            p_ref[j * BLOCK : (j + 1) * BLOCK, :] = jnp.zeros((BLOCK, BLOCK), jnp.bfloat16)


def date_weights_kernel(targets, sources, offsets, live):
    rows, factors = targets.shape
    cols = sources.shape[0]
    row_tiles, col_tiles = rows // BLOCK, cols // BLOCK
    kernel = lambda *refs: weights_kernel(*refs, scale=sharpness / factors**0.5, col_tiles=col_tiles)
    return pl.pallas_call(
        kernel,
        out_shape=(
            jax.ShapeDtypeStruct((cols, rows), jnp.bfloat16),
            jax.ShapeDtypeStruct((2, rows), jnp.float32),
        ),
        grid_spec=pltpu.PrefetchScalarGridSpec(
            num_scalar_prefetch=1,
            grid=(row_tiles,),
            in_specs=[
                pl.BlockSpec((BLOCK, factors), lambda i, m: (i, 0)),
                pl.BlockSpec((cols, factors), lambda i, m: (0, 0)),
                pl.BlockSpec((cols, 1), lambda i, m: (0, 0)),
            ],
            out_specs=(
                pl.BlockSpec((cols, BLOCK), lambda i, m: (0, i)),
                pl.BlockSpec((2, BLOCK), lambda i, m: (0, i)),
            ),
        ),
        compiler_params=pltpu.CompilerParams(dimension_semantics=("arbitrary",)),
    )(live.reshape(-1).astype(jnp.int32), targets, sources, offsets.astype(jnp.float32).reshape(cols, 1))


def local_live(targets, tile_mask, col_tile_ids):
    row_tiles = targets.shape[0] // BLOCK
    row_ids = lax.axis_index("tgt") * row_tiles + jnp.arange(row_tiles)
    return tile_mask[row_ids][:, col_tile_ids]


def date_partials(targets, sources, offsets, values_t, tile_mask, col_tile_ids):
    live = local_live(targets, tile_mask, col_tile_ids)
    return date_partials_kernel(targets, sources, offsets, values_t, live)


HALVING_BITS = (3,)
EXCHANGE_BITS = (0, 1, 2)


def xor_perm(size, bit):
    return [(i, i ^ (1 << bit)) for i in range(size)]


def merge(mine, theirs):
    width = mine.shape[0] - 2
    peak_a, peak_b = mine[width + 1 :], theirs[width + 1 :]
    peak = jnp.maximum(peak_a, peak_b)
    scale_a = jnp.exp(peak_a - peak)
    scale_b = jnp.exp(peak_b - peak)
    body = mine[: width + 1] * scale_a + theirs[: width + 1] * scale_b
    return jnp.concatenate([body, peak], axis=0)


def finish(packed, exercise):
    src_size = lax.axis_size("src")
    me = lax.axis_index("src")
    exercise = exercise.astype(jnp.float32)
    for bit in HALVING_BITS:
        half = packed.shape[1] // 2
        mine_hi = (me >> bit) & 1
        keep = lax.dynamic_slice_in_dim(packed, mine_hi * half, half, 1)
        send = lax.dynamic_slice_in_dim(packed, (1 - mine_hi) * half, half, 1)
        packed = merge(keep, lax.ppermute(send, "src", xor_perm(src_size, bit)))
        exercise = lax.dynamic_slice_in_dim(exercise, mine_hi * half, half, 0)
    for bit in EXCHANGE_BITS:
        packed = merge(packed, lax.ppermute(packed, "src", xor_perm(src_size, bit)))
    width = packed.shape[0] - 2
    continuation = packed[:width] / packed[width : width + 1]
    value = jnp.maximum(continuation, exercise.T).astype(jnp.bfloat16)
    for bit in reversed(HALVING_BITS):
        mine_hi = (me >> bit) & 1
        got = lax.ppermute(value, "src", xor_perm(src_size, bit))
        value = jnp.where(
            mine_hi == 1,
            jnp.concatenate([got, value], 1),
            jnp.concatenate([value, got], 1),
        )
    return value


def lin(t, s):
    return t * lax.axis_size("src") + s


def source_pair(t, s):
    x_count = lax.axis_size("tgt") // 8
    z_hi, x = t // (2 * x_count), (t // 2) % x_count
    return ((z_hi + s // 4) % 4) * x_count + (x + s % 4) % x_count


def regroup(block_rows):
    tgt_size = lax.axis_size("tgt")
    src_size = lax.axis_size("src")
    perms = ([], [])
    for t in range(tgt_size):
        for s in range(src_size):
            pair = source_pair(t, s)
            for flip in range(2):
                u = 2 * pair + ((t % 2) ^ flip)
                perms[flip].append((lin(u, s), lin(t, s)))
    return [lax.ppermute(block_rows, ("tgt", "src"), p) for p in perms]


def regroup_order(got, axis=0):
    odd = lax.axis_index("tgt") % 2 == 1
    return jnp.concatenate(
        [jnp.where(odd, got[1], got[0]), jnp.where(odd, got[0], got[1])], axis
    )


def regroup_offsets(offsets):
    tgt_size = lax.axis_size("tgt")
    src_size = lax.axis_size("src")
    pairs = [
        (lin(t, source_pair(t, s)), lin(t, s)) for t in range(tgt_size) for s in range(src_size)
    ]
    return lax.ppermute(offsets, ("tgt", "src"), pairs)


def per_device(
    states_late,
    offset_late,
    values_late,
    states_mid,
    offset_mid,
    exercise_mid,
    mask_mid,
    states_early,
    exercise_early,
    mask_early,
):
    src_tiles = states_late.shape[0] // BLOCK
    col_ids = lax.axis_index("src") * src_tiles + jnp.arange(src_tiles)
    pair = source_pair(lax.axis_index("tgt"), lax.axis_index("src"))
    early_col_ids = pair * src_tiles + jnp.arange(src_tiles)
    mid_sources = regroup_order(regroup(states_mid))
    mid_offsets = regroup_offsets(offset_mid)
    partials = date_partials(states_mid, states_late, offset_late, values_late.T, mask_mid, col_ids)
    partials, mid_sources, mid_offsets = lax.optimization_barrier(
        (partials, mid_sources, mid_offsets)
    )
    early_weights, early_stats = date_weights_kernel(
        states_early, mid_sources, mid_offsets, local_live(states_early, mask_early, early_col_ids)
    )
    value_mid_t = finish(partials, exercise_mid)
    mid_values_t = regroup_order(regroup(value_mid_t), axis=1)
    early_weighted = jnp.dot(mid_values_t, early_weights, preferred_element_type=jnp.float32)
    value_early_t = finish(jnp.concatenate([early_weighted, early_stats], 0), exercise_early)
    value_mid, value_early = value_mid_t.T, value_early_t.T
    return (value_mid, value_early)


def solution(mesh):
    in_specs = (
        P("src", None),
        P("src"),
        P("src", None),
        P("tgt", None),
        P("src"),
        P("tgt", None),
        P(),
        P("tgt", None),
        P("tgt", None),
        P(),
    )
    out_specs = (P("tgt", None), P("tgt", None))
    return jax.shard_map(
        per_device, mesh=mesh, in_specs=in_specs, out_specs=out_specs, check_vma=False
    )
```

```python
import jax
import jax.numpy as jnp
from jax import lax
from jax.experimental import pallas as pl
from jax.experimental.pallas import tpu as pltpu
from jax.sharding import PartitionSpec as P

BLOCK = 512


sharpness = 3.5
very_low = -1e30

def partials_kernel(mask_ref, x_ref, y_ref, off_ref, v_ref, out_ref, m_ref, l_ref, acc_ref, *, scale, col_tiles):
    i = pl.program_id(0)
    j = pl.program_id(1)

    @pl.when(j == 0)
    def _():
        m_ref[...] = jnp.full(m_ref.shape, very_low, jnp.float32)
        l_ref[...] = jnp.zeros(l_ref.shape, jnp.float32)
        acc_ref[...] = jnp.zeros(acc_ref.shape, jnp.float32)

    @pl.when(mask_ref[i * col_tiles + j] > 0)
    def _():
        s = lax.dot_general(y_ref[...], x_ref[...], (((1,), (1,)), ((), ())), preferred_element_type=jnp.float32)
        s = s * scale - off_ref[...]
        m_old = m_ref[...]
        m_new = jnp.maximum(m_old, jnp.max(s, axis=0, keepdims=True))
        shrink = jnp.exp(m_old - m_new)
        p = jnp.exp(s - m_new)
        l_ref[...] = l_ref[...] * shrink + jnp.sum(p, axis=0, keepdims=True)
        acc_ref[...] = acc_ref[...] * shrink + jnp.dot(v_ref[...], p.astype(jnp.bfloat16), preferred_element_type=jnp.float32)
        m_ref[...] = m_new

    @pl.when(j == col_tiles - 1)
    def _():
        w = acc_ref.shape[0]
        out_ref[0:w, :] = acc_ref[...]
        out_ref[w:w + 1, :] = l_ref[...]
        out_ref[w + 1:w + 2, :] = m_ref[...]


def date_partials_kernel(targets, sources, offsets, values_t, live):
    rows, factors = targets.shape
    cols = sources.shape[0]
    width = values_t.shape[0]
    row_tiles, col_tiles = rows // BLOCK, cols // BLOCK
    kernel = lambda *refs: partials_kernel(*refs, scale=sharpness / factors**0.5, col_tiles=col_tiles)
    return pl.pallas_call(
        kernel,
        out_shape=jax.ShapeDtypeStruct((width + 2, rows), jnp.float32),
        grid_spec=pltpu.PrefetchScalarGridSpec(
            num_scalar_prefetch=1,
            grid=(row_tiles, col_tiles),
            in_specs=[
                pl.BlockSpec((BLOCK, factors), lambda i, j, m: (i, 0)),
                pl.BlockSpec((BLOCK, factors), lambda i, j, m: (j, 0)),
                pl.BlockSpec((BLOCK, 1), lambda i, j, m: (j, 0)),
                pl.BlockSpec((width, BLOCK), lambda i, j, m: (0, j)),
            ],
            out_specs=pl.BlockSpec((width + 2, BLOCK), lambda i, j, m: (0, i)),
            scratch_shapes=[
                pltpu.VMEM((1, BLOCK), jnp.float32),
                pltpu.VMEM((1, BLOCK), jnp.float32),
                pltpu.VMEM((width, BLOCK), jnp.float32),
            ],
        ),
        compiler_params=pltpu.CompilerParams(dimension_semantics=("arbitrary", "arbitrary")),
    )(live.reshape(-1).astype(jnp.int32), targets, sources, offsets.astype(jnp.float32).reshape(cols, 1), values_t)


def weights_kernel(mask_ref, x_ref, y_ref, off_ref, p_ref, stats_ref, *, scale, col_tiles):
    i = pl.program_id(0)

    def scores(j):
        y = y_ref[j * BLOCK : (j + 1) * BLOCK, :]
        s = lax.dot_general(y, x_ref[...], (((1,), (1,)), ((), ())), preferred_element_type=jnp.float32)
        return s * scale - off_ref[j * BLOCK : (j + 1) * BLOCK, :]

    stats_ref[...] = jnp.concatenate(
        [jnp.zeros((1, BLOCK), jnp.float32), jnp.full((1, BLOCK), very_low, jnp.float32)], 0
    )
    for j in range(col_tiles):

        @pl.when(mask_ref[i * col_tiles + j] > 0)
        def _():
            tile_peak = jnp.max(scores(j), axis=0, keepdims=True)
            stats_ref[1:2, :] = jnp.maximum(stats_ref[1:2, :], tile_peak)

    for j in range(col_tiles):
        live = mask_ref[i * col_tiles + j] > 0

        @pl.when(live)
        def _():
            p = jnp.exp(scores(j) - stats_ref[1:2, :])
            p_ref[j * BLOCK : (j + 1) * BLOCK, :] = p.astype(jnp.bfloat16)
            stats_ref[0:1, :] = stats_ref[0:1, :] + jnp.sum(p, axis=0, keepdims=True)

        @pl.when(jnp.logical_not(live))
        def _():
            p_ref[j * BLOCK : (j + 1) * BLOCK, :] = jnp.zeros((BLOCK, BLOCK), jnp.bfloat16)


def date_weights_kernel(targets, sources, offsets, live):
    rows, factors = targets.shape
    cols = sources.shape[0]
    row_tiles, col_tiles = rows // BLOCK, cols // BLOCK
    kernel = lambda *refs: weights_kernel(*refs, scale=sharpness / factors**0.5, col_tiles=col_tiles)
    return pl.pallas_call(
        kernel,
        out_shape=(
            jax.ShapeDtypeStruct((cols, rows), jnp.bfloat16),
            jax.ShapeDtypeStruct((2, rows), jnp.float32),
        ),
        grid_spec=pltpu.PrefetchScalarGridSpec(
            num_scalar_prefetch=1,
            grid=(row_tiles,),
            in_specs=[
                pl.BlockSpec((BLOCK, factors), lambda i, m: (i, 0)),
                pl.BlockSpec((cols, factors), lambda i, m: (0, 0)),
                pl.BlockSpec((cols, 1), lambda i, m: (0, 0)),
            ],
            out_specs=(
                pl.BlockSpec((cols, BLOCK), lambda i, m: (0, i)),
                pl.BlockSpec((2, BLOCK), lambda i, m: (0, i)),
            ),
        ),
        compiler_params=pltpu.CompilerParams(dimension_semantics=("arbitrary",)),
    )(live.reshape(-1).astype(jnp.int32), targets, sources, offsets.astype(jnp.float32).reshape(cols, 1))


def local_live(targets, tile_mask, col_tile_ids):
    row_tiles = targets.shape[0] // BLOCK
    row_ids = lax.axis_index("tgt") * row_tiles + jnp.arange(row_tiles)
    return tile_mask[row_ids][:, col_tile_ids]


def date_partials(targets, sources, offsets, values_t, tile_mask, col_tile_ids):
    live = local_live(targets, tile_mask, col_tile_ids)
    return date_partials_kernel(targets, sources, offsets, values_t, live)


HALVING_BITS = (3,)
EXCHANGE_BITS = (0, 1, 2)


def xor_perm(size, bit):
    return [(i, i ^ (1 << bit)) for i in range(size)]


def merge(mine, theirs):
    width = mine.shape[0] - 2
    peak_a, peak_b = mine[width + 1 :], theirs[width + 1 :]
    peak = jnp.maximum(peak_a, peak_b)
    scale_a = jnp.exp(peak_a - peak)
    scale_b = jnp.exp(peak_b - peak)
    body = mine[: width + 1] * scale_a + theirs[: width + 1] * scale_b
    return jnp.concatenate([body, peak], axis=0)


def finish(packed, exercise):
    src_size = lax.axis_size("src")
    me = lax.axis_index("src")
    exercise = exercise.astype(jnp.float32)
    for bit in HALVING_BITS:
        half = packed.shape[1] // 2
        mine_hi = (me >> bit) & 1
        keep = lax.dynamic_slice_in_dim(packed, mine_hi * half, half, 1)
        send = lax.dynamic_slice_in_dim(packed, (1 - mine_hi) * half, half, 1)
        packed = merge(keep, lax.ppermute(send, "src", xor_perm(src_size, bit)))
        exercise = lax.dynamic_slice_in_dim(exercise, mine_hi * half, half, 0)
    for bit in EXCHANGE_BITS:
        packed = merge(packed, lax.ppermute(packed, "src", xor_perm(src_size, bit)))
    width = packed.shape[0] - 2
    continuation = packed[:width] / packed[width : width + 1]
    value = jnp.maximum(continuation, exercise.T).astype(jnp.bfloat16)
    for bit in reversed(HALVING_BITS):
        mine_hi = (me >> bit) & 1
        got = lax.ppermute(value, "src", xor_perm(src_size, bit))
        value = jnp.where(
            mine_hi == 1,
            jnp.concatenate([got, value], 1),
            jnp.concatenate([value, got], 1),
        )
    return value


def lin(t, s):
    return t * lax.axis_size("src") + s


Z_PLAN = ((3, 1, 1), (3, 1, 1), (3, 1, 1), (3, 1, 1), (2, 2, 1), (2, 2, 1), (0, 0, 0), (0, 0, 0))


def column_offset(s):
    y, z_lo = s % 8, s // 8
    dz = Z_PLAN[y][z_lo]
    same_dz = [(yy, zz) for yy in range(8) for zz in range(2) if Z_PLAN[yy][zz] == dz]
    return dz, same_dz.index((y, z_lo))


def holder(s):
    return s ^ (8 * Z_PLAN[s % 8][2])


def source_pair(t, s):
    x_count = lax.axis_size("tgt") // 8
    z_hi, x = t // (2 * x_count), (t // 2) % x_count
    if isinstance(s, int):
        dz, dx = column_offset(s)
    else:
        table = [column_offset(v) for v in range(lax.axis_size("src"))]
        dz = jnp.array([d for d, _ in table])[s]
        dx = jnp.array([d for _, d in table])[s]
    return ((z_hi + dz) % 4) * x_count + (x + dx) % x_count


def regroup(block_rows):
    tgt_size = lax.axis_size("tgt")
    src_size = lax.axis_size("src")
    perms = ([], [])
    for t in range(tgt_size):
        for s in range(src_size):
            pair = source_pair(t, s)
            for flip in range(2):
                u = 2 * pair + ((t % 2) ^ flip)
                perms[flip].append((lin(u, holder(s)), lin(t, s)))
    return [lax.ppermute(block_rows, ("tgt", "src"), p) for p in perms]


def regroup_order(got, axis=0):
    odd = lax.axis_index("tgt") % 2 == 1
    return jnp.concatenate(
        [jnp.where(odd, got[1], got[0]), jnp.where(odd, got[0], got[1])], axis
    )


def regroup_offsets(offsets):
    tgt_size = lax.axis_size("tgt")
    src_size = lax.axis_size("src")
    pairs = [
        (lin(t, source_pair(t, s)), lin(t, s)) for t in range(tgt_size) for s in range(src_size)
    ]
    return lax.ppermute(offsets, ("tgt", "src"), pairs)


def per_device(
    states_late,
    offset_late,
    values_late,
    states_mid,
    offset_mid,
    exercise_mid,
    mask_mid,
    states_early,
    exercise_early,
    mask_early,
):
    src_tiles = states_late.shape[0] // BLOCK
    col_ids = lax.axis_index("src") * src_tiles + jnp.arange(src_tiles)
    pair = source_pair(lax.axis_index("tgt"), lax.axis_index("src"))
    early_col_ids = pair * src_tiles + jnp.arange(src_tiles)
    mid_sources = regroup_order(regroup(states_mid))
    mid_offsets = regroup_offsets(offset_mid)
    partials = date_partials(states_mid, states_late, offset_late, values_late.T, mask_mid, col_ids)
    partials, mid_sources, mid_offsets = lax.optimization_barrier(
        (partials, mid_sources, mid_offsets)
    )
    early_weights, early_stats = date_weights_kernel(
        states_early, mid_sources, mid_offsets, local_live(states_early, mask_early, early_col_ids)
    )
    value_mid_t = finish(partials, exercise_mid)
    mid_values_t = regroup_order(regroup(value_mid_t), axis=1)
    early_weighted = jnp.dot(mid_values_t, early_weights, preferred_element_type=jnp.float32)
    value_early_t = finish(jnp.concatenate([early_weighted, early_stats], 0), exercise_early)
    value_mid, value_early = value_mid_t.T, value_early_t.T
    return (value_mid, value_early)


def solution(mesh):
    in_specs = (
        P("src", None),
        P("src"),
        P("src", None),
        P("tgt", None),
        P("src"),
        P("tgt", None),
        P(),
        P("tgt", None),
        P("tgt", None),
        P(),
    )
    out_specs = (P("tgt", None), P("tgt", None))
    return jax.shard_map(
        per_device, mesh=mesh, in_specs=in_specs, out_specs=out_specs, check_vma=False
    )
```

```python
import jax
import jax.numpy as jnp
from jax import lax
from jax.experimental import pallas as pl
from jax.experimental.pallas import tpu as pltpu
from jax.sharding import PartitionSpec as P


BLOCK = 512


sharpness = 3.5
very_low = -1e30


def partials_kernel(mask_ref, x_ref, y_ref, off_ref, v_ref, out_ref, m_ref, l_ref, acc_ref, *, scale, col_tiles):
    i = pl.program_id(0)
    j = pl.program_id(1)

    @pl.when(j == 0)
    def _():
        m_ref[...] = jnp.full(m_ref.shape, very_low, jnp.float32)
        l_ref[...] = jnp.zeros(l_ref.shape, jnp.float32)
        acc_ref[...] = jnp.zeros(acc_ref.shape, jnp.float32)

    @pl.when(mask_ref[i * col_tiles + j] > 0)
    def _():
        s = lax.dot_general(y_ref[...], x_ref[...], (((1,), (1,)), ((), ())), preferred_element_type=jnp.float32)
        s = s * scale - off_ref[...]
        m_old = m_ref[...]
        m_new = jnp.maximum(m_old, jnp.max(s, axis=0, keepdims=True))
        shrink = jnp.exp(m_old - m_new)
        p = jnp.exp(s - m_new)
        l_ref[...] = l_ref[...] * shrink + jnp.sum(p, axis=0, keepdims=True)
        acc_ref[...] = acc_ref[...] * shrink + jnp.dot(v_ref[...], p.astype(jnp.bfloat16), preferred_element_type=jnp.float32)
        m_ref[...] = m_new

    @pl.when(j == col_tiles - 1)
    def _():
        w = acc_ref.shape[0]
        out_ref[0:w, :] = acc_ref[...]
        out_ref[w:w + 1, :] = l_ref[...]
        out_ref[w + 1:w + 2, :] = m_ref[...]


def date_partials_kernel(targets, sources, offsets, values_t, live):
    rows, factors = targets.shape
    cols = sources.shape[0]
    width = values_t.shape[0]
    row_tiles, col_tiles = rows // BLOCK, cols // BLOCK
    kernel = lambda *refs: partials_kernel(*refs, scale=sharpness / factors**0.5, col_tiles=col_tiles)
    return pl.pallas_call(
        kernel,
        out_shape=jax.ShapeDtypeStruct((width + 2, rows), jnp.float32),
        grid_spec=pltpu.PrefetchScalarGridSpec(
            num_scalar_prefetch=1,
            grid=(row_tiles, col_tiles),
            in_specs=[
                pl.BlockSpec((BLOCK, factors), lambda i, j, m: (i, 0)),
                pl.BlockSpec((BLOCK, factors), lambda i, j, m: (j, 0)),
                pl.BlockSpec((BLOCK, 1), lambda i, j, m: (j, 0)),
                pl.BlockSpec((width, BLOCK), lambda i, j, m: (0, j)),
            ],
            out_specs=pl.BlockSpec((width + 2, BLOCK), lambda i, j, m: (0, i)),
            scratch_shapes=[
                pltpu.VMEM((1, BLOCK), jnp.float32),
                pltpu.VMEM((1, BLOCK), jnp.float32),
                pltpu.VMEM((width, BLOCK), jnp.float32),
            ],
        ),
        compiler_params=pltpu.CompilerParams(dimension_semantics=("arbitrary", "arbitrary")),
    )(live.reshape(-1).astype(jnp.int32), targets, sources, offsets.astype(jnp.float32).reshape(cols, 1), values_t)


def weights_kernel(mask_ref, x_ref, y_ref, off_ref, p_ref, stats_ref, *, scale, col_tiles):
    i = pl.program_id(0)

    def scores(j):
        y = y_ref[j * BLOCK : (j + 1) * BLOCK, :]
        s = lax.dot_general(y, x_ref[...], (((1,), (1,)), ((), ())), preferred_element_type=jnp.float32)
        return s * scale - off_ref[j * BLOCK : (j + 1) * BLOCK, :]

    stats_ref[...] = jnp.concatenate(
        [jnp.zeros((1, BLOCK), jnp.float32), jnp.full((1, BLOCK), very_low, jnp.float32)], 0
    )
    for j in range(col_tiles):

        @pl.when(mask_ref[i * col_tiles + j] > 0)
        def _():
            tile_peak = jnp.max(scores(j), axis=0, keepdims=True)
            stats_ref[1:2, :] = jnp.maximum(stats_ref[1:2, :], tile_peak)

    for j in range(col_tiles):
        live = mask_ref[i * col_tiles + j] > 0

        @pl.when(live)
        def _():
            p = jnp.exp(scores(j) - stats_ref[1:2, :])
            p_ref[j * BLOCK : (j + 1) * BLOCK, :] = p.astype(jnp.bfloat16)
            stats_ref[0:1, :] = stats_ref[0:1, :] + jnp.sum(p, axis=0, keepdims=True)

        @pl.when(jnp.logical_not(live))
        def _():
            p_ref[j * BLOCK : (j + 1) * BLOCK, :] = jnp.zeros((BLOCK, BLOCK), jnp.bfloat16)


def date_weights_kernel(targets, sources, offsets, live):
    rows, factors = targets.shape
    cols = sources.shape[0]
    row_tiles, col_tiles = rows // BLOCK, cols // BLOCK
    kernel = lambda *refs: weights_kernel(*refs, scale=sharpness / factors**0.5, col_tiles=col_tiles)
    return pl.pallas_call(
        kernel,
        out_shape=(
            jax.ShapeDtypeStruct((cols, rows), jnp.bfloat16),
            jax.ShapeDtypeStruct((2, rows), jnp.float32),
        ),
        grid_spec=pltpu.PrefetchScalarGridSpec(
            num_scalar_prefetch=1,
            grid=(row_tiles,),
            in_specs=[
                pl.BlockSpec((BLOCK, factors), lambda i, m: (i, 0)),
                pl.BlockSpec((cols, factors), lambda i, m: (0, 0)),
                pl.BlockSpec((cols, 1), lambda i, m: (0, 0)),
            ],
            out_specs=(
                pl.BlockSpec((cols, BLOCK), lambda i, m: (0, i)),
                pl.BlockSpec((2, BLOCK), lambda i, m: (0, i)),
            ),
        ),
        compiler_params=pltpu.CompilerParams(dimension_semantics=("arbitrary",)),
    )(live.reshape(-1).astype(jnp.int32), targets, sources, offsets.astype(jnp.float32).reshape(cols, 1))


def local_live(targets, tile_mask, col_tile_ids):
    row_tiles = targets.shape[0] // BLOCK
    row_ids = lax.axis_index("tgt") * row_tiles + jnp.arange(row_tiles)
    return tile_mask[row_ids][:, col_tile_ids]


def date_partials(targets, sources, offsets, values_t, tile_mask, col_tile_ids):
    live = local_live(targets, tile_mask, col_tile_ids)
    return date_partials_kernel(targets, sources, offsets, values_t, live)


HALVING_BITS = (3,)
EXCHANGE_BITS = (0, 1, 2)


def xor_perm(size, bit):
    return [(i, i ^ (1 << bit)) for i in range(size)]


def merge(mine, theirs):
    width = mine.shape[0] - 2
    peak_a, peak_b = mine[width + 1 :], theirs[width + 1 :]
    peak = jnp.maximum(peak_a, peak_b)
    scale_a = jnp.exp(peak_a - peak)
    scale_b = jnp.exp(peak_b - peak)
    body = mine[: width + 1] * scale_a + theirs[: width + 1] * scale_b
    return jnp.concatenate([body, peak], axis=0)


def finish(packed, exercise):
    src_size = lax.axis_size("src")
    me = lax.axis_index("src")
    exercise = exercise.astype(jnp.float32)
    for bit in HALVING_BITS:
        half = packed.shape[1] // 2
        mine_hi = (me >> bit) & 1
        keep = lax.dynamic_slice_in_dim(packed, mine_hi * half, half, 1)
        send = lax.dynamic_slice_in_dim(packed, (1 - mine_hi) * half, half, 1)
        got = lax.ppermute(send, "src", xor_perm(src_size, bit))
        packed = merge(keep, got)
        exercise = lax.dynamic_slice_in_dim(exercise, mine_hi * half, half, 0)
    for bit in EXCHANGE_BITS:
        got = lax.ppermute(packed, "src", xor_perm(src_size, bit))
        packed = merge(packed, got)
    width = packed.shape[0] - 2
    continuation = packed[:width] / packed[width : width + 1]
    value = jnp.maximum(continuation, exercise.T).astype(jnp.bfloat16)
    for bit in reversed(HALVING_BITS):
        mine_hi = (me >> bit) & 1
        got = lax.ppermute(value, "src", xor_perm(src_size, bit))
        value = jnp.where(
            mine_hi == 1,
            jnp.concatenate([got, value], 1),
            jnp.concatenate([value, got], 1),
        )
    return value


def lin(t, s):
    return t * lax.axis_size("src") + s


Z_PLAN = ((3, 1, 1), (3, 1, 1), (3, 1, 1), (3, 1, 1), (2, 2, 1), (2, 2, 1), (0, 0, 0), (0, 0, 0))


def column_offset(s):
    y, z_lo = s % 8, s // 8
    dz = Z_PLAN[y][z_lo]
    same_dz = [(yy, zz) for yy in range(8) for zz in range(2) if Z_PLAN[yy][zz] == dz]
    return dz, same_dz.index((y, z_lo))


def holder(s):
    return s ^ (8 * Z_PLAN[s % 8][2])


def source_pair(t, s):
    x_count = lax.axis_size("tgt") // 8
    z_hi, x = t // (2 * x_count), (t // 2) % x_count
    if isinstance(s, int):
        dz, dx = column_offset(s)
    else:
        y, z_lo = s % 8, s // 8
        dz = jnp.where(y < 4, 3 - 2 * z_lo, jnp.where(y < 6, 2, 0))
        dx = jnp.where(y < 4, y, (y % 2) * 2 + z_lo)
    return ((z_hi + dz) % 4) * x_count + (x + dx) % x_count


def regroup(block_rows):
    tgt_size = lax.axis_size("tgt")
    src_size = lax.axis_size("src")
    perms = ([], [])
    for t in range(tgt_size):
        for s in range(src_size):
            pair = source_pair(t, s)
            for flip in range(2):
                u = 2 * pair + ((t % 2) ^ flip)
                perms[flip].append((lin(u, holder(s)), lin(t, s)))
    return [lax.ppermute(block_rows, ("tgt", "src"), p) for p in perms]


def regroup_order(got, axis=0):
    odd = lax.axis_index("tgt") % 2 == 1
    return jnp.concatenate(
        [jnp.where(odd, got[1], got[0]), jnp.where(odd, got[0], got[1])], axis
    )


def regroup_offsets(offsets):
    tgt_size = lax.axis_size("tgt")
    src_size = lax.axis_size("src")
    pairs = [
        (lin(t, source_pair(t, s)), lin(t, s)) for t in range(tgt_size) for s in range(src_size)
    ]
    return lax.ppermute(offsets, ("tgt", "src"), pairs)


def per_device(
    states_late,
    offset_late,
    values_late,
    states_mid,
    offset_mid,
    exercise_mid,
    mask_mid,
    states_early,
    exercise_early,
    mask_early,
):
    src_tiles = states_late.shape[0] // BLOCK
    col_ids = lax.axis_index("src") * src_tiles + jnp.arange(src_tiles)
    pair = source_pair(lax.axis_index("tgt"), lax.axis_index("src"))
    early_col_ids = pair * src_tiles + jnp.arange(src_tiles)
    mid_sources = regroup_order(regroup(states_mid))
    mid_offsets = regroup_offsets(offset_mid)
    partials = date_partials(states_mid, states_late, offset_late, values_late.T, mask_mid, col_ids)
    partials, mid_sources, mid_offsets = lax.optimization_barrier(
        (partials, mid_sources, mid_offsets)
    )
    early_live = local_live(states_early, mask_early, early_col_ids)
    early_parts = []
    for row_tile in range(early_live.shape[0]):
        rows = states_early[row_tile * BLOCK : (row_tile + 1) * BLOCK]
        early_parts.append(
            date_weights_kernel(rows, mid_sources, mid_offsets, early_live[row_tile : row_tile + 1])
        )
    value_mid_t = finish(partials, exercise_mid)
    mid_values_t = regroup_order(regroup(value_mid_t), axis=1)
    early_weighted = jnp.concatenate(
        [jnp.dot(mid_values_t, w, preferred_element_type=jnp.float32) for w, _ in early_parts], 1
    )
    early_stats = jnp.concatenate([s for _, s in early_parts], 1)
    value_early_t = finish(jnp.concatenate([early_weighted, early_stats], 0), exercise_early)
    value_mid, value_early = value_mid_t.T, value_early_t.T
    return (value_mid, value_early)


def solution(mesh):
    in_specs = (
        P("src", None),
        P("src"),
        P("src", None),
        P("tgt", None),
        P("src"),
        P("tgt", None),
        P(),
        P("tgt", None),
        P("tgt", None),
        P(),
    )
    out_specs = (P("tgt", None), P("tgt", None))
    return jax.shard_map(per_device, mesh=mesh, in_specs=in_specs, out_specs=out_specs, check_vma=False)
```

```python
import jax
import jax.numpy as jnp
from jax import lax
from jax.experimental import pallas as pl
from jax.experimental.pallas import tpu as pltpu
from jax.sharding import PartitionSpec as P


BLOCK = 512


sharpness = 3.5
very_low = -1e30


def partials_kernel(mask_ref, x_ref, y_ref, off_ref, v_ref, out_ref, m_ref, l_ref, acc_ref, *, scale, col_tiles):
    i = pl.program_id(0)
    j = pl.program_id(1)

    @pl.when(j == 0)
    def _():
        m_ref[...] = jnp.full(m_ref.shape, very_low, jnp.float32)
        l_ref[...] = jnp.zeros(l_ref.shape, jnp.float32)
        acc_ref[...] = jnp.zeros(acc_ref.shape, jnp.float32)

    @pl.when(mask_ref[i * col_tiles + j] > 0)
    def _():
        s = lax.dot_general(y_ref[...], x_ref[...], (((1,), (1,)), ((), ())), preferred_element_type=jnp.float32)
        s = s * scale - jnp.transpose(off_ref[...])[:, 0:1]
        m_old = m_ref[...]
        m_new = jnp.maximum(m_old, jnp.max(s, axis=0, keepdims=True))
        shrink = jnp.exp(m_old - m_new)
        p = jnp.exp(s - m_new)
        l_ref[...] = l_ref[...] * shrink + jnp.sum(p, axis=0, keepdims=True)
        acc_ref[...] = acc_ref[...] * shrink + lax.dot_general(
            v_ref[...], p.astype(jnp.bfloat16), (((0,), (0,)), ((), ())), preferred_element_type=jnp.float32
        )
        m_ref[...] = m_new

    @pl.when(j == col_tiles - 1)
    def _():
        w = acc_ref.shape[0]
        out_ref[0:w, :] = acc_ref[...]
        out_ref[w:w + 1, :] = l_ref[...]
        out_ref[w + 1:w + 2, :] = m_ref[...]


def lane_offsets(offsets):
    return jnp.broadcast_to(offsets.astype(jnp.float32)[None, :], (8, offsets.shape[0]))


def date_partials_kernel(targets, sources, offsets, values, live):
    rows, factors = targets.shape
    cols = sources.shape[0]
    width = values.shape[1]
    row_tiles, col_tiles = rows // BLOCK, cols // BLOCK
    kernel = lambda *refs: partials_kernel(*refs, scale=sharpness / factors**0.5, col_tiles=col_tiles)
    return pl.pallas_call(
        kernel,
        out_shape=jax.ShapeDtypeStruct((width + 2, rows), jnp.float32),
        grid_spec=pltpu.PrefetchScalarGridSpec(
            num_scalar_prefetch=1,
            grid=(row_tiles, col_tiles),
            in_specs=[
                pl.BlockSpec((BLOCK, factors), lambda i, j, m: (i, 0)),
                pl.BlockSpec((BLOCK, factors), lambda i, j, m: (j, 0)),
                pl.BlockSpec((8, BLOCK), lambda i, j, m: (0, j)),
                pl.BlockSpec((BLOCK, width), lambda i, j, m: (j, 0)),
            ],
            out_specs=pl.BlockSpec((width + 2, BLOCK), lambda i, j, m: (0, i)),
            scratch_shapes=[
                pltpu.VMEM((1, BLOCK), jnp.float32),
                pltpu.VMEM((1, BLOCK), jnp.float32),
                pltpu.VMEM((width, BLOCK), jnp.float32),
            ],
        ),
        compiler_params=pltpu.CompilerParams(dimension_semantics=("arbitrary", "arbitrary")),
    )(live.reshape(-1).astype(jnp.int32), targets, sources, lane_offsets(offsets), values)


def weights_kernel(mask_ref, x_ref, y_ref, off_ref, p_ref, stats_ref, *, scale, col_tiles):
    i = pl.program_id(0)

    def scores(j):
        y = y_ref[j * BLOCK : (j + 1) * BLOCK, :]
        s = lax.dot_general(y, x_ref[...], (((1,), (1,)), ((), ())), preferred_element_type=jnp.float32)
        return s * scale - jnp.transpose(off_ref[:, j * BLOCK : (j + 1) * BLOCK])[:, 0:1]

    stats_ref[...] = jnp.concatenate(
        [jnp.zeros((1, BLOCK), jnp.float32), jnp.full((1, BLOCK), very_low, jnp.float32)], 0
    )
    for j in range(col_tiles):

        @pl.when(mask_ref[i * col_tiles + j] > 0)
        def _():
            tile_peak = jnp.max(scores(j), axis=0, keepdims=True)
            stats_ref[1:2, :] = jnp.maximum(stats_ref[1:2, :], tile_peak)

    for j in range(col_tiles):
        live = mask_ref[i * col_tiles + j] > 0

        @pl.when(live)
        def _():
            p = jnp.exp(scores(j) - stats_ref[1:2, :])
            p_ref[j * BLOCK : (j + 1) * BLOCK, :] = p.astype(jnp.bfloat16)
            stats_ref[0:1, :] = stats_ref[0:1, :] + jnp.sum(p, axis=0, keepdims=True)

        @pl.when(jnp.logical_not(live))
        def _():
            p_ref[j * BLOCK : (j + 1) * BLOCK, :] = jnp.zeros((BLOCK, BLOCK), jnp.bfloat16)


def date_weights_kernel(targets, sources, offsets, live):
    rows, factors = targets.shape
    cols = sources.shape[0]
    row_tiles, col_tiles = rows // BLOCK, cols // BLOCK
    kernel = lambda *refs: weights_kernel(*refs, scale=sharpness / factors**0.5, col_tiles=col_tiles)
    return pl.pallas_call(
        kernel,
        out_shape=(
            jax.ShapeDtypeStruct((cols, rows), jnp.bfloat16),
            jax.ShapeDtypeStruct((2, rows), jnp.float32),
        ),
        grid_spec=pltpu.PrefetchScalarGridSpec(
            num_scalar_prefetch=1,
            grid=(row_tiles,),
            in_specs=[
                pl.BlockSpec((BLOCK, factors), lambda i, m: (i, 0)),
                pl.BlockSpec((cols, factors), lambda i, m: (0, 0)),
                pl.BlockSpec((8, cols), lambda i, m: (0, 0)),
            ],
            out_specs=(
                pl.BlockSpec((cols, BLOCK), lambda i, m: (0, i)),
                pl.BlockSpec((2, BLOCK), lambda i, m: (0, i)),
            ),
        ),
        compiler_params=pltpu.CompilerParams(dimension_semantics=("arbitrary",)),
    )(live.reshape(-1).astype(jnp.int32), targets, sources, lane_offsets(offsets))


def local_live(targets, tile_mask, col_tile_ids):
    row_tiles = targets.shape[0] // BLOCK
    row_ids = lax.axis_index("tgt") * row_tiles + jnp.arange(row_tiles)
    return tile_mask[row_ids][:, col_tile_ids]


def date_partials(targets, sources, offsets, values, tile_mask, col_tile_ids):
    live = local_live(targets, tile_mask, col_tile_ids)
    return date_partials_kernel(targets, sources, offsets, values, live)


HALVING_BITS = (3,)
EXCHANGE_BITS = (0, 1, 2)


def xor_perm(size, bit):
    return [(i, i ^ (1 << bit)) for i in range(size)]


def merge(mine, theirs):
    width = mine.shape[0] - 2
    peak_a, peak_b = mine[width + 1 :], theirs[width + 1 :]
    peak = jnp.maximum(peak_a, peak_b)
    scale_a = jnp.exp(peak_a - peak)
    scale_b = jnp.exp(peak_b - peak)
    body = mine[: width + 1] * scale_a + theirs[: width + 1] * scale_b
    return jnp.concatenate([body, peak], axis=0)


def finish(packed, exercise):
    src_size = lax.axis_size("src")
    me = lax.axis_index("src")
    exercise = exercise.astype(jnp.float32)
    for bit in HALVING_BITS:
        half = packed.shape[1] // 2
        mine_hi = (me >> bit) & 1
        keep = lax.dynamic_slice_in_dim(packed, mine_hi * half, half, 1)
        send = lax.dynamic_slice_in_dim(packed, (1 - mine_hi) * half, half, 1)
        got = lax.ppermute(send, "src", xor_perm(src_size, bit))
        packed = merge(keep, got)
        exercise = lax.dynamic_slice_in_dim(exercise, mine_hi * half, half, 0)
    for bit in EXCHANGE_BITS:
        got = lax.ppermute(packed, "src", xor_perm(src_size, bit))
        packed = merge(packed, got)
    width = packed.shape[0] - 2
    continuation = packed[:width] / packed[width : width + 1]
    value = jnp.maximum(continuation, exercise.T).astype(jnp.bfloat16)
    for bit in reversed(HALVING_BITS):
        mine_hi = (me >> bit) & 1
        got = lax.ppermute(value, "src", xor_perm(src_size, bit))
        value = jnp.where(
            mine_hi == 1,
            jnp.concatenate([got, value], 1),
            jnp.concatenate([value, got], 1),
        )
    return value


def lin(t, s):
    return t * lax.axis_size("src") + s


Z_PLAN = ((3, 1, 1), (3, 1, 1), (3, 1, 1), (3, 1, 1), (2, 2, 1), (2, 2, 1), (0, 0, 0), (0, 0, 0))


def column_offset(s):
    y, z_lo = s % 8, s // 8
    dz = Z_PLAN[y][z_lo]
    same_dz = [(yy, zz) for yy in range(8) for zz in range(2) if Z_PLAN[yy][zz] == dz]
    return dz, same_dz.index((y, z_lo))


def holder(s):
    return s ^ (8 * Z_PLAN[s % 8][2])


def source_pair(t, s):
    x_count = lax.axis_size("tgt") // 8
    z_hi, x = t // (2 * x_count), (t // 2) % x_count
    if isinstance(s, int):
        dz, dx = column_offset(s)
    else:
        y, z_lo = s % 8, s // 8
        dz = jnp.where(y < 4, 3 - 2 * z_lo, jnp.where(y < 6, 2, 0))
        dx = jnp.where(y < 4, y, (y % 2) * 2 + z_lo)
    return ((z_hi + dz) % 4) * x_count + (x + dx) % x_count


def regroup(block_rows):
    tgt_size = lax.axis_size("tgt")
    src_size = lax.axis_size("src")
    perms = ([], [])
    for t in range(tgt_size):
        for s in range(src_size):
            pair = source_pair(t, s)
            for flip in range(2):
                u = 2 * pair + ((t % 2) ^ flip)
                perms[flip].append((lin(u, holder(s)), lin(t, s)))
    return [lax.ppermute(block_rows, ("tgt", "src"), p) for p in perms]


def regroup_order(got, axis=0):
    odd = lax.axis_index("tgt") % 2 == 1
    return jnp.concatenate(
        [jnp.where(odd, got[1], got[0]), jnp.where(odd, got[0], got[1])], axis
    )


def regroup_offsets(offsets):
    tgt_size = lax.axis_size("tgt")
    src_size = lax.axis_size("src")
    pairs = [
        (lin(t, source_pair(t, s)), lin(t, s)) for t in range(tgt_size) for s in range(src_size)
    ]
    return lax.ppermute(offsets, ("tgt", "src"), pairs)


def per_device(
    states_late,
    offset_late,
    values_late,
    states_mid,
    offset_mid,
    exercise_mid,
    mask_mid,
    states_early,
    exercise_early,
    mask_early,
):
    src_tiles = states_late.shape[0] // BLOCK
    col_ids = lax.axis_index("src") * src_tiles + jnp.arange(src_tiles)
    pair = source_pair(lax.axis_index("tgt"), lax.axis_index("src"))
    early_col_ids = pair * src_tiles + jnp.arange(src_tiles)
    mid_sources = regroup_order(regroup(states_mid))
    mid_offsets = regroup_offsets(offset_mid)
    partials = date_partials(states_mid, states_late, offset_late, values_late, mask_mid, col_ids)
    partials, mid_sources, mid_offsets = lax.optimization_barrier(
        (partials, mid_sources, mid_offsets)
    )
    early_live = local_live(states_early, mask_early, early_col_ids)
    early_parts = []
    for row_tile in range(early_live.shape[0]):
        rows = states_early[row_tile * BLOCK : (row_tile + 1) * BLOCK]
        early_parts.append(
            date_weights_kernel(rows, mid_sources, mid_offsets, early_live[row_tile : row_tile + 1])
        )
    value_mid_t = finish(partials, exercise_mid)
    mid_values_t = regroup_order(regroup(value_mid_t), axis=1)
    early_weighted = jnp.concatenate(
        [jnp.dot(mid_values_t, w, preferred_element_type=jnp.float32) for w, _ in early_parts], 1
    )
    early_stats = jnp.concatenate([s for _, s in early_parts], 1)
    value_early_t = finish(jnp.concatenate([early_weighted, early_stats], 0), exercise_early)
    value_mid, value_early = value_mid_t.T, value_early_t.T
    return (value_mid, value_early)


def solution(mesh):
    in_specs = (
        P("src", None),
        P("src"),
        P("src", None),
        P("tgt", None),
        P("src"),
        P("tgt", None),
        P(),
        P("tgt", None),
        P("tgt", None),
        P(),
    )
    out_specs = (P("tgt", None), P("tgt", None))
    return jax.shard_map(per_device, mesh=mesh, in_specs=in_specs, out_specs=out_specs, check_vma=False)
```

```python
import jax
import jax.numpy as jnp
from jax import lax
from jax.experimental import pallas as pl
from jax.experimental.pallas import tpu as pltpu
from jax.sharding import PartitionSpec as P


BLOCK = 512


sharpness = 3.5
very_low = -1e30


def partials_kernel(mask_ref, x_ref, y_ref, off_ref, v_ref, out_ref, m_ref, l_ref, acc_ref, *, scale, col_tiles):
    i = pl.program_id(0)
    j = pl.program_id(1)

    @pl.when(j == 0)
    def _():
        m_ref[...] = jnp.full(m_ref.shape, very_low, jnp.float32)
        l_ref[...] = jnp.zeros(l_ref.shape, jnp.float32)
        acc_ref[...] = jnp.zeros(acc_ref.shape, jnp.float32)

    @pl.when(mask_ref[i * col_tiles + j] > 0)
    def _():
        s = lax.dot_general(y_ref[...], x_ref[...], (((1,), (1,)), ((), ())), preferred_element_type=jnp.float32)
        s = s * scale - jnp.transpose(off_ref[...])[:, 0:1]
        m_old = m_ref[...]
        m_new = jnp.maximum(m_old, jnp.max(s, axis=0, keepdims=True))
        shrink = jnp.exp(m_old - m_new)
        p = jnp.exp(s - m_new)
        l_ref[...] = l_ref[...] * shrink + jnp.sum(p, axis=0, keepdims=True)
        acc_ref[...] = acc_ref[...] * shrink + lax.dot_general(
            v_ref[...], p.astype(jnp.bfloat16), (((0,), (0,)), ((), ())), preferred_element_type=jnp.float32
        )
        m_ref[...] = m_new

    @pl.when(j == col_tiles - 1)
    def _():
        w = acc_ref.shape[0]
        out_ref[0:w, :] = acc_ref[...]
        out_ref[w:w + 1, :] = l_ref[...]
        out_ref[w + 1:w + 2, :] = m_ref[...]


def lane_offsets(offsets):
    return jnp.broadcast_to(offsets.astype(jnp.float32)[None, :], (8, offsets.shape[0]))


def date_partials_kernel(targets, sources, offsets, values, live):
    rows, factors = targets.shape
    cols = sources.shape[0]
    width = values.shape[1]
    row_tiles, col_tiles = rows // BLOCK, cols // BLOCK
    kernel = lambda *refs: partials_kernel(*refs, scale=sharpness / factors**0.5, col_tiles=col_tiles)
    return pl.pallas_call(
        kernel,
        out_shape=jax.ShapeDtypeStruct((width + 2, rows), jnp.float32),
        grid_spec=pltpu.PrefetchScalarGridSpec(
            num_scalar_prefetch=1,
            grid=(row_tiles, col_tiles),
            in_specs=[
                pl.BlockSpec((BLOCK, factors), lambda i, j, m: (i, 0)),
                pl.BlockSpec((BLOCK, factors), lambda i, j, m: (j, 0)),
                pl.BlockSpec((8, BLOCK), lambda i, j, m: (0, j)),
                pl.BlockSpec((BLOCK, width), lambda i, j, m: (j, 0)),
            ],
            out_specs=pl.BlockSpec((width + 2, BLOCK), lambda i, j, m: (0, i)),
            scratch_shapes=[
                pltpu.VMEM((1, BLOCK), jnp.float32),
                pltpu.VMEM((1, BLOCK), jnp.float32),
                pltpu.VMEM((width, BLOCK), jnp.float32),
            ],
        ),
        compiler_params=pltpu.CompilerParams(dimension_semantics=("arbitrary", "arbitrary")),
    )(live.reshape(-1).astype(jnp.int32), targets, sources, lane_offsets(offsets), values)


def weights_kernel(mask_ref, x_ref, y_ref, off_ref, p_ref, stats_ref, *, scale, col_tiles):
    i = pl.program_id(0)

    def scores(j):
        y = y_ref[j * BLOCK : (j + 1) * BLOCK, :]
        s = lax.dot_general(y, x_ref[...], (((1,), (1,)), ((), ())), preferred_element_type=jnp.float32)
        return s * scale - jnp.transpose(off_ref[:, j * BLOCK : (j + 1) * BLOCK])[:, 0:1]

    stats_ref[...] = jnp.concatenate(
        [jnp.zeros((1, BLOCK), jnp.float32), jnp.full((1, BLOCK), very_low, jnp.float32)], 0
    )
    for j in range(col_tiles):

        @pl.when(mask_ref[i * col_tiles + j] > 0)
        def _():
            tile_peak = jnp.max(scores(j), axis=0, keepdims=True)
            stats_ref[1:2, :] = jnp.maximum(stats_ref[1:2, :], tile_peak)

    for j in range(col_tiles):
        live = mask_ref[i * col_tiles + j] > 0

        @pl.when(live)
        def _():
            p = jnp.exp(scores(j) - stats_ref[1:2, :])
            p_ref[j * BLOCK : (j + 1) * BLOCK, :] = p.astype(jnp.bfloat16)
            stats_ref[0:1, :] = stats_ref[0:1, :] + jnp.sum(p, axis=0, keepdims=True)

        @pl.when(jnp.logical_not(live))
        def _():
            p_ref[j * BLOCK : (j + 1) * BLOCK, :] = jnp.zeros((BLOCK, BLOCK), jnp.bfloat16)


def date_weights_kernel(targets, sources, offsets, live):
    rows, factors = targets.shape
    cols = sources.shape[0]
    row_tiles, col_tiles = rows // BLOCK, cols // BLOCK
    kernel = lambda *refs: weights_kernel(*refs, scale=sharpness / factors**0.5, col_tiles=col_tiles)
    return pl.pallas_call(
        kernel,
        out_shape=(
            jax.ShapeDtypeStruct((cols, rows), jnp.bfloat16),
            jax.ShapeDtypeStruct((2, rows), jnp.float32),
        ),
        grid_spec=pltpu.PrefetchScalarGridSpec(
            num_scalar_prefetch=1,
            grid=(row_tiles,),
            in_specs=[
                pl.BlockSpec((BLOCK, factors), lambda i, m: (i, 0)),
                pl.BlockSpec((cols, factors), lambda i, m: (0, 0)),
                pl.BlockSpec((8, cols), lambda i, m: (0, 0)),
            ],
            out_specs=(
                pl.BlockSpec((cols, BLOCK), lambda i, m: (0, i)),
                pl.BlockSpec((2, BLOCK), lambda i, m: (0, i)),
            ),
        ),
        compiler_params=pltpu.CompilerParams(dimension_semantics=("arbitrary",)),
    )(live.reshape(-1).astype(jnp.int32), targets, sources, lane_offsets(offsets))


def local_live(targets, tile_mask, col_tile_ids):
    row_tiles = targets.shape[0] // BLOCK
    row_ids = lax.axis_index("tgt") * row_tiles + jnp.arange(row_tiles)
    return tile_mask[row_ids][:, col_tile_ids]


def date_partials(targets, sources, offsets, values, tile_mask, col_tile_ids):
    live = local_live(targets, tile_mask, col_tile_ids)
    return date_partials_kernel(targets, sources, offsets, values, live)


HALVING_BITS = (3,)
FAR_PARTNER = (6, 7, 4, 5, 2, 3, 0, 1)
EXCHANGES = (lambda y: y ^ 1, lambda y: y ^ 2, lambda y: FAR_PARTNER[y])


def xor_perm(size, bit):
    return [(i, i ^ (1 << bit)) for i in range(size)]


def exchange_perm(size, partner):
    return [(i, (i // 8) * 8 + partner(i % 8)) for i in range(size)]


def merge(mine, theirs):
    width = mine.shape[0] - 2
    peak_a, peak_b = mine[width + 1 :], theirs[width + 1 :]
    peak = jnp.maximum(peak_a, peak_b)
    scale_a = jnp.exp(peak_a - peak)
    scale_b = jnp.exp(peak_b - peak)
    body = mine[: width + 1] * scale_a + theirs[: width + 1] * scale_b
    return jnp.concatenate([body, peak], axis=0)


def finish(packed, exercise):
    src_size = lax.axis_size("src")
    me = lax.axis_index("src")
    exercise = exercise.astype(jnp.float32)
    for bit in HALVING_BITS:
        half = packed.shape[1] // 2
        mine_hi = (me >> bit) & 1
        keep = lax.dynamic_slice_in_dim(packed, mine_hi * half, half, 1)
        send = lax.dynamic_slice_in_dim(packed, (1 - mine_hi) * half, half, 1)
        got = lax.ppermute(send, "src", xor_perm(src_size, bit))
        packed = merge(keep, got)
        exercise = lax.dynamic_slice_in_dim(exercise, mine_hi * half, half, 0)
    for partner in EXCHANGES:
        got = lax.ppermute(packed, "src", exchange_perm(src_size, partner))
        packed = merge(packed, got)
    width = packed.shape[0] - 2
    continuation = packed[:width] / packed[width : width + 1]
    value = jnp.maximum(continuation, exercise.T).astype(jnp.bfloat16)
    for bit in reversed(HALVING_BITS):
        mine_hi = (me >> bit) & 1
        got = lax.ppermute(value, "src", xor_perm(src_size, bit))
        value = jnp.where(
            mine_hi == 1,
            jnp.concatenate([got, value], 1),
            jnp.concatenate([value, got], 1),
        )
    return value


def lin(t, s):
    return t * lax.axis_size("src") + s


Z_PLAN = ((3, 1, 1), (3, 1, 1), (3, 1, 1), (3, 1, 1), (2, 2, 1), (2, 2, 1), (0, 0, 0), (0, 0, 0))


def column_offset(s):
    y, z_lo = s % 8, s // 8
    dz = Z_PLAN[y][z_lo]
    same_dz = [(yy, zz) for yy in range(8) for zz in range(2) if Z_PLAN[yy][zz] == dz]
    return dz, same_dz.index((y, z_lo))


def holder(s):
    return s ^ (8 * Z_PLAN[s % 8][2])


def source_pair(t, s):
    x_count = lax.axis_size("tgt") // 8
    z_hi, x = t // (2 * x_count), (t // 2) % x_count
    if isinstance(s, int):
        dz, dx = column_offset(s)
    else:
        y, z_lo = s % 8, s // 8
        dz = jnp.where(y < 4, 3 - 2 * z_lo, jnp.where(y < 6, 2, 0))
        dx = jnp.where(y < 4, y, (y % 2) * 2 + z_lo)
    return ((z_hi + dz) % 4) * x_count + (x + dx) % x_count


def regroup(block_rows):
    tgt_size = lax.axis_size("tgt")
    src_size = lax.axis_size("src")
    perms = ([], [])
    for t in range(tgt_size):
        for s in range(src_size):
            pair = source_pair(t, s)
            for flip in range(2):
                u = 2 * pair + ((t % 2) ^ flip)
                perms[flip].append((lin(u, holder(s)), lin(t, s)))
    return [lax.ppermute(block_rows, ("tgt", "src"), p) for p in perms]


def regroup_order(got, axis=0):
    odd = lax.axis_index("tgt") % 2 == 1
    return jnp.concatenate(
        [jnp.where(odd, got[1], got[0]), jnp.where(odd, got[0], got[1])], axis
    )


def regroup_offsets(offsets):
    tgt_size = lax.axis_size("tgt")
    src_size = lax.axis_size("src")
    pairs = [
        (lin(t, source_pair(t, s)), lin(t, s)) for t in range(tgt_size) for s in range(src_size)
    ]
    return lax.ppermute(offsets, ("tgt", "src"), pairs)


def per_device(
    states_late,
    offset_late,
    values_late,
    states_mid,
    offset_mid,
    exercise_mid,
    mask_mid,
    states_early,
    exercise_early,
    mask_early,
):
    src_tiles = states_late.shape[0] // BLOCK
    col_ids = lax.axis_index("src") * src_tiles + jnp.arange(src_tiles)
    pair = source_pair(lax.axis_index("tgt"), lax.axis_index("src"))
    early_col_ids = pair * src_tiles + jnp.arange(src_tiles)
    mid_sources = regroup_order(regroup(states_mid))
    mid_offsets = regroup_offsets(offset_mid)
    partials = date_partials(states_mid, states_late, offset_late, values_late, mask_mid, col_ids)
    partials, mid_sources, mid_offsets = lax.optimization_barrier(
        (partials, mid_sources, mid_offsets)
    )
    early_live = local_live(states_early, mask_early, early_col_ids)
    early_parts = []
    for row_tile in range(early_live.shape[0]):
        rows = states_early[row_tile * BLOCK : (row_tile + 1) * BLOCK]
        early_parts.append(
            date_weights_kernel(rows, mid_sources, mid_offsets, early_live[row_tile : row_tile + 1])
        )
    value_mid_t = finish(partials, exercise_mid)
    mid_values_t = regroup_order(regroup(value_mid_t), axis=1)
    early_weighted = jnp.concatenate(
        [jnp.dot(mid_values_t, w, preferred_element_type=jnp.float32) for w, _ in early_parts], 1
    )
    early_stats = jnp.concatenate([s for _, s in early_parts], 1)
    value_early_t = finish(jnp.concatenate([early_weighted, early_stats], 0), exercise_early)
    value_mid, value_early = value_mid_t.T, value_early_t.T
    return (value_mid, value_early)


def solution(mesh):
    in_specs = (
        P("src", None),
        P("src"),
        P("src", None),
        P("tgt", None),
        P("src"),
        P("tgt", None),
        P(),
        P("tgt", None),
        P("tgt", None),
        P(),
    )
    out_specs = (P("tgt", None), P("tgt", None))
    return jax.shard_map(per_device, mesh=mesh, in_specs=in_specs, out_specs=out_specs, check_vma=False)
```

```python
import jax
import jax.numpy as jnp
from jax import lax
from jax.experimental import pallas as pl
from jax.experimental.pallas import tpu as pltpu
from jax.sharding import PartitionSpec as P


BLOCK = 512


sharpness = 3.5
very_low = -1e30


def row_tile_base(row_tiles):
    return lax.axis_index("tgt") * row_tiles


def offset_column(off_row):
    wide = jnp.broadcast_to(off_row.astype(jnp.float32), (8, off_row.shape[1]))
    return jnp.transpose(wide)[:, 0:1]


def partials_kernel(mask_ref, x_ref, y_ref, off_ref, v_ref, out_ref, m_ref, l_ref, acc_ref, *, scale, row_tiles, col_tiles, col_base):
    i = pl.program_id(0)
    j = pl.program_id(1)

    @pl.when(j == 0)
    def _():
        m_ref[...] = jnp.full(m_ref.shape, very_low, jnp.float32)
        l_ref[...] = jnp.zeros(l_ref.shape, jnp.float32)
        acc_ref[...] = jnp.zeros(acc_ref.shape, jnp.float32)

    @pl.when(mask_ref[row_tile_base(row_tiles) + i, col_base() + j] > 0)
    def _():
        s = lax.dot_general(y_ref[...], x_ref[...], (((1,), (1,)), ((), ())), preferred_element_type=jnp.float32)
        s = s * scale - offset_column(off_ref[...])
        m_old = m_ref[...]
        m_new = jnp.maximum(m_old, jnp.max(s, axis=0, keepdims=True))
        shrink = jnp.exp(m_old - m_new)
        p = jnp.exp(s - m_new)
        l_ref[...] = l_ref[...] * shrink + jnp.sum(p, axis=0, keepdims=True)
        acc_ref[...] = acc_ref[...] * shrink + jnp.dot(v_ref[...], p.astype(jnp.bfloat16), preferred_element_type=jnp.float32)
        m_ref[...] = m_new

    @pl.when(j == col_tiles - 1)
    def _():
        w = acc_ref.shape[0]
        out_ref[0:w, :] = acc_ref[...]
        out_ref[w:w + 1, :] = l_ref[...]
        out_ref[w + 1:w + 2, :] = m_ref[...]


def date_partials_kernel(targets, sources, offsets, values_t, tile_mask, col_base):
    rows, factors = targets.shape
    cols = sources.shape[0]
    width = values_t.shape[0]
    row_tiles, col_tiles = rows // BLOCK, cols // BLOCK
    kernel = lambda *refs: partials_kernel(
        *refs, scale=sharpness / factors**0.5, row_tiles=row_tiles, col_tiles=col_tiles, col_base=col_base
    )
    return pl.pallas_call(
        kernel,
        out_shape=jax.ShapeDtypeStruct((width + 2, rows), jnp.float32),
        grid_spec=pltpu.PrefetchScalarGridSpec(
            num_scalar_prefetch=1,
            grid=(row_tiles, col_tiles),
            in_specs=[
                pl.BlockSpec((BLOCK, factors), lambda i, j, m: (i, 0)),
                pl.BlockSpec((BLOCK, factors), lambda i, j, m: (j, 0)),
                pl.BlockSpec((1, BLOCK), lambda i, j, m: (0, j)),
                pl.BlockSpec((width, BLOCK), lambda i, j, m: (0, j)),
            ],
            out_specs=pl.BlockSpec((width + 2, BLOCK), lambda i, j, m: (0, i)),
            scratch_shapes=[
                pltpu.VMEM((1, BLOCK), jnp.float32),
                pltpu.VMEM((1, BLOCK), jnp.float32),
                pltpu.VMEM((width, BLOCK), jnp.float32),
            ],
        ),
        compiler_params=pltpu.CompilerParams(dimension_semantics=("arbitrary", "arbitrary")),
    )(tile_mask, targets, sources, offsets.reshape(1, cols), values_t)


def weights_kernel(mask_ref, x_ref, y_ref, off_ref, p_ref, stats_ref, *, scale, row_tile, col_tiles, col_base):
    row = row_tile_base(2) + row_tile
    col0 = col_base()

    def scores(j):
        y = y_ref[j * BLOCK : (j + 1) * BLOCK, :]
        s = lax.dot_general(y, x_ref[...], (((1,), (1,)), ((), ())), preferred_element_type=jnp.float32)
        return s * scale - offset_column(off_ref[:, j * BLOCK : (j + 1) * BLOCK])

    stats_ref[...] = jnp.concatenate(
        [jnp.zeros((1, BLOCK), jnp.float32), jnp.full((1, BLOCK), very_low, jnp.float32)], 0
    )
    for j in range(col_tiles):

        @pl.when(mask_ref[row, col0 + j] > 0)
        def _():
            tile_peak = jnp.max(scores(j), axis=0, keepdims=True)
            stats_ref[1:2, :] = jnp.maximum(stats_ref[1:2, :], tile_peak)

    for j in range(col_tiles):
        live = mask_ref[row, col0 + j] > 0

        @pl.when(live)
        def _():
            p = jnp.exp(scores(j) - stats_ref[1:2, :])
            p_ref[j * BLOCK : (j + 1) * BLOCK, :] = p.astype(jnp.bfloat16)
            stats_ref[0:1, :] = stats_ref[0:1, :] + jnp.sum(p, axis=0, keepdims=True)

        @pl.when(jnp.logical_not(live))
        def _():
            p_ref[j * BLOCK : (j + 1) * BLOCK, :] = jnp.zeros((BLOCK, BLOCK), jnp.bfloat16)


def date_weights_kernel(targets, sources, offsets, tile_mask, row_tile, col_base):
    rows, factors = targets.shape
    cols = sources.shape[0]
    col_tiles = cols // BLOCK
    kernel = lambda *refs: weights_kernel(
        *refs, scale=sharpness / factors**0.5, row_tile=row_tile, col_tiles=col_tiles, col_base=col_base
    )
    return pl.pallas_call(
        kernel,
        out_shape=(
            jax.ShapeDtypeStruct((cols, rows), jnp.bfloat16),
            jax.ShapeDtypeStruct((2, rows), jnp.float32),
        ),
        grid_spec=pltpu.PrefetchScalarGridSpec(
            num_scalar_prefetch=1,
            grid=(1,),
            in_specs=[
                pl.BlockSpec((BLOCK, factors), lambda i, m: (0, 0)),
                pl.BlockSpec((cols, factors), lambda i, m: (0, 0)),
                pl.BlockSpec((1, cols), lambda i, m: (0, 0)),
            ],
            out_specs=(
                pl.BlockSpec((cols, BLOCK), lambda i, m: (0, 0)),
                pl.BlockSpec((2, BLOCK), lambda i, m: (0, 0)),
            ),
        ),
        compiler_params=pltpu.CompilerParams(dimension_semantics=("arbitrary",)),
    )(tile_mask, targets, sources, offsets.reshape(1, cols))


HALVING_BITS = (3,)
FAR_PARTNER = (6, 7, 4, 5, 2, 3, 0, 1)
EXCHANGES = (lambda y: y ^ 1, lambda y: y ^ 2, lambda y: FAR_PARTNER[y])


def xor_perm(size, bit):
    return [(i, i ^ (1 << bit)) for i in range(size)]


def exchange_perm(size, partner):
    return [(i, (i // 8) * 8 + partner(i % 8)) for i in range(size)]


def merge(mine, theirs):
    width = mine.shape[0] - 2
    peak_a, peak_b = mine[width + 1 :], theirs[width + 1 :]
    peak = jnp.maximum(peak_a, peak_b)
    scale_a = jnp.exp(peak_a - peak)
    scale_b = jnp.exp(peak_b - peak)
    body = mine[: width + 1] * scale_a + theirs[: width + 1] * scale_b
    return jnp.concatenate([body, peak], axis=0)


def finish(packed, exercise):
    src_size = lax.axis_size("src")
    me = lax.axis_index("src")
    exercise = exercise.astype(jnp.float32)
    for bit in HALVING_BITS:
        half = packed.shape[1] // 2
        mine_hi = (me >> bit) & 1
        keep = lax.dynamic_slice_in_dim(packed, mine_hi * half, half, 1)
        send = lax.dynamic_slice_in_dim(packed, (1 - mine_hi) * half, half, 1)
        got = lax.ppermute(send, "src", xor_perm(src_size, bit))
        packed = merge(keep, got)
        exercise = lax.dynamic_slice_in_dim(exercise, mine_hi * half, half, 0)
    for partner in EXCHANGES:
        got = lax.ppermute(packed, "src", exchange_perm(src_size, partner))
        packed = merge(packed, got)
    width = packed.shape[0] - 2
    continuation = packed[:width] / packed[width : width + 1]
    value = jnp.maximum(continuation, exercise.T).astype(jnp.bfloat16)
    for bit in reversed(HALVING_BITS):
        mine_hi = (me >> bit) & 1
        got = lax.ppermute(value, "src", xor_perm(src_size, bit))
        value = jnp.where(
            mine_hi == 1,
            jnp.concatenate([got, value], 1),
            jnp.concatenate([value, got], 1),
        )
    return value


def lin(t, s):
    return t * lax.axis_size("src") + s


Z_PLAN = ((3, 1, 1), (3, 1, 1), (3, 1, 1), (3, 1, 1), (2, 2, 1), (2, 2, 1), (0, 0, 0), (0, 0, 0))


def column_offset(s):
    y, z_lo = s % 8, s // 8
    dz = Z_PLAN[y][z_lo]
    same_dz = [(yy, zz) for yy in range(8) for zz in range(2) if Z_PLAN[yy][zz] == dz]
    return dz, same_dz.index((y, z_lo))


def holder(s):
    return s ^ (8 * Z_PLAN[s % 8][2])


def source_pair(t, s):
    x_count = lax.axis_size("tgt") // 8
    z_hi, x = t // (2 * x_count), (t // 2) % x_count
    if isinstance(s, int):
        dz, dx = column_offset(s)
    else:
        y, z_lo = s % 8, s // 8
        dz = jnp.where(y < 4, 3 - 2 * z_lo, jnp.where(y < 6, 2, 0))
        dx = jnp.where(y < 4, y, (y % 2) * 2 + z_lo)
    return ((z_hi + dz) % 4) * x_count + (x + dx) % x_count


def regroup(block_rows):
    tgt_size = lax.axis_size("tgt")
    src_size = lax.axis_size("src")
    perms = ([], [])
    for t in range(tgt_size):
        for s in range(src_size):
            pair = source_pair(t, s)
            for flip in range(2):
                u = 2 * pair + ((t % 2) ^ flip)
                perms[flip].append((lin(u, holder(s)), lin(t, s)))
    return [lax.ppermute(block_rows, ("tgt", "src"), p) for p in perms]


def regroup_order(got, axis=0):
    odd = lax.axis_index("tgt") % 2 == 1
    return jnp.concatenate(
        [jnp.where(odd, got[1], got[0]), jnp.where(odd, got[0], got[1])], axis
    )


def regroup_offsets(offsets):
    tgt_size = lax.axis_size("tgt")
    src_size = lax.axis_size("src")
    pairs = [
        (lin(t, source_pair(t, s)), lin(t, s)) for t in range(tgt_size) for s in range(src_size)
    ]
    return lax.ppermute(offsets, ("tgt", "src"), pairs)


def per_device(
    states_late,
    offset_late,
    values_late,
    states_mid,
    offset_mid,
    exercise_mid,
    mask_mid,
    states_early,
    exercise_early,
    mask_early,
):
    src_tiles = states_late.shape[0] // BLOCK

    def mid_col_base():
        return lax.axis_index("src") * src_tiles

    def early_col_base():
        return source_pair(lax.axis_index("tgt"), lax.axis_index("src")) * src_tiles

    mid_sources = regroup_order(regroup(states_mid))
    mid_offsets = regroup_offsets(offset_mid)
    partials = date_partials_kernel(
        states_mid, states_late, offset_late, values_late.T, mask_mid, mid_col_base
    )
    partials, mid_sources, mid_offsets = lax.optimization_barrier(
        (partials, mid_sources, mid_offsets)
    )
    early_parts = []
    for row_tile in range(states_early.shape[0] // BLOCK):
        rows = states_early[row_tile * BLOCK : (row_tile + 1) * BLOCK]
        early_parts.append(
            date_weights_kernel(
                rows, mid_sources, mid_offsets, mask_early, row_tile, early_col_base
            )
        )
    value_mid_t = finish(partials, exercise_mid)
    mid_values_t = regroup_order(regroup(value_mid_t), axis=1)
    early_weighted = jnp.concatenate(
        [jnp.dot(mid_values_t, w, preferred_element_type=jnp.float32) for w, _ in early_parts], 1
    )
    early_stats = jnp.concatenate([s for _, s in early_parts], 1)
    value_early_t = finish(jnp.concatenate([early_weighted, early_stats], 0), exercise_early)
    value_mid, value_early = value_mid_t.T, value_early_t.T
    return (value_mid, value_early)


def solution(mesh):
    in_specs = (
        P("src", None),
        P("src"),
        P("src", None),
        P("tgt", None),
        P("src"),
        P("tgt", None),
        P(),
        P("tgt", None),
        P("tgt", None),
        P(),
    )
    out_specs = (P("tgt", None), P("tgt", None))
    return jax.shard_map(per_device, mesh=mesh, in_specs=in_specs, out_specs=out_specs, check_vma=False)
```

```python
import jax
import jax.numpy as jnp
from jax import lax
from jax.experimental import pallas as pl
from jax.experimental.pallas import tpu as pltpu
from jax.sharding import PartitionSpec as P


BLOCK = 512


sharpness = 3.5
very_low = -1e30


def row_tile_base(row_tiles):
    return lax.axis_index("tgt") * row_tiles


def offset_column(off_row):
    wide = jnp.broadcast_to(off_row.astype(jnp.float32), (8, off_row.shape[1]))
    return jnp.transpose(wide)[:, 0:1]


def partials_kernel(mask_ref, x_ref, y_ref, off_ref, v_ref, out_ref, *, scale, row_tiles, col_tiles, col_base):
    i = pl.program_id(0)
    row = row_tile_base(row_tiles) + i
    col0 = col_base()
    width = v_ref.shape[0]
    out_ref[0 : width + 1, :] = jnp.zeros((width + 1, BLOCK), jnp.float32)
    out_ref[width + 1 : width + 2, :] = jnp.full((1, BLOCK), very_low, jnp.float32)
    for j in range(col_tiles):

        @pl.when(mask_ref[row, col0 + j] > 0)
        def _():
            y = y_ref[j * BLOCK : (j + 1) * BLOCK, :]
            s = lax.dot_general(y, x_ref[...], (((1,), (1,)), ((), ())), preferred_element_type=jnp.float32)
            s = s * scale - offset_column(off_ref[:, j * BLOCK : (j + 1) * BLOCK])
            m_old = out_ref[width + 1 : width + 2, :]
            m_new = jnp.maximum(m_old, jnp.max(s, axis=0, keepdims=True))
            shrink = jnp.exp(m_old - m_new)
            p = jnp.exp(s - m_new)
            out_ref[width : width + 1, :] = out_ref[width : width + 1, :] * shrink + jnp.sum(p, axis=0, keepdims=True)
            out_ref[0:width, :] = out_ref[0:width, :] * shrink + jnp.dot(
                v_ref[:, j * BLOCK : (j + 1) * BLOCK], p.astype(jnp.bfloat16), preferred_element_type=jnp.float32
            )
            out_ref[width + 1 : width + 2, :] = m_new


def date_partials_kernel(targets, sources, offsets, values_t, tile_mask, col_base):
    rows, factors = targets.shape
    cols = sources.shape[0]
    width = values_t.shape[0]
    row_tiles, col_tiles = rows // BLOCK, cols // BLOCK
    kernel = lambda *refs: partials_kernel(
        *refs, scale=sharpness / factors**0.5, row_tiles=row_tiles, col_tiles=col_tiles, col_base=col_base
    )
    return pl.pallas_call(
        kernel,
        out_shape=jax.ShapeDtypeStruct((width + 2, rows), jnp.float32),
        grid_spec=pltpu.PrefetchScalarGridSpec(
            num_scalar_prefetch=1,
            grid=(row_tiles,),
            in_specs=[
                pl.BlockSpec((BLOCK, factors), lambda i, m: (i, 0)),
                pl.BlockSpec((cols, factors), lambda i, m: (0, 0)),
                pl.BlockSpec((1, cols), lambda i, m: (0, 0)),
                pl.BlockSpec((width, cols), lambda i, m: (0, 0)),
            ],
            out_specs=pl.BlockSpec((width + 2, BLOCK), lambda i, m: (0, i)),
        ),
        compiler_params=pltpu.CompilerParams(dimension_semantics=("arbitrary",)),
    )(tile_mask, targets, sources, offsets.reshape(1, cols), values_t)


def weights_kernel(mask_ref, x_ref, y_ref, off_ref, p_ref, stats_ref, *, scale, row_tile, col_tiles, col_base):
    row = row_tile_base(2) + row_tile
    col0 = col_base()

    def scores(j):
        y = y_ref[j * BLOCK : (j + 1) * BLOCK, :]
        s = lax.dot_general(y, x_ref[...], (((1,), (1,)), ((), ())), preferred_element_type=jnp.float32)
        return s * scale - offset_column(off_ref[:, j * BLOCK : (j + 1) * BLOCK])

    stats_ref[...] = jnp.concatenate(
        [jnp.zeros((1, BLOCK), jnp.float32), jnp.full((1, BLOCK), very_low, jnp.float32)], 0
    )
    for j in range(col_tiles):

        @pl.when(mask_ref[row, col0 + j] > 0)
        def _():
            tile_peak = jnp.max(scores(j), axis=0, keepdims=True)
            stats_ref[1:2, :] = jnp.maximum(stats_ref[1:2, :], tile_peak)

    for j in range(col_tiles):
        live = mask_ref[row, col0 + j] > 0

        @pl.when(live)
        def _():
            p = jnp.exp(scores(j) - stats_ref[1:2, :])
            p_ref[j * BLOCK : (j + 1) * BLOCK, :] = p.astype(jnp.bfloat16)
            stats_ref[0:1, :] = stats_ref[0:1, :] + jnp.sum(p, axis=0, keepdims=True)

        @pl.when(jnp.logical_not(live))
        def _():
            p_ref[j * BLOCK : (j + 1) * BLOCK, :] = jnp.zeros((BLOCK, BLOCK), jnp.bfloat16)


def date_weights_kernel(targets, sources, offsets, tile_mask, row_tile, col_base):
    rows, factors = targets.shape
    cols = sources.shape[0]
    col_tiles = cols // BLOCK
    kernel = lambda *refs: weights_kernel(
        *refs, scale=sharpness / factors**0.5, row_tile=row_tile, col_tiles=col_tiles, col_base=col_base
    )
    return pl.pallas_call(
        kernel,
        out_shape=(
            jax.ShapeDtypeStruct((cols, rows), jnp.bfloat16),
            jax.ShapeDtypeStruct((2, rows), jnp.float32),
        ),
        grid_spec=pltpu.PrefetchScalarGridSpec(
            num_scalar_prefetch=1,
            grid=(1,),
            in_specs=[
                pl.BlockSpec((BLOCK, factors), lambda i, m: (0, 0)),
                pl.BlockSpec((cols, factors), lambda i, m: (0, 0)),
                pl.BlockSpec((1, cols), lambda i, m: (0, 0)),
            ],
            out_specs=(
                pl.BlockSpec((cols, BLOCK), lambda i, m: (0, 0)),
                pl.BlockSpec((2, BLOCK), lambda i, m: (0, 0)),
            ),
        ),
        compiler_params=pltpu.CompilerParams(dimension_semantics=("arbitrary",)),
    )(tile_mask, targets, sources, offsets.reshape(1, cols))


HALVING_BITS = (3,)
FAR_PARTNER = (6, 7, 4, 5, 2, 3, 0, 1)
EXCHANGES = (lambda y: y ^ 1, lambda y: y ^ 2, lambda y: FAR_PARTNER[y])


def xor_perm(size, bit):
    return [(i, i ^ (1 << bit)) for i in range(size)]


def exchange_perm(size, partner):
    return [(i, (i // 8) * 8 + partner(i % 8)) for i in range(size)]


def merge(mine, theirs):
    width = mine.shape[0] - 2
    peak_a, peak_b = mine[width + 1 :], theirs[width + 1 :]
    peak = jnp.maximum(peak_a, peak_b)
    scale_a = jnp.exp(peak_a - peak)
    scale_b = jnp.exp(peak_b - peak)
    body = mine[: width + 1] * scale_a + theirs[: width + 1] * scale_b
    return jnp.concatenate([body, peak], axis=0)


def finish(packed, exercise):
    src_size = lax.axis_size("src")
    me = lax.axis_index("src")
    exercise = exercise.astype(jnp.float32)
    for bit in HALVING_BITS:
        half = packed.shape[1] // 2
        mine_hi = (me >> bit) & 1
        keep = lax.dynamic_slice_in_dim(packed, mine_hi * half, half, 1)
        send = lax.dynamic_slice_in_dim(packed, (1 - mine_hi) * half, half, 1)
        got = lax.ppermute(send, "src", xor_perm(src_size, bit))
        packed = merge(keep, got)
        exercise = lax.dynamic_slice_in_dim(exercise, mine_hi * half, half, 0)
    for partner in EXCHANGES:
        got = lax.ppermute(packed, "src", exchange_perm(src_size, partner))
        packed = merge(packed, got)
    width = packed.shape[0] - 2
    continuation = packed[:width] / packed[width : width + 1]
    value = jnp.maximum(continuation, exercise.T).astype(jnp.bfloat16)
    for bit in reversed(HALVING_BITS):
        mine_hi = (me >> bit) & 1
        got = lax.ppermute(value, "src", xor_perm(src_size, bit))
        value = jnp.where(
            mine_hi == 1,
            jnp.concatenate([got, value], 1),
            jnp.concatenate([value, got], 1),
        )
    return value


def lin(t, s):
    return t * lax.axis_size("src") + s


Z_PLAN = ((3, 1, 1), (3, 1, 1), (3, 1, 1), (3, 1, 1), (2, 2, 1), (2, 2, 1), (0, 0, 0), (0, 0, 0))


def column_offset(s):
    y, z_lo = s % 8, s // 8
    dz = Z_PLAN[y][z_lo]
    same_dz = [(yy, zz) for yy in range(8) for zz in range(2) if Z_PLAN[yy][zz] == dz]
    return dz, same_dz.index((y, z_lo))


def holder(s):
    return s ^ (8 * Z_PLAN[s % 8][2])


def source_pair(t, s):
    x_count = lax.axis_size("tgt") // 8
    z_hi, x = t // (2 * x_count), (t // 2) % x_count
    if isinstance(s, int):
        dz, dx = column_offset(s)
    else:
        y, z_lo = s % 8, s // 8
        dz = jnp.where(y < 4, 3 - 2 * z_lo, jnp.where(y < 6, 2, 0))
        dx = jnp.where(y < 4, y, (y % 2) * 2 + z_lo)
    return ((z_hi + dz) % 4) * x_count + (x + dx) % x_count


def regroup(block_rows):
    tgt_size = lax.axis_size("tgt")
    src_size = lax.axis_size("src")
    perms = ([], [])
    for t in range(tgt_size):
        for s in range(src_size):
            pair = source_pair(t, s)
            for flip in range(2):
                u = 2 * pair + ((t % 2) ^ flip)
                perms[flip].append((lin(u, holder(s)), lin(t, s)))
    return [lax.ppermute(block_rows, ("tgt", "src"), p) for p in perms]


def regroup_order(got, axis=0):
    odd = lax.axis_index("tgt") % 2 == 1
    return jnp.concatenate(
        [jnp.where(odd, got[1], got[0]), jnp.where(odd, got[0], got[1])], axis
    )


def regroup_offsets(offsets):
    tgt_size = lax.axis_size("tgt")
    src_size = lax.axis_size("src")
    pairs = [
        (lin(t, source_pair(t, s)), lin(t, s)) for t in range(tgt_size) for s in range(src_size)
    ]
    return lax.ppermute(offsets, ("tgt", "src"), pairs)


def per_device(
    states_late,
    offset_late,
    values_late,
    states_mid,
    offset_mid,
    exercise_mid,
    mask_mid,
    states_early,
    exercise_early,
    mask_early,
):
    src_tiles = states_late.shape[0] // BLOCK

    def mid_col_base():
        return lax.axis_index("src") * src_tiles

    def early_col_base():
        return source_pair(lax.axis_index("tgt"), lax.axis_index("src")) * src_tiles

    mid_sources = regroup_order(regroup(states_mid))
    mid_offsets = regroup_offsets(offset_mid)
    partials = date_partials_kernel(
        states_mid, states_late, offset_late, values_late.T, mask_mid, mid_col_base
    )
    partials, mid_sources, mid_offsets = lax.optimization_barrier(
        (partials, mid_sources, mid_offsets)
    )
    early_parts = []
    for row_tile in range(states_early.shape[0] // BLOCK):
        rows = states_early[row_tile * BLOCK : (row_tile + 1) * BLOCK]
        early_parts.append(
            date_weights_kernel(
                rows, mid_sources, mid_offsets, mask_early, row_tile, early_col_base
            )
        )
    value_mid_t = finish(partials, exercise_mid)
    mid_values_t = regroup_order(regroup(value_mid_t), axis=1)
    early_weighted = jnp.concatenate(
        [jnp.dot(mid_values_t, w, preferred_element_type=jnp.float32) for w, _ in early_parts], 1
    )
    early_stats = jnp.concatenate([s for _, s in early_parts], 1)
    value_early_t = finish(jnp.concatenate([early_weighted, early_stats], 0), exercise_early)
    value_mid, value_early = value_mid_t.T, value_early_t.T
    return (value_mid, value_early)


def solution(mesh):
    in_specs = (
        P("src", None),
        P("src"),
        P("src", None),
        P("tgt", None),
        P("src"),
        P("tgt", None),
        P(),
        P("tgt", None),
        P("tgt", None),
        P(),
    )
    out_specs = (P("tgt", None), P("tgt", None))
    return jax.shard_map(per_device, mesh=mesh, in_specs=in_specs, out_specs=out_specs, check_vma=False)
```

```python
import jax
import jax.numpy as jnp
from jax import lax
from jax.experimental import pallas as pl
from jax.experimental.pallas import tpu as pltpu
from jax.sharding import PartitionSpec as P


BLOCK = 512


sharpness = 3.5
very_low = -1e30


def row_tile_base(row_tiles):
    return lax.axis_index("tgt") * row_tiles


def offset_column(off_row):
    wide = jnp.broadcast_to(off_row.astype(jnp.float32), (8, off_row.shape[1]))
    return jnp.transpose(wide)[:, 0:1]


def partials_kernel(mask_ref, x_ref, y_ref, off_ref, v_ref, out_ref, *, scale, row_tiles, col_tiles, col_base):
    i = pl.program_id(0)
    row = row_tile_base(row_tiles) + i
    col0 = col_base()
    width = v_ref.shape[0]
    out_ref[0 : width + 1, :] = jnp.zeros((width + 1, BLOCK), jnp.float32)
    out_ref[width + 1 : width + 2, :] = jnp.full((1, BLOCK), very_low, jnp.float32)
    for j in range(col_tiles):
        live = mask_ref[row, col0 + j] > 0
        y = y_ref[j * BLOCK : (j + 1) * BLOCK, :]
        s = lax.dot_general(y, x_ref[...], (((1,), (1,)), ((), ())), preferred_element_type=jnp.float32)
        s = s * scale - offset_column(off_ref[:, j * BLOCK : (j + 1) * BLOCK])
        m_old = out_ref[width + 1 : width + 2, :]
        m_new = jnp.where(live, jnp.maximum(m_old, jnp.max(s, axis=0, keepdims=True)), m_old)
        shrink = jnp.exp(m_old - m_new)
        p = jnp.where(live, jnp.exp(s - m_new), 0.0)
        out_ref[width : width + 1, :] = out_ref[width : width + 1, :] * shrink + jnp.sum(p, axis=0, keepdims=True)
        out_ref[0:width, :] = out_ref[0:width, :] * shrink + jnp.dot(
            v_ref[:, j * BLOCK : (j + 1) * BLOCK], p.astype(jnp.bfloat16), preferred_element_type=jnp.float32
        )
        out_ref[width + 1 : width + 2, :] = m_new


def date_partials_kernel(targets, sources, offsets, values_t, tile_mask, col_base):
    rows, factors = targets.shape
    cols = sources.shape[0]
    width = values_t.shape[0]
    row_tiles, col_tiles = rows // BLOCK, cols // BLOCK
    kernel = lambda *refs: partials_kernel(
        *refs, scale=sharpness / factors**0.5, row_tiles=row_tiles, col_tiles=col_tiles, col_base=col_base
    )
    return pl.pallas_call(
        kernel,
        out_shape=jax.ShapeDtypeStruct((width + 2, rows), jnp.float32),
        grid_spec=pltpu.PrefetchScalarGridSpec(
            num_scalar_prefetch=1,
            grid=(row_tiles,),
            in_specs=[
                pl.BlockSpec((BLOCK, factors), lambda i, m: (i, 0)),
                pl.BlockSpec((cols, factors), lambda i, m: (0, 0)),
                pl.BlockSpec((1, cols), lambda i, m: (0, 0)),
                pl.BlockSpec((width, cols), lambda i, m: (0, 0)),
            ],
            out_specs=pl.BlockSpec((width + 2, BLOCK), lambda i, m: (0, i)),
        ),
        compiler_params=pltpu.CompilerParams(dimension_semantics=("arbitrary",)),
    )(tile_mask, targets, sources, offsets.reshape(1, cols), values_t)


def weights_kernel(mask_ref, x_ref, y_ref, off_ref, p_ref, stats_ref, *, scale, row_tile, col_tiles, col_base):
    row = row_tile_base(2) + row_tile
    col0 = col_base()

    def scores(j):
        y = y_ref[j * BLOCK : (j + 1) * BLOCK, :]
        s = lax.dot_general(y, x_ref[...], (((1,), (1,)), ((), ())), preferred_element_type=jnp.float32)
        return s * scale - offset_column(off_ref[:, j * BLOCK : (j + 1) * BLOCK])

    peak = jnp.full((1, BLOCK), very_low, jnp.float32)
    for j in range(col_tiles):
        live = mask_ref[row, col0 + j] > 0
        peak = jnp.where(live, jnp.maximum(peak, jnp.max(scores(j), axis=0, keepdims=True)), peak)
    total = jnp.zeros((1, BLOCK), jnp.float32)
    for j in range(col_tiles):
        live = mask_ref[row, col0 + j] > 0
        p = jnp.where(live, jnp.exp(scores(j) - peak), 0.0)
        p_ref[j * BLOCK : (j + 1) * BLOCK, :] = p.astype(jnp.bfloat16)
        total = total + jnp.sum(p, axis=0, keepdims=True)
    stats_ref[0:1, :] = total
    stats_ref[1:2, :] = peak


def date_weights_kernel(targets, sources, offsets, tile_mask, row_tile, col_base):
    rows, factors = targets.shape
    cols = sources.shape[0]
    col_tiles = cols // BLOCK
    kernel = lambda *refs: weights_kernel(
        *refs, scale=sharpness / factors**0.5, row_tile=row_tile, col_tiles=col_tiles, col_base=col_base
    )
    return pl.pallas_call(
        kernel,
        out_shape=(
            jax.ShapeDtypeStruct((cols, rows), jnp.bfloat16),
            jax.ShapeDtypeStruct((2, rows), jnp.float32),
        ),
        grid_spec=pltpu.PrefetchScalarGridSpec(
            num_scalar_prefetch=1,
            grid=(1,),
            in_specs=[
                pl.BlockSpec((BLOCK, factors), lambda i, m: (0, 0)),
                pl.BlockSpec((cols, factors), lambda i, m: (0, 0)),
                pl.BlockSpec((1, cols), lambda i, m: (0, 0)),
            ],
            out_specs=(
                pl.BlockSpec((cols, BLOCK), lambda i, m: (0, 0)),
                pl.BlockSpec((2, BLOCK), lambda i, m: (0, 0)),
            ),
        ),
        compiler_params=pltpu.CompilerParams(dimension_semantics=("arbitrary",)),
    )(tile_mask, targets, sources, offsets.reshape(1, cols))


HALVING_BITS = (3,)
FAR_PARTNER = (6, 7, 4, 5, 2, 3, 0, 1)
EXCHANGES = (lambda y: y ^ 1, lambda y: y ^ 2, lambda y: FAR_PARTNER[y])


def xor_perm(size, bit):
    return [(i, i ^ (1 << bit)) for i in range(size)]


def exchange_perm(size, partner):
    return [(i, (i // 8) * 8 + partner(i % 8)) for i in range(size)]


def merge(mine, theirs):
    width = mine.shape[0] - 2
    peak_a, peak_b = mine[width + 1 :], theirs[width + 1 :]
    peak = jnp.maximum(peak_a, peak_b)
    scale_a = jnp.exp(peak_a - peak)
    scale_b = jnp.exp(peak_b - peak)
    body = mine[: width + 1] * scale_a + theirs[: width + 1] * scale_b
    return jnp.concatenate([body, peak], axis=0)


def finish(packed, exercise):
    src_size = lax.axis_size("src")
    me = lax.axis_index("src")
    exercise = exercise.astype(jnp.float32)
    for bit in HALVING_BITS:
        half = packed.shape[1] // 2
        mine_hi = (me >> bit) & 1
        keep = lax.dynamic_slice_in_dim(packed, mine_hi * half, half, 1)
        send = lax.dynamic_slice_in_dim(packed, (1 - mine_hi) * half, half, 1)
        got = lax.ppermute(send, "src", xor_perm(src_size, bit))
        packed = merge(keep, got)
        exercise = lax.dynamic_slice_in_dim(exercise, mine_hi * half, half, 0)
    for partner in EXCHANGES:
        got = lax.ppermute(packed, "src", exchange_perm(src_size, partner))
        packed = merge(packed, got)
    width = packed.shape[0] - 2
    continuation = packed[:width] / packed[width : width + 1]
    value = jnp.maximum(continuation, exercise.T).astype(jnp.bfloat16)
    for bit in reversed(HALVING_BITS):
        mine_hi = (me >> bit) & 1
        got = lax.ppermute(value, "src", xor_perm(src_size, bit))
        value = jnp.where(
            mine_hi == 1,
            jnp.concatenate([got, value], 1),
            jnp.concatenate([value, got], 1),
        )
    return value


def lin(t, s):
    return t * lax.axis_size("src") + s


Z_PLAN = ((3, 1, 1), (3, 1, 1), (3, 1, 1), (3, 1, 1), (2, 2, 1), (2, 2, 1), (0, 0, 0), (0, 0, 0))


def column_offset(s):
    y, z_lo = s % 8, s // 8
    dz = Z_PLAN[y][z_lo]
    same_dz = [(yy, zz) for yy in range(8) for zz in range(2) if Z_PLAN[yy][zz] == dz]
    return dz, same_dz.index((y, z_lo))


def holder(s):
    return s ^ (8 * Z_PLAN[s % 8][2])


def source_pair(t, s):
    x_count = lax.axis_size("tgt") // 8
    z_hi, x = t // (2 * x_count), (t // 2) % x_count
    if isinstance(s, int):
        dz, dx = column_offset(s)
    else:
        y, z_lo = s % 8, s // 8
        dz = jnp.where(y < 4, 3 - 2 * z_lo, jnp.where(y < 6, 2, 0))
        dx = jnp.where(y < 4, y, (y % 2) * 2 + z_lo)
    return ((z_hi + dz) % 4) * x_count + (x + dx) % x_count


def regroup(block_rows):
    tgt_size = lax.axis_size("tgt")
    src_size = lax.axis_size("src")
    perms = ([], [])
    for t in range(tgt_size):
        for s in range(src_size):
            pair = source_pair(t, s)
            for flip in range(2):
                u = 2 * pair + ((t % 2) ^ flip)
                perms[flip].append((lin(u, holder(s)), lin(t, s)))
    return [lax.ppermute(block_rows, ("tgt", "src"), p) for p in perms]


def regroup_order(got, axis=0):
    odd = lax.axis_index("tgt") % 2 == 1
    return jnp.concatenate(
        [jnp.where(odd, got[1], got[0]), jnp.where(odd, got[0], got[1])], axis
    )


def regroup_offsets(offsets):
    tgt_size = lax.axis_size("tgt")
    src_size = lax.axis_size("src")
    pairs = [
        (lin(t, source_pair(t, s)), lin(t, s)) for t in range(tgt_size) for s in range(src_size)
    ]
    return lax.ppermute(offsets, ("tgt", "src"), pairs)


def per_device(
    states_late,
    offset_late,
    values_late,
    states_mid,
    offset_mid,
    exercise_mid,
    mask_mid,
    states_early,
    exercise_early,
    mask_early,
):
    src_tiles = states_late.shape[0] // BLOCK

    def mid_col_base():
        return lax.axis_index("src") * src_tiles

    def early_col_base():
        return source_pair(lax.axis_index("tgt"), lax.axis_index("src")) * src_tiles

    mid_sources = regroup_order(regroup(states_mid))
    mid_offsets = regroup_offsets(offset_mid)
    partials = date_partials_kernel(
        states_mid, states_late, offset_late, values_late.T, mask_mid, mid_col_base
    )
    partials, mid_sources, mid_offsets = lax.optimization_barrier(
        (partials, mid_sources, mid_offsets)
    )
    early_parts = []
    for row_tile in range(states_early.shape[0] // BLOCK):
        rows = states_early[row_tile * BLOCK : (row_tile + 1) * BLOCK]
        early_parts.append(
            date_weights_kernel(
                rows, mid_sources, mid_offsets, mask_early, row_tile, early_col_base
            )
        )
    value_mid_t = finish(partials, exercise_mid)
    mid_values_t = regroup_order(regroup(value_mid_t), axis=1)
    early_weighted = jnp.concatenate(
        [jnp.dot(mid_values_t, w, preferred_element_type=jnp.float32) for w, _ in early_parts], 1
    )
    early_stats = jnp.concatenate([s for _, s in early_parts], 1)
    value_early_t = finish(jnp.concatenate([early_weighted, early_stats], 0), exercise_early)
    value_mid, value_early = value_mid_t.T, value_early_t.T
    return (value_mid, value_early)


def solution(mesh):
    in_specs = (
        P("src", None),
        P("src"),
        P("src", None),
        P("tgt", None),
        P("src"),
        P("tgt", None),
        P(),
        P("tgt", None),
        P("tgt", None),
        P(),
    )
    out_specs = (P("tgt", None), P("tgt", None))
    return jax.shard_map(per_device, mesh=mesh, in_specs=in_specs, out_specs=out_specs, check_vma=False)
```

```python
import jax
import jax.numpy as jnp
from jax import lax
from jax.experimental import pallas as pl
from jax.experimental.pallas import tpu as pltpu
from jax.sharding import PartitionSpec as P


BLOCK = 512


sharpness = 3.5
very_low = -1e30


def row_tile_base(row_tiles):
    return lax.axis_index("tgt") * row_tiles


def offset_column(off_row):
    wide = jnp.broadcast_to(off_row.astype(jnp.float32), (8, off_row.shape[1]))
    return jnp.transpose(wide)[:, 0:1]


def partials_kernel(mask_ref, x_ref, y_ref, off_ref, v_ref, out_ref, *, scale, row_tiles, col_tiles, col_base):
    i = pl.program_id(0)
    row = row_tile_base(row_tiles) + i
    col0 = col_base()
    width = v_ref.shape[0]
    out_ref[0 : width + 1, :] = jnp.zeros((width + 1, BLOCK), jnp.float32)
    out_ref[width + 1 : width + 2, :] = jnp.full((1, BLOCK), very_low, jnp.float32)
    for j in range(col_tiles):
        live = mask_ref[row, col0 + j] > 0
        y = y_ref[j * BLOCK : (j + 1) * BLOCK, :]
        s = lax.dot_general(y, x_ref[...], (((1,), (1,)), ((), ())), preferred_element_type=jnp.float32)
        s = s * scale - offset_column(off_ref[:, j * BLOCK : (j + 1) * BLOCK])
        m_old = out_ref[width + 1 : width + 2, :]
        m_new = jnp.where(live, jnp.maximum(m_old, jnp.max(s, axis=0, keepdims=True)), m_old)
        shrink = jnp.exp(m_old - m_new)
        p = jnp.where(live, jnp.exp(s - m_new), 0.0)
        out_ref[width : width + 1, :] = out_ref[width : width + 1, :] * shrink + jnp.sum(p, axis=0, keepdims=True)
        out_ref[0:width, :] = out_ref[0:width, :] * shrink + jnp.dot(
            v_ref[:, j * BLOCK : (j + 1) * BLOCK], p.astype(jnp.bfloat16), preferred_element_type=jnp.float32
        )
        out_ref[width + 1 : width + 2, :] = m_new


def date_partials_kernel(targets, sources, offsets, values_t, tile_mask, col_base):
    rows, factors = targets.shape
    cols = sources.shape[0]
    width = values_t.shape[0]
    row_tiles, col_tiles = rows // BLOCK, cols // BLOCK
    kernel = lambda *refs: partials_kernel(
        *refs, scale=sharpness / factors**0.5, row_tiles=row_tiles, col_tiles=col_tiles, col_base=col_base
    )
    return pl.pallas_call(
        kernel,
        out_shape=jax.ShapeDtypeStruct((width + 2, rows), jnp.float32),
        grid_spec=pltpu.PrefetchScalarGridSpec(
            num_scalar_prefetch=1,
            grid=(row_tiles,),
            in_specs=[
                pl.BlockSpec((BLOCK, factors), lambda i, m: (i, 0)),
                pl.BlockSpec((cols, factors), lambda i, m: (0, 0)),
                pl.BlockSpec((1, cols), lambda i, m: (0, 0)),
                pl.BlockSpec((width, cols), lambda i, m: (0, 0)),
            ],
            out_specs=pl.BlockSpec((width + 2, BLOCK), lambda i, m: (0, i)),
        ),
        compiler_params=pltpu.CompilerParams(dimension_semantics=("arbitrary",)),
    )(tile_mask, targets, sources, offsets.reshape(1, cols), values_t)


def weights_kernel(mask_ref, x_ref, y_ref, off_ref, p_ref, stats_ref, *, scale, row_tile, col_tiles, col_base):
    row = row_tile_base(2) + row_tile
    col0 = col_base()

    def scores(j):
        y = y_ref[j * BLOCK : (j + 1) * BLOCK, :]
        s = lax.dot_general(y, x_ref[...], (((1,), (1,)), ((), ())), preferred_element_type=jnp.float32)
        return s * scale - offset_column(off_ref[:, j * BLOCK : (j + 1) * BLOCK])

    peak = jnp.full((1, BLOCK), very_low, jnp.float32)
    for j in range(col_tiles):
        live = mask_ref[row, col0 + j] > 0
        peak = jnp.where(live, jnp.maximum(peak, jnp.max(scores(j), axis=0, keepdims=True)), peak)
    total = jnp.zeros((1, BLOCK), jnp.float32)
    for j in range(col_tiles):
        live = mask_ref[row, col0 + j] > 0
        p = jnp.where(live, jnp.exp(scores(j) - peak), 0.0)
        p_ref[j * BLOCK : (j + 1) * BLOCK, :] = p.astype(jnp.bfloat16)
        total = total + jnp.sum(p, axis=0, keepdims=True)
    stats_ref[0:1, :] = total
    stats_ref[1:2, :] = peak


def date_weights_kernel(targets, sources, offsets, tile_mask, row_tile, col_base):
    rows, factors = targets.shape
    cols = sources.shape[0]
    col_tiles = cols // BLOCK
    kernel = lambda *refs: weights_kernel(
        *refs, scale=sharpness / factors**0.5, row_tile=row_tile, col_tiles=col_tiles, col_base=col_base
    )
    return pl.pallas_call(
        kernel,
        out_shape=(
            jax.ShapeDtypeStruct((cols, rows), jnp.bfloat16),
            jax.ShapeDtypeStruct((2, rows), jnp.float32),
        ),
        grid_spec=pltpu.PrefetchScalarGridSpec(
            num_scalar_prefetch=1,
            grid=(1,),
            in_specs=[
                pl.BlockSpec((BLOCK, factors), lambda i, m: (0, 0)),
                pl.BlockSpec((cols, factors), lambda i, m: (0, 0)),
                pl.BlockSpec((1, cols), lambda i, m: (0, 0)),
            ],
            out_specs=(
                pl.BlockSpec((cols, BLOCK), lambda i, m: (0, 0)),
                pl.BlockSpec((2, BLOCK), lambda i, m: (0, 0)),
            ),
        ),
        compiler_params=pltpu.CompilerParams(dimension_semantics=("arbitrary",)),
    )(tile_mask, targets, sources, offsets.reshape(1, cols))


HALVING_BITS = (3,)
FAR_PARTNER = (6, 7, 4, 5, 2, 3, 0, 1)
EXCHANGES = (lambda y: y ^ 1, lambda y: y ^ 2, lambda y: FAR_PARTNER[y])


def xor_perm(size, bit):
    return [(i, i ^ (1 << bit)) for i in range(size)]


def exchange_perm(size, partner):
    return [(i, (i // 8) * 8 + partner(i % 8)) for i in range(size)]


def merge(mine, theirs):
    width = mine.shape[0] - 2
    peak_a, peak_b = mine[width + 1 :], theirs[width + 1 :]
    peak = jnp.maximum(peak_a, peak_b)
    scale_a = jnp.exp(peak_a - peak)
    scale_b = jnp.exp(peak_b - peak)
    body = mine[: width + 1] * scale_a + theirs[: width + 1] * scale_b
    return jnp.concatenate([body, peak], axis=0)


def finish(packed, exercise):
    src_size = lax.axis_size("src")
    me = lax.axis_index("src")
    exercise = exercise.astype(jnp.float32)
    for bit in HALVING_BITS:
        half = packed.shape[1] // 2
        mine_hi = (me >> bit) & 1
        keep = lax.dynamic_slice_in_dim(packed, mine_hi * half, half, 1)
        send = lax.dynamic_slice_in_dim(packed, (1 - mine_hi) * half, half, 1)
        got = lax.ppermute(send, "src", xor_perm(src_size, bit))
        packed = merge(keep, got)
        exercise = lax.dynamic_slice_in_dim(exercise, mine_hi * half, half, 0)
    for partner in EXCHANGES:
        got = lax.ppermute(packed, "src", exchange_perm(src_size, partner))
        packed = merge(packed, got)
    width = packed.shape[0] - 2
    continuation = packed[:width] / packed[width : width + 1]
    value = jnp.maximum(continuation, exercise.T).astype(jnp.bfloat16)
    for bit in reversed(HALVING_BITS):
        mine_hi = (me >> bit) & 1
        got = lax.ppermute(value, "src", xor_perm(src_size, bit))
        value = jnp.where(
            mine_hi == 1,
            jnp.concatenate([got, value], 1),
            jnp.concatenate([value, got], 1),
        )
    return value


def lin(t, s):
    return t * lax.axis_size("src") + s


Z_PLAN = ((3, 1, 1), (3, 1, 1), (3, 1, 1), (3, 1, 1), (2, 2, 1), (2, 2, 1), (0, 0, 0), (0, 0, 0))


def column_offset(s):
    y, z_lo = s % 8, s // 8
    dz = Z_PLAN[y][z_lo]
    same_dz = [(yy, zz) for yy in range(8) for zz in range(2) if Z_PLAN[yy][zz] == dz]
    return dz, same_dz.index((y, z_lo))


def holder(s):
    return s ^ (8 * Z_PLAN[s % 8][2])


def source_pair(t, s):
    x_count = lax.axis_size("tgt") // 8
    z_hi, x = t // (2 * x_count), (t // 2) % x_count
    if isinstance(s, int):
        dz, dx = column_offset(s)
    else:
        y, z_lo = s % 8, s // 8
        dz = jnp.where(y < 4, 3 - 2 * z_lo, jnp.where(y < 6, 2, 0))
        dx = jnp.where(y < 4, y, (y % 2) * 2 + z_lo)
    return ((z_hi + dz) % 4) * x_count + (x + dx) % x_count


def regroup(block_rows):
    tgt_size = lax.axis_size("tgt")
    src_size = lax.axis_size("src")
    perms = ([], [])
    for t in range(tgt_size):
        for s in range(src_size):
            pair = source_pair(t, s)
            for flip in range(2):
                u = 2 * pair + ((t % 2) ^ flip)
                perms[flip].append((lin(u, holder(s)), lin(t, s)))
    return [lax.ppermute(block_rows, ("tgt", "src"), p) for p in perms]


def forward_perms():
    tgt_size = lax.axis_size("tgt")
    src_size = lax.axis_size("src")
    direct, swap = [], []
    for t in range(tgt_size):
        for s in range(src_size):
            u = 2 * source_pair(t, s) + t % 2
            direct.append((lin(u, holder(s)), lin(t, s)))
            swap.append((lin(t ^ 1, s), lin(t, s)))
    return direct, swap


def regroup_order(got, axis=0):
    odd = lax.axis_index("tgt") % 2 == 1
    return jnp.concatenate(
        [jnp.where(odd, got[1], got[0]), jnp.where(odd, got[0], got[1])], axis
    )


def regroup_offsets(offsets):
    tgt_size = lax.axis_size("tgt")
    src_size = lax.axis_size("src")
    pairs = [
        (lin(t, source_pair(t, s)), lin(t, s)) for t in range(tgt_size) for s in range(src_size)
    ]
    return lax.ppermute(offsets, ("tgt", "src"), pairs)


def per_device(
    states_late,
    offset_late,
    values_late,
    states_mid,
    offset_mid,
    exercise_mid,
    mask_mid,
    states_early,
    exercise_early,
    mask_early,
):
    src_tiles = states_late.shape[0] // BLOCK

    def mid_col_base():
        return lax.axis_index("src") * src_tiles

    def early_col_base():
        return source_pair(lax.axis_index("tgt"), lax.axis_index("src")) * src_tiles

    direct, swap = forward_perms()
    own_sources = lax.ppermute(states_mid, ("tgt", "src"), direct)
    mid_offsets = regroup_offsets(offset_mid)
    partials = date_partials_kernel(
        states_mid, states_late, offset_late, values_late.T, mask_mid, mid_col_base
    )
    partials, own_sources, mid_offsets = lax.optimization_barrier(
        (partials, own_sources, mid_offsets)
    )
    mid_sources = regroup_order(
        [own_sources, lax.ppermute(own_sources, ("tgt", "src"), swap)]
    )
    early_parts = []
    for row_tile in range(states_early.shape[0] // BLOCK):
        rows = states_early[row_tile * BLOCK : (row_tile + 1) * BLOCK]
        early_parts.append(
            date_weights_kernel(
                rows, mid_sources, mid_offsets, mask_early, row_tile, early_col_base
            )
        )
    value_mid_t = finish(partials, exercise_mid)
    mid_values_t = regroup_order(regroup(value_mid_t), axis=1)
    early_weighted = jnp.concatenate(
        [jnp.dot(mid_values_t, w, preferred_element_type=jnp.float32) for w, _ in early_parts], 1
    )
    early_stats = jnp.concatenate([s for _, s in early_parts], 1)
    value_early_t = finish(jnp.concatenate([early_weighted, early_stats], 0), exercise_early)
    value_mid, value_early = value_mid_t.T, value_early_t.T
    return (value_mid, value_early)


def solution(mesh):
    in_specs = (
        P("src", None),
        P("src"),
        P("src", None),
        P("tgt", None),
        P("src"),
        P("tgt", None),
        P(),
        P("tgt", None),
        P("tgt", None),
        P(),
    )
    out_specs = (P("tgt", None), P("tgt", None))
    return jax.shard_map(per_device, mesh=mesh, in_specs=in_specs, out_specs=out_specs, check_vma=False)
```

```python
import jax
import jax.numpy as jnp
from jax import lax
from jax.experimental import pallas as pl
from jax.experimental.pallas import tpu as pltpu
from jax.sharding import PartitionSpec as P


BLOCK = 512


sharpness = 3.5
very_low = -1e30


def row_tile_base(row_tiles):
    return lax.axis_index("tgt") * row_tiles


def offset_column(off_row):
    wide = jnp.broadcast_to(off_row.astype(jnp.float32), (8, off_row.shape[1]))
    return jnp.transpose(wide)[:, 0:1]


def partials_kernel(mask_ref, x_ref, y_ref, off_ref, v_ref, out_ref, *, scale, row_tiles, col_tiles, col_base):
    i = pl.program_id(0)
    row = row_tile_base(row_tiles) + i
    col0 = col_base()
    width = v_ref.shape[0]
    out_ref[0 : width + 1, :] = jnp.zeros((width + 1, BLOCK), jnp.float32)
    out_ref[width + 1 : width + 2, :] = jnp.full((1, BLOCK), very_low, jnp.float32)
    for j in range(col_tiles):
        live = mask_ref[row, col0 + j] > 0
        y = y_ref[j * BLOCK : (j + 1) * BLOCK, :]
        s = lax.dot_general(y, x_ref[...], (((1,), (1,)), ((), ())), preferred_element_type=jnp.float32)
        s = s * scale - offset_column(off_ref[:, j * BLOCK : (j + 1) * BLOCK])
        m_old = out_ref[width + 1 : width + 2, :]
        m_new = jnp.where(live, jnp.maximum(m_old, jnp.max(s, axis=0, keepdims=True)), m_old)
        shrink = jnp.exp(m_old - m_new)
        p = jnp.where(live, jnp.exp(s - m_new), 0.0)
        out_ref[width : width + 1, :] = out_ref[width : width + 1, :] * shrink + jnp.sum(p, axis=0, keepdims=True)
        out_ref[0:width, :] = out_ref[0:width, :] * shrink + jnp.dot(
            v_ref[:, j * BLOCK : (j + 1) * BLOCK], p.astype(jnp.bfloat16), preferred_element_type=jnp.float32
        )
        out_ref[width + 1 : width + 2, :] = m_new


def date_partials_kernel(targets, sources, offsets, values_t, tile_mask, col_base):
    rows, factors = targets.shape
    cols = sources.shape[0]
    width = values_t.shape[0]
    row_tiles, col_tiles = rows // BLOCK, cols // BLOCK
    kernel = lambda *refs: partials_kernel(
        *refs, scale=sharpness / factors**0.5, row_tiles=row_tiles, col_tiles=col_tiles, col_base=col_base
    )
    return pl.pallas_call(
        kernel,
        out_shape=jax.ShapeDtypeStruct((width + 2, rows), jnp.float32),
        grid_spec=pltpu.PrefetchScalarGridSpec(
            num_scalar_prefetch=1,
            grid=(row_tiles,),
            in_specs=[
                pl.BlockSpec((BLOCK, factors), lambda i, m: (i, 0)),
                pl.BlockSpec((cols, factors), lambda i, m: (0, 0)),
                pl.BlockSpec((1, cols), lambda i, m: (0, 0)),
                pl.BlockSpec((width, cols), lambda i, m: (0, 0)),
            ],
            out_specs=pl.BlockSpec((width + 2, BLOCK), lambda i, m: (0, i)),
        ),
        compiler_params=pltpu.CompilerParams(dimension_semantics=("arbitrary",)),
    )(tile_mask, targets, sources, offsets.reshape(1, cols), values_t)


def weights_kernel(mask_ref, x_ref, y_ref, off_ref, p_ref, stats_ref, *, scale, row_tile, col_tiles, col_base):
    row = row_tile_base(2) + row_tile
    col0 = col_base()

    def scores(j):
        y = y_ref[j * BLOCK : (j + 1) * BLOCK, :]
        s = lax.dot_general(y, x_ref[...], (((1,), (1,)), ((), ())), preferred_element_type=jnp.float32)
        return s * scale - offset_column(off_ref[:, j * BLOCK : (j + 1) * BLOCK])

    peak = jnp.full((1, BLOCK), very_low, jnp.float32)
    for j in range(col_tiles):
        live = mask_ref[row, col0 + j] > 0
        peak = jnp.where(live, jnp.maximum(peak, jnp.max(scores(j), axis=0, keepdims=True)), peak)
    total = jnp.zeros((1, BLOCK), jnp.float32)
    for j in range(col_tiles):
        live = mask_ref[row, col0 + j] > 0
        p = jnp.where(live, jnp.exp(scores(j) - peak), 0.0)
        p_ref[j * BLOCK : (j + 1) * BLOCK, :] = p.astype(jnp.bfloat16)
        total = total + jnp.sum(p, axis=0, keepdims=True)
    stats_ref[0:1, :] = total
    stats_ref[1:2, :] = peak


def date_weights_kernel(targets, sources, offsets, tile_mask, row_tile, col_base):
    rows, factors = targets.shape
    cols = sources.shape[0]
    col_tiles = cols // BLOCK
    kernel = lambda *refs: weights_kernel(
        *refs, scale=sharpness / factors**0.5, row_tile=row_tile, col_tiles=col_tiles, col_base=col_base
    )
    return pl.pallas_call(
        kernel,
        out_shape=(
            jax.ShapeDtypeStruct((cols, rows), jnp.bfloat16),
            jax.ShapeDtypeStruct((2, rows), jnp.float32),
        ),
        grid_spec=pltpu.PrefetchScalarGridSpec(
            num_scalar_prefetch=1,
            grid=(1,),
            in_specs=[
                pl.BlockSpec((BLOCK, factors), lambda i, m: (0, 0)),
                pl.BlockSpec((cols, factors), lambda i, m: (0, 0)),
                pl.BlockSpec((1, cols), lambda i, m: (0, 0)),
            ],
            out_specs=(
                pl.BlockSpec((cols, BLOCK), lambda i, m: (0, 0)),
                pl.BlockSpec((2, BLOCK), lambda i, m: (0, 0)),
            ),
        ),
        compiler_params=pltpu.CompilerParams(dimension_semantics=("arbitrary",)),
    )(tile_mask, targets, sources, offsets.reshape(1, cols))


HALVING_BITS = (3,)
FAR_PARTNER = (6, 7, 4, 5, 2, 3, 0, 1)
EXCHANGES = (lambda y: y ^ 1, lambda y: y ^ 2, lambda y: FAR_PARTNER[y])


def xor_perm(size, bit):
    return [(i, i ^ (1 << bit)) for i in range(size)]


def exchange_perm(size, partner):
    return [(i, (i // 8) * 8 + partner(i % 8)) for i in range(size)]


def merge(mine, theirs):
    width = mine.shape[0] - 2
    peak_a, peak_b = mine[width + 1 :], theirs[width + 1 :]
    peak = jnp.maximum(peak_a, peak_b)
    scale_a = jnp.exp(peak_a - peak)
    scale_b = jnp.exp(peak_b - peak)
    body = mine[: width + 1] * scale_a + theirs[: width + 1] * scale_b
    return jnp.concatenate([body, peak], axis=0)


def finish(packed, exercise):
    src_size = lax.axis_size("src")
    me = lax.axis_index("src")
    exercise = exercise.astype(jnp.float32)
    for bit in HALVING_BITS:
        half = packed.shape[1] // 2
        mine_hi = (me >> bit) & 1
        keep = lax.dynamic_slice_in_dim(packed, mine_hi * half, half, 1)
        send = lax.dynamic_slice_in_dim(packed, (1 - mine_hi) * half, half, 1)
        got = lax.ppermute(send, "src", xor_perm(src_size, bit))
        packed = merge(keep, got)
        exercise = lax.dynamic_slice_in_dim(exercise, mine_hi * half, half, 0)
    for partner in EXCHANGES:
        got = lax.ppermute(packed, "src", exchange_perm(src_size, partner))
        packed = merge(packed, got)
    width = packed.shape[0] - 2
    continuation = packed[:width] / packed[width : width + 1]
    value = jnp.maximum(continuation, exercise.T).astype(jnp.bfloat16)
    for bit in reversed(HALVING_BITS):
        mine_hi = (me >> bit) & 1
        got = lax.ppermute(value, "src", xor_perm(src_size, bit))
        value = jnp.where(
            mine_hi == 1,
            jnp.concatenate([got, value], 1),
            jnp.concatenate([value, got], 1),
        )
    return value


def lin(t, s):
    return t * lax.axis_size("src") + s


Z_PLAN = ((3, 1, 1), (3, 1, 1), (3, 1, 1), (3, 1, 1), (2, 2, 1), (2, 2, 1), (0, 0, 0), (0, 0, 0))


def column_offset(s):
    y, z_lo = s % 8, s // 8
    dz = Z_PLAN[y][z_lo]
    same_dz = [(yy, zz) for yy in range(8) for zz in range(2) if Z_PLAN[yy][zz] == dz]
    return dz, same_dz.index((y, z_lo))


def holder(s):
    return s ^ (8 * Z_PLAN[s % 8][2])


def source_pair(t, s):
    x_count = lax.axis_size("tgt") // 8
    z_hi, x = t // (2 * x_count), (t // 2) % x_count
    if isinstance(s, int):
        dz, dx = column_offset(s)
    else:
        y, z_lo = s % 8, s // 8
        dz = jnp.where(y < 4, 3 - 2 * z_lo, jnp.where(y < 6, 2, 0))
        dx = jnp.where(y < 4, y, (y % 2) * 2 + z_lo)
    return ((z_hi + dz) % 4) * x_count + (x + dx) % x_count


def regroup(block_rows):
    tgt_size = lax.axis_size("tgt")
    src_size = lax.axis_size("src")
    perms = ([], [])
    for t in range(tgt_size):
        for s in range(src_size):
            pair = source_pair(t, s)
            for flip in range(2):
                u = 2 * pair + ((t % 2) ^ flip)
                perms[flip].append((lin(u, holder(s)), lin(t, s)))
    return [lax.ppermute(block_rows, ("tgt", "src"), p) for p in perms]


def forward_perms():
    tgt_size = lax.axis_size("tgt")
    src_size = lax.axis_size("src")
    direct, swap = [], []
    for t in range(tgt_size):
        for s in range(src_size):
            u = 2 * source_pair(t, s) + t % 2
            direct.append((lin(u, holder(s)), lin(t, s)))
            swap.append((lin(t ^ 1, s), lin(t, s)))
    return direct, swap


def regroup_order(got, axis=0):
    odd = lax.axis_index("tgt") % 2 == 1
    return jnp.concatenate(
        [jnp.where(odd, got[1], got[0]), jnp.where(odd, got[0], got[1])], axis
    )


def regroup_offsets(offsets):
    tgt_size = lax.axis_size("tgt")
    src_size = lax.axis_size("src")
    pairs = [
        (lin(t, source_pair(t, s)), lin(t, s)) for t in range(tgt_size) for s in range(src_size)
    ]
    return lax.ppermute(offsets, ("tgt", "src"), pairs)


def per_device(
    states_late,
    offset_late,
    values_late,
    states_mid,
    offset_mid,
    exercise_mid,
    mask_mid,
    states_early,
    exercise_early,
    mask_early,
):
    src_tiles = states_late.shape[0] // BLOCK

    def mid_col_base():
        return lax.axis_index("src") * src_tiles

    def early_col_base():
        return source_pair(lax.axis_index("tgt"), lax.axis_index("src")) * src_tiles

    direct, swap = forward_perms()
    own_sources = lax.ppermute(states_mid, ("tgt", "src"), direct)
    mid_offsets = regroup_offsets(offset_mid)
    partials = date_partials_kernel(
        states_mid, states_late, offset_late, values_late.T, mask_mid, mid_col_base
    )
    swapped = lax.ppermute(own_sources, ("tgt", "src"), swap)
    mid_sources = regroup_order([own_sources, swapped])
    early_parts = []
    for row_tile in range(states_early.shape[0] // BLOCK):
        rows = states_early[row_tile * BLOCK : (row_tile + 1) * BLOCK]
        early_parts.append(
            date_weights_kernel(
                rows, mid_sources, mid_offsets, mask_early, row_tile, early_col_base
            )
        )
    value_mid_t = finish(partials, exercise_mid)
    mid_values_t = regroup_order(regroup(value_mid_t), axis=1)
    early_weighted = jnp.concatenate(
        [jnp.dot(mid_values_t, w, preferred_element_type=jnp.float32) for w, _ in early_parts], 1
    )
    early_stats = jnp.concatenate([s for _, s in early_parts], 1)
    value_early_t = finish(jnp.concatenate([early_weighted, early_stats], 0), exercise_early)
    value_mid, value_early = value_mid_t.T, value_early_t.T
    return (value_mid, value_early)


def solution(mesh):
    in_specs = (
        P("src", None),
        P("src"),
        P("src", None),
        P("tgt", None),
        P("src"),
        P("tgt", None),
        P(),
        P("tgt", None),
        P("tgt", None),
        P(),
    )
    out_specs = (P("tgt", None), P("tgt", None))
    return jax.shard_map(per_device, mesh=mesh, in_specs=in_specs, out_specs=out_specs, check_vma=False)
```

```python
import jax
import jax.numpy as jnp
from jax import lax
from jax.experimental import pallas as pl
from jax.experimental.pallas import tpu as pltpu
from jax.sharding import PartitionSpec as P


BLOCK = 512


sharpness = 3.5
very_low = -1e30


def row_tile_base(row_tiles):
    return lax.axis_index("tgt") * row_tiles


def offset_column(off_row):
    wide = jnp.broadcast_to(off_row.astype(jnp.float32), (8, off_row.shape[1]))
    return jnp.transpose(wide)[:, 0:1]


def partials_kernel(mask_ref, x_ref, y_ref, off_ref, v_ref, out_ref, *, scale, row_tiles, col_tiles, col_base):
    i = pl.program_id(0)
    row = row_tile_base(row_tiles) + i
    col0 = col_base()
    width = v_ref.shape[0]
    out_ref[0 : width + 1, :] = jnp.zeros((width + 1, BLOCK), jnp.float32)
    out_ref[width + 1 : width + 2, :] = jnp.full((1, BLOCK), very_low, jnp.float32)
    for j in range(col_tiles):
        live = mask_ref[row, col0 + j] > 0
        y = y_ref[j * BLOCK : (j + 1) * BLOCK, :]
        s = lax.dot_general(y, x_ref[...], (((1,), (1,)), ((), ())), preferred_element_type=jnp.float32)
        s = s * scale - offset_column(off_ref[:, j * BLOCK : (j + 1) * BLOCK])
        m_old = out_ref[width + 1 : width + 2, :]
        m_new = jnp.where(live, jnp.maximum(m_old, jnp.max(s, axis=0, keepdims=True)), m_old)
        shrink = jnp.exp(m_old - m_new)
        p = jnp.where(live, jnp.exp(s - m_new), 0.0)
        out_ref[width : width + 1, :] = out_ref[width : width + 1, :] * shrink + jnp.sum(p, axis=0, keepdims=True)
        out_ref[0:width, :] = out_ref[0:width, :] * shrink + jnp.dot(
            v_ref[:, j * BLOCK : (j + 1) * BLOCK], p.astype(jnp.bfloat16), preferred_element_type=jnp.float32
        )
        out_ref[width + 1 : width + 2, :] = m_new


def date_partials_kernel(targets, sources, offsets, values_t, tile_mask, col_base):
    rows, factors = targets.shape
    cols = sources.shape[0]
    width = values_t.shape[0]
    row_tiles, col_tiles = rows // BLOCK, cols // BLOCK
    kernel = lambda *refs: partials_kernel(
        *refs, scale=sharpness / factors**0.5, row_tiles=row_tiles, col_tiles=col_tiles, col_base=col_base
    )
    return pl.pallas_call(
        kernel,
        out_shape=jax.ShapeDtypeStruct((width + 2, rows), jnp.float32),
        grid_spec=pltpu.PrefetchScalarGridSpec(
            num_scalar_prefetch=1,
            grid=(row_tiles,),
            in_specs=[
                pl.BlockSpec((BLOCK, factors), lambda i, m: (i, 0)),
                pl.BlockSpec((cols, factors), lambda i, m: (0, 0)),
                pl.BlockSpec((1, cols), lambda i, m: (0, 0)),
                pl.BlockSpec((width, cols), lambda i, m: (0, 0)),
            ],
            out_specs=pl.BlockSpec((width + 2, BLOCK), lambda i, m: (0, i)),
        ),
        compiler_params=pltpu.CompilerParams(dimension_semantics=("arbitrary",)),
    )(tile_mask, targets, sources, offsets.reshape(1, cols), values_t)


def weights_kernel(mask_ref, x_ref, y_ref, off_ref, p_ref, stats_ref, *, scale, row_tile, col_tiles, col_base):
    row = row_tile_base(2) + row_tile
    col0 = col_base()

    def scores(j):
        y = y_ref[j * BLOCK : (j + 1) * BLOCK, :]
        s = lax.dot_general(y, x_ref[...], (((1,), (1,)), ((), ())), preferred_element_type=jnp.float32)
        return s * scale - offset_column(off_ref[:, j * BLOCK : (j + 1) * BLOCK])

    peak = jnp.full((1, BLOCK), very_low, jnp.float32)
    for j in range(col_tiles):
        live = mask_ref[row, col0 + j] > 0
        peak = jnp.where(live, jnp.maximum(peak, jnp.max(scores(j), axis=0, keepdims=True)), peak)
    total = jnp.zeros((1, BLOCK), jnp.float32)
    for j in range(col_tiles):
        live = mask_ref[row, col0 + j] > 0
        p = jnp.where(live, jnp.exp(scores(j) - peak), 0.0)
        p_ref[j * BLOCK : (j + 1) * BLOCK, :] = p.astype(jnp.bfloat16)
        total = total + jnp.sum(p, axis=0, keepdims=True)
    stats_ref[0:1, :] = total
    stats_ref[1:2, :] = peak


def date_weights_kernel(targets, sources, offsets, tile_mask, row_tile, col_base):
    rows, factors = targets.shape
    cols = sources.shape[0]
    col_tiles = cols // BLOCK
    kernel = lambda *refs: weights_kernel(
        *refs, scale=sharpness / factors**0.5, row_tile=row_tile, col_tiles=col_tiles, col_base=col_base
    )
    return pl.pallas_call(
        kernel,
        out_shape=(
            jax.ShapeDtypeStruct((cols, rows), jnp.bfloat16),
            jax.ShapeDtypeStruct((2, rows), jnp.float32),
        ),
        grid_spec=pltpu.PrefetchScalarGridSpec(
            num_scalar_prefetch=1,
            grid=(1,),
            in_specs=[
                pl.BlockSpec((BLOCK, factors), lambda i, m: (0, 0)),
                pl.BlockSpec((cols, factors), lambda i, m: (0, 0)),
                pl.BlockSpec((1, cols), lambda i, m: (0, 0)),
            ],
            out_specs=(
                pl.BlockSpec((cols, BLOCK), lambda i, m: (0, 0)),
                pl.BlockSpec((2, BLOCK), lambda i, m: (0, 0)),
            ),
        ),
        compiler_params=pltpu.CompilerParams(dimension_semantics=("arbitrary",)),
    )(tile_mask, targets, sources, offsets.reshape(1, cols))


HALVING_BITS = (3,)
FAR_PARTNER = (6, 7, 4, 5, 2, 3, 0, 1)
EXCHANGES = (lambda y: y ^ 1, lambda y: y ^ 2, lambda y: FAR_PARTNER[y])


def xor_perm(size, bit):
    return [(i, i ^ (1 << bit)) for i in range(size)]


def exchange_perm(size, partner):
    return [(i, (i // 8) * 8 + partner(i % 8)) for i in range(size)]


def merge(mine, theirs):
    width = mine.shape[0] - 2
    peak_a, peak_b = mine[width + 1 :], theirs[width + 1 :]
    peak = jnp.maximum(peak_a, peak_b)
    scale_a = jnp.exp(peak_a - peak)
    scale_b = jnp.exp(peak_b - peak)
    body = mine[: width + 1] * scale_a + theirs[: width + 1] * scale_b
    return jnp.concatenate([body, peak], axis=0)


def finish(packed, exercise):
    src_size = lax.axis_size("src")
    me = lax.axis_index("src")
    exercise = exercise.astype(jnp.float32)
    for bit in HALVING_BITS:
        half = packed.shape[1] // 2
        mine_hi = (me >> bit) & 1
        keep = lax.dynamic_slice_in_dim(packed, mine_hi * half, half, 1)
        send = lax.dynamic_slice_in_dim(packed, (1 - mine_hi) * half, half, 1)
        got = lax.ppermute(send, "src", xor_perm(src_size, bit))
        packed = merge(keep, got)
        exercise = lax.dynamic_slice_in_dim(exercise, mine_hi * half, half, 0)
    for partner in EXCHANGES:
        got = lax.ppermute(packed, "src", exchange_perm(src_size, partner))
        packed = merge(packed, got)
    width = packed.shape[0] - 2
    continuation = packed[:width] / packed[width : width + 1]
    value = jnp.maximum(continuation, exercise.T).astype(jnp.bfloat16)
    for bit in reversed(HALVING_BITS):
        mine_hi = (me >> bit) & 1
        got = lax.ppermute(value, "src", xor_perm(src_size, bit))
        value = jnp.where(
            mine_hi == 1,
            jnp.concatenate([got, value], 1),
            jnp.concatenate([value, got], 1),
        )
    return value


def lin(t, s):
    return t * lax.axis_size("src") + s


Z_PLAN = ((3, 1, 1), (3, 1, 1), (3, 1, 1), (3, 1, 1), (2, 2, 1), (2, 2, 1), (0, 0, 0), (0, 0, 0))


def column_offset(s):
    y, z_lo = s % 8, s // 8
    dz = Z_PLAN[y][z_lo]
    same_dz = [(yy, zz) for yy in range(8) for zz in range(2) if Z_PLAN[yy][zz] == dz]
    return dz, same_dz.index((y, z_lo))


def holder(s):
    return s ^ (8 * Z_PLAN[s % 8][2])


def source_pair(t, s):
    x_count = lax.axis_size("tgt") // 8
    z_hi, x = t // (2 * x_count), (t // 2) % x_count
    if isinstance(s, int):
        dz, dx = column_offset(s)
    else:
        y, z_lo = s % 8, s // 8
        dz = jnp.where(y < 4, 3 - 2 * z_lo, jnp.where(y < 6, 2, 0))
        dx = jnp.where(y < 4, y, (y % 2) * 2 + z_lo)
    return ((z_hi + dz) % 4) * x_count + (x + dx) % x_count


def forward_perms():
    tgt_size = lax.axis_size("tgt")
    src_size = lax.axis_size("src")
    direct, swap = [], []
    for t in range(tgt_size):
        for s in range(src_size):
            u = 2 * source_pair(t, s) + t % 2
            direct.append((lin(u, holder(s)), lin(t, s)))
            swap.append((lin(t ^ 1, s), lin(t, s)))
    return direct, swap


def regroup_order(got, axis=0):
    odd = lax.axis_index("tgt") % 2 == 1
    return jnp.concatenate(
        [jnp.where(odd, got[1], got[0]), jnp.where(odd, got[0], got[1])], axis
    )


def regroup_offsets(offsets):
    tgt_size = lax.axis_size("tgt")
    src_size = lax.axis_size("src")
    pairs = [
        (lin(t, source_pair(t, s)), lin(t, s)) for t in range(tgt_size) for s in range(src_size)
    ]
    return lax.ppermute(offsets, ("tgt", "src"), pairs)


def per_device(
    states_late,
    offset_late,
    values_late,
    states_mid,
    offset_mid,
    exercise_mid,
    mask_mid,
    states_early,
    exercise_early,
    mask_early,
):
    src_tiles = states_late.shape[0] // BLOCK

    def mid_col_base():
        return lax.axis_index("src") * src_tiles

    def early_col_base():
        return source_pair(lax.axis_index("tgt"), lax.axis_index("src")) * src_tiles

    direct, swap = forward_perms()
    own_sources = lax.ppermute(states_mid, ("tgt", "src"), direct)
    mid_offsets = regroup_offsets(offset_mid)
    partials = date_partials_kernel(
        states_mid, states_late, offset_late, values_late.T, mask_mid, mid_col_base
    )
    partials, own_sources, mid_offsets = lax.optimization_barrier(
        (partials, own_sources, mid_offsets)
    )
    mid_sources = regroup_order(
        [own_sources, lax.ppermute(own_sources, ("tgt", "src"), swap)]
    )
    early_parts = []
    for row_tile in range(states_early.shape[0] // BLOCK):
        rows = states_early[row_tile * BLOCK : (row_tile + 1) * BLOCK]
        early_parts.append(
            date_weights_kernel(
                rows, mid_sources, mid_offsets, mask_early, row_tile, early_col_base
            )
        )
    value_mid_t = finish(partials, exercise_mid)
    own_values = lax.ppermute(value_mid_t, ("tgt", "src"), direct)
    other_values = lax.ppermute(own_values, ("tgt", "src"), swap)
    half = own_values.shape[1]
    odd = lax.axis_index("tgt") % 2

    def weighted_part(w):
        own_w = lax.dynamic_slice_in_dim(w, odd * half, half, 0)
        other_w = lax.dynamic_slice_in_dim(w, (1 - odd) * half, half, 0)
        own_part = jnp.dot(own_values, own_w, preferred_element_type=jnp.float32)
        return own_part + jnp.dot(other_values, other_w, preferred_element_type=jnp.float32)

    early_weighted = jnp.concatenate([weighted_part(w) for w, _ in early_parts], 1)
    early_stats = jnp.concatenate([s for _, s in early_parts], 1)
    value_early_t = finish(jnp.concatenate([early_weighted, early_stats], 0), exercise_early)
    value_mid, value_early = value_mid_t.T, value_early_t.T
    return (value_mid, value_early)


def solution(mesh):
    in_specs = (
        P("src", None),
        P("src"),
        P("src", None),
        P("tgt", None),
        P("src"),
        P("tgt", None),
        P(),
        P("tgt", None),
        P("tgt", None),
        P(),
    )
    out_specs = (P("tgt", None), P("tgt", None))
    return jax.shard_map(per_device, mesh=mesh, in_specs=in_specs, out_specs=out_specs, check_vma=False)
```

```python
import jax
import jax.numpy as jnp
from jax import lax
from jax.experimental import pallas as pl
from jax.experimental.pallas import tpu as pltpu
from jax.sharding import PartitionSpec as P


BLOCK = 512


sharpness = 3.5
very_low = -1e30


def row_tile_base(row_tiles):
    return lax.axis_index("tgt") * row_tiles


def offset_column(off_row):
    wide = jnp.broadcast_to(off_row.astype(jnp.float32)[None, :], (8, off_row.shape[0]))
    return jnp.transpose(wide)[:, 0:1]


def partials_kernel(mask_ref, x_ref, y_ref, off_ref, v_ref, out_ref, *, scale, row_tiles, col_tiles, col_base):
    i = pl.program_id(0)
    row = row_tile_base(row_tiles) + i
    col0 = col_base()
    width = v_ref.shape[0]
    out_ref[0 : width + 1, :] = jnp.zeros((width + 1, BLOCK), jnp.float32)
    out_ref[width + 1 : width + 2, :] = jnp.full((1, BLOCK), very_low, jnp.float32)
    for j in range(col_tiles):
        live = mask_ref[row, col0 + j] > 0
        y = y_ref[j * BLOCK : (j + 1) * BLOCK, :]
        s = lax.dot_general(y, x_ref[...], (((1,), (1,)), ((), ())), preferred_element_type=jnp.float32)
        s = s * scale - offset_column(off_ref[j * BLOCK : (j + 1) * BLOCK])
        m_old = out_ref[width + 1 : width + 2, :]
        m_new = jnp.where(live, jnp.maximum(m_old, jnp.max(s, axis=0, keepdims=True)), m_old)
        shrink = jnp.exp(m_old - m_new)
        p = jnp.where(live, jnp.exp(s - m_new), 0.0)
        out_ref[width : width + 1, :] = out_ref[width : width + 1, :] * shrink + jnp.sum(p, axis=0, keepdims=True)
        out_ref[0:width, :] = out_ref[0:width, :] * shrink + jnp.dot(
            v_ref[:, j * BLOCK : (j + 1) * BLOCK], p.astype(jnp.bfloat16), preferred_element_type=jnp.float32
        )
        out_ref[width + 1 : width + 2, :] = m_new


def date_partials_kernel(targets, sources, offsets, values_t, tile_mask, col_base):
    rows, factors = targets.shape
    cols = sources.shape[0]
    width = values_t.shape[0]
    row_tiles, col_tiles = rows // BLOCK, cols // BLOCK
    kernel = lambda *refs: partials_kernel(
        *refs, scale=sharpness / factors**0.5, row_tiles=row_tiles, col_tiles=col_tiles, col_base=col_base
    )
    return pl.pallas_call(
        kernel,
        out_shape=jax.ShapeDtypeStruct((width + 2, rows), jnp.float32),
        grid_spec=pltpu.PrefetchScalarGridSpec(
            num_scalar_prefetch=1,
            grid=(row_tiles,),
            in_specs=[
                pl.BlockSpec((BLOCK, factors), lambda i, m: (i, 0)),
                pl.BlockSpec((cols, factors), lambda i, m: (0, 0)),
                pl.BlockSpec((cols,), lambda i, m: (0,)),
                pl.BlockSpec((width, cols), lambda i, m: (0, 0)),
            ],
            out_specs=pl.BlockSpec((width + 2, BLOCK), lambda i, m: (0, i)),
        ),
        compiler_params=pltpu.CompilerParams(dimension_semantics=("arbitrary",)),
    )(tile_mask, targets, sources, offsets, values_t)


def weights_kernel(mask_ref, x_ref, y_ref, off_ref, p_ref, stats_ref, *, scale, row_tile, col_tiles, col_base):
    row = row_tile_base(2) + row_tile
    col0 = col_base()

    def scores(j):
        y = y_ref[j * BLOCK : (j + 1) * BLOCK, :]
        s = lax.dot_general(y, x_ref[...], (((1,), (1,)), ((), ())), preferred_element_type=jnp.float32)
        return s * scale - offset_column(off_ref[j * BLOCK : (j + 1) * BLOCK])

    peak = jnp.full((1, BLOCK), very_low, jnp.float32)
    for j in range(col_tiles):
        live = mask_ref[row, col0 + j] > 0
        peak = jnp.where(live, jnp.maximum(peak, jnp.max(scores(j), axis=0, keepdims=True)), peak)
    total = jnp.zeros((1, BLOCK), jnp.float32)
    for j in range(col_tiles):
        live = mask_ref[row, col0 + j] > 0
        p = jnp.where(live, jnp.exp(scores(j) - peak), 0.0)
        p_ref[j * BLOCK : (j + 1) * BLOCK, :] = p.astype(jnp.bfloat16)
        total = total + jnp.sum(p, axis=0, keepdims=True)
    stats_ref[0:1, :] = total
    stats_ref[1:2, :] = peak


def date_weights_kernel(targets, sources, offsets, tile_mask, row_tile, col_base):
    rows, factors = targets.shape
    cols = sources.shape[0]
    col_tiles = cols // BLOCK
    kernel = lambda *refs: weights_kernel(
        *refs, scale=sharpness / factors**0.5, row_tile=row_tile, col_tiles=col_tiles, col_base=col_base
    )
    return pl.pallas_call(
        kernel,
        out_shape=(
            jax.ShapeDtypeStruct((cols, rows), jnp.bfloat16),
            jax.ShapeDtypeStruct((2, rows), jnp.float32),
        ),
        grid_spec=pltpu.PrefetchScalarGridSpec(
            num_scalar_prefetch=1,
            grid=(1,),
            in_specs=[
                pl.BlockSpec((BLOCK, factors), lambda i, m: (0, 0)),
                pl.BlockSpec((cols, factors), lambda i, m: (0, 0)),
                pl.BlockSpec((cols,), lambda i, m: (0,)),
            ],
            out_specs=(
                pl.BlockSpec((cols, BLOCK), lambda i, m: (0, 0)),
                pl.BlockSpec((2, BLOCK), lambda i, m: (0, 0)),
            ),
        ),
        compiler_params=pltpu.CompilerParams(dimension_semantics=("arbitrary",)),
    )(tile_mask, targets, sources, offsets)


HALVING_BITS = (3,)
FAR_PARTNER = (6, 7, 4, 5, 2, 3, 0, 1)
EXCHANGES = (lambda y: y ^ 1, lambda y: y ^ 2, lambda y: FAR_PARTNER[y])


def xor_perm(size, bit):
    return [(i, i ^ (1 << bit)) for i in range(size)]


def exchange_perm(size, partner):
    return [(i, (i // 8) * 8 + partner(i % 8)) for i in range(size)]


def merge(mine, theirs):
    width = mine.shape[0] - 2
    peak_a, peak_b = mine[width + 1 :], theirs[width + 1 :]
    peak = jnp.maximum(peak_a, peak_b)
    scale_a = jnp.exp(peak_a - peak)
    scale_b = jnp.exp(peak_b - peak)
    body = mine[: width + 1] * scale_a + theirs[: width + 1] * scale_b
    return jnp.concatenate([body, peak], axis=0)


def finish(packed, exercise):
    src_size = lax.axis_size("src")
    me = lax.axis_index("src")
    exercise = exercise.astype(jnp.float32)
    for bit in HALVING_BITS:
        half = packed.shape[1] // 2
        mine_hi = (me >> bit) & 1
        keep = lax.dynamic_slice_in_dim(packed, mine_hi * half, half, 1)
        send = lax.dynamic_slice_in_dim(packed, (1 - mine_hi) * half, half, 1)
        got = lax.ppermute(send, "src", xor_perm(src_size, bit))
        packed = merge(keep, got)
        exercise = lax.dynamic_slice_in_dim(exercise, mine_hi * half, half, 0)
    for partner in EXCHANGES:
        got = lax.ppermute(packed, "src", exchange_perm(src_size, partner))
        packed = merge(packed, got)
    width = packed.shape[0] - 2
    continuation = packed[:width] / packed[width : width + 1]
    value = jnp.maximum(continuation, exercise.T).astype(jnp.bfloat16)
    for bit in reversed(HALVING_BITS):
        mine_hi = (me >> bit) & 1
        got = lax.ppermute(value, "src", xor_perm(src_size, bit))
        value = jnp.where(
            mine_hi == 1,
            jnp.concatenate([got, value], 1),
            jnp.concatenate([value, got], 1),
        )
    return value


def lin(t, s):
    return t * lax.axis_size("src") + s


Z_PLAN = ((3, 1, 1), (3, 1, 1), (3, 1, 1), (3, 1, 1), (2, 2, 1), (2, 2, 1), (0, 0, 0), (0, 0, 0))


def column_offset(s):
    y, z_lo = s % 8, s // 8
    dz = Z_PLAN[y][z_lo]
    same_dz = [(yy, zz) for yy in range(8) for zz in range(2) if Z_PLAN[yy][zz] == dz]
    return dz, same_dz.index((y, z_lo))


def holder(s):
    return s ^ (8 * Z_PLAN[s % 8][2])


def source_pair(t, s):
    x_count = lax.axis_size("tgt") // 8
    z_hi, x = t // (2 * x_count), (t // 2) % x_count
    if isinstance(s, int):
        dz, dx = column_offset(s)
    else:
        y, z_lo = s % 8, s // 8
        dz = jnp.where(y < 4, 3 - 2 * z_lo, jnp.where(y < 6, 2, 0))
        dx = jnp.where(y < 4, y, (y % 2) * 2 + z_lo)
    return ((z_hi + dz) % 4) * x_count + (x + dx) % x_count


def regroup(block_rows):
    tgt_size = lax.axis_size("tgt")
    src_size = lax.axis_size("src")
    perms = ([], [])
    for t in range(tgt_size):
        for s in range(src_size):
            pair = source_pair(t, s)
            for flip in range(2):
                u = 2 * pair + ((t % 2) ^ flip)
                perms[flip].append((lin(u, holder(s)), lin(t, s)))
    return [lax.ppermute(block_rows, ("tgt", "src"), p) for p in perms]


def forward_perms():
    tgt_size = lax.axis_size("tgt")
    src_size = lax.axis_size("src")
    direct, swap = [], []
    for t in range(tgt_size):
        for s in range(src_size):
            u = 2 * source_pair(t, s) + t % 2
            direct.append((lin(u, holder(s)), lin(t, s)))
            swap.append((lin(t ^ 1, s), lin(t, s)))
    return direct, swap


def regroup_order(got, axis=0):
    odd = lax.axis_index("tgt") % 2 == 1
    return jnp.concatenate(
        [jnp.where(odd, got[1], got[0]), jnp.where(odd, got[0], got[1])], axis
    )


def regroup_offsets(offsets):
    tgt_size = lax.axis_size("tgt")
    src_size = lax.axis_size("src")
    pairs = [
        (lin(t, source_pair(t, s)), lin(t, s)) for t in range(tgt_size) for s in range(src_size)
    ]
    return lax.ppermute(offsets, ("tgt", "src"), pairs)


def per_device(
    states_late,
    offset_late,
    values_late,
    states_mid,
    offset_mid,
    exercise_mid,
    mask_mid,
    states_early,
    exercise_early,
    mask_early,
):
    src_tiles = states_late.shape[0] // BLOCK

    def mid_col_base():
        return lax.axis_index("src") * src_tiles

    def early_col_base():
        return source_pair(lax.axis_index("tgt"), lax.axis_index("src")) * src_tiles

    direct, swap = forward_perms()
    own_sources = lax.ppermute(states_mid, ("tgt", "src"), direct)
    mid_offsets = regroup_offsets(offset_mid)
    partials = date_partials_kernel(
        states_mid, states_late, offset_late, values_late.T, mask_mid, mid_col_base
    )
    partials, own_sources, mid_offsets = lax.optimization_barrier(
        (partials, own_sources, mid_offsets)
    )
    mid_sources = regroup_order(
        [own_sources, lax.ppermute(own_sources, ("tgt", "src"), swap)]
    )
    early_parts = []
    for row_tile in range(states_early.shape[0] // BLOCK):
        rows = states_early[row_tile * BLOCK : (row_tile + 1) * BLOCK]
        early_parts.append(
            date_weights_kernel(
                rows, mid_sources, mid_offsets, mask_early, row_tile, early_col_base
            )
        )
    value_mid_t = finish(partials, exercise_mid)
    mid_values_t = regroup_order(regroup(value_mid_t), axis=1)
    early_weighted = jnp.concatenate(
        [jnp.dot(mid_values_t, w, preferred_element_type=jnp.float32) for w, _ in early_parts], 1
    )
    early_stats = jnp.concatenate([s for _, s in early_parts], 1)
    value_early_t = finish(jnp.concatenate([early_weighted, early_stats], 0), exercise_early)
    value_mid, value_early = value_mid_t.T, value_early_t.T
    return (value_mid, value_early)


def solution(mesh):
    in_specs = (
        P("src", None),
        P("src"),
        P("src", None),
        P("tgt", None),
        P("src"),
        P("tgt", None),
        P(),
        P("tgt", None),
        P("tgt", None),
        P(),
    )
    out_specs = (P("tgt", None), P("tgt", None))
    return jax.shard_map(per_device, mesh=mesh, in_specs=in_specs, out_specs=out_specs, check_vma=False)
```
